256 devices in a mesh: req: 32 (over y, z), vocab: 8 (over x, core).
Axes of the slice: x: 4, y: 4, z: 8, core: 2. Of those that a mesh axis runs over, the one named last changes fastest.
Arguments:
- draft_states: bfloat16 [64, 64, 1536], P('req')
- parents: int32 [64, 64], P('req'), may hold values from -1 to 62, as said below
- live_draft_count: int32 [64], replicated, may hold values from 32 to 64, as said below
- path_index: int32 [64, 8], P('req'), may hold values from 0 to 63, as said below
- cached_length_list: int32 [64], P('req'), may hold values from 256 to 1792, as said below
- cached_key_rows: bfloat16 [65536, 768], P('req', 'vocab')
- cached_value_rows: bfloat16 [65536, 768], P('req', 'vocab'), may hold values from -6 to 6
- attend_gain: bfloat16 [1536], replicated, may hold values from 0.099609375 to 1.8984375
- hidden_gain: bfloat16 [1536], replicated, may hold values from 0.099609375 to 1.8984375
- final_gain: bfloat16 [1536], replicated, may hold values from 0.099609375 to 1.8984375
- query_weight: bfloat16 [1536, 1536], P(None, 'vocab')
- key_matrix: bfloat16 [1536, 768], P(None, 'vocab')
- value_matrix: bfloat16 [1536, 768], P(None, 'vocab'), may hold values from -0.15625 to 0.15625
- out_weight: bfloat16 [1536, 1536], P('vocab'), may hold values from -0.15625 to 0.15625
- gate_weight: bfloat16 [1536, 4096], P(None, 'vocab'), may hold values from -0.15625 to 0.15625
- up_weight: bfloat16 [1536, 4096], P(None, 'vocab'), may hold values from -0.15625 to 0.15625
- down_weight: bfloat16 [4096, 1536], P('vocab'), may hold values from -0.09375 to 0.09375
- head_weight: bfloat16 [1536, 32000], P(None, 'req'), may hold values from -0.4375 to 0.4375
Outputs:
- layer_output_rows: bfloat16 [64, 64, 1536], P('req', None, 'vocab')
- accepted_keys: bfloat16 [64, 8, 768], P('req', None, 'vocab')
- accepted_values: bfloat16 [64, 8, 768], P('req', None, 'vocab')
- norm_values: float32 [64, 8], P('req', 'vocab')
- maxima: float32 [64, 8], P(None, 'vocab')
The draws below stay inside these ranges and needn't reach their ends.
Inputs may be any that keep to these rules, and one draw needn't show every extreme that they name: `live_draft_count`: the counts of all requests sum to exactly 3072. `parents`: each draft token's parent lies below its own index; the first token's is -1. `path_index`: each row lists 8 live draft tokens of its request, each the parent of the next. `cached_length_list`: the lengths of the 2 requests of one index of req sum to at most 2048, and to exactly 2048 on a quarter of the indices of req (at least one); on such an index one request is long and the others hold 256 each.
All inputs are finite; a program needn't handle non-finite values.
Results may differ from the reference program's by a relative error of at most 0.012.
Values may be sent and summed in bfloat16 or wider, within the bound.
No kernel may reach another device: no remote copies, remote signals or barrier semaphores. Data moves between devices by JAX's collectives and lax.ppermute only.
A program may use at most 64 MiB of HBM per device.

```python
import jax
import jax.numpy as jnp
from jax import lax

MODEL_SIZE = 1536
QUERY_HEADS = 16
KEY_HEADS = 8
HEAD_SIZE = 96
FF = 4096
VOCAB = 32000
REQUESTS_LOCAL = 2
DRAFT_SLOTS = 64
PATH = 8
POOL_ROWS = 2048
REQUEST_TOTAL = 64
SHORT = 512
N_REQ = 32


def tree_tables(key):
    random_base_key = jax.random.fold_in(key, 7001)
    pair_key, order_key, parent_key, finish_key = jax.random.split(random_base_key, 4)
    spread = jax.random.randint(pair_key, (REQUEST_TOTAL // 2,), 0, DRAFT_SLOTS // 4 + 1)
    spread = spread.at[0].set(DRAFT_SLOTS // 4)
    middle = 3 * DRAFT_SLOTS // 4
    counts = jax.random.permutation(order_key, jnp.concatenate([middle + spread, middle - spread]))
    placed = jnp.arange(DRAFT_SLOTS, dtype=jnp.int32)[None, :]
    stepback = jnp.minimum(jax.random.randint(parent_key, (REQUEST_TOTAL, DRAFT_SLOTS), 0, 4), jnp.maximum(placed - 1, 0))
    parents = jnp.where(placed == 0, -1, placed - 1 - stepback)
    current = jax.random.randint(finish_key, (REQUEST_TOTAL,), 4 * (PATH - 1), counts)
    current = jnp.where(counts == DRAFT_SLOTS, DRAFT_SLOTS - 1, current)
    chained = [current]
    for hop_number in range(PATH - 1):
        current = jnp.take_along_axis(parents, current[:, None], axis=1)[:, 0]
        chained.append(current)
    path = jnp.stack(chained[::-1], axis=1)
    return (counts.astype(jnp.int32), parents.astype(jnp.int32), path.astype(jnp.int32))


def draw_live_draft_count(key, part):
    return tree_tables(key)[0]


def draw_parents(key, part):
    return tree_tables(key)[1]


def draw_path_index(key, part):
    return tree_tables(key)[2]


def draw_cached_length_list(key, part):
    random_base_key = jax.random.fold_in(key, 7002)
    short_key, order_key, chosen_key = jax.random.split(random_base_key, 3)
    groups = REQUEST_TOTAL // REQUESTS_LOCAL
    short_length = jax.random.randint(short_key, (groups, REQUESTS_LOCAL), SHORT // 2, SHORT + 1)
    group_rank = jax.random.permutation(order_key, groups)
    is_long = group_rank < max(1, groups // 4)
    chosen = jax.random.randint(chosen_key, (groups, 1), 0, REQUESTS_LOCAL)
    column_no = jnp.arange(REQUESTS_LOCAL, dtype=jnp.int32)[None, :]
    long_length = POOL_ROWS - (REQUESTS_LOCAL - 1) * (SHORT // 2)
    long_row = jnp.where(column_no == chosen, long_length, SHORT // 2)
    lengths = jnp.where(is_long[:, None], long_row, short_length)
    return lengths.reshape(REQUEST_TOTAL).astype(jnp.int32)


def draw_cached_key_rows(key, part):
    every_row = POOL_ROWS * (REQUEST_TOTAL // REQUESTS_LOCAL)
    random_base_key = jax.random.fold_in(jax.random.fold_in(key, 7003), 0)
    key_rows = jax.random.normal(random_base_key, (every_row, KEY_HEADS * HEAD_SIZE))
    return key_rows.astype(jnp.bfloat16)


def draw_draft_states(key, part):
    random_base_key, row_key, column_key = jax.random.split(jax.random.fold_in(key, 7004), 3)
    row_scale = jnp.exp(jax.random.uniform(row_key, (REQUEST_TOTAL, DRAFT_SLOTS, 1), minval=jnp.log(0.3), maxval=jnp.log(3.0)))
    column_scale = jnp.exp(jax.random.uniform(column_key, (1, 1, MODEL_SIZE), minval=jnp.log(0.3), maxval=jnp.log(3.0)))
    value_base_rows = jax.random.normal(random_base_key, (REQUEST_TOTAL, DRAFT_SLOTS, MODEL_SIZE))
    return (value_base_rows * row_scale * column_scale).astype(jnp.bfloat16)


def query_and_key(key):
    query_key, jitter_key = jax.random.split(jax.random.fold_in(key, 7005), 2)
    query_vectors = jax.random.normal(query_key, (MODEL_SIZE, QUERY_HEADS * HEAD_SIZE)) * MODEL_SIZE ** (-0.5)
    random_jitter = jax.random.normal(jitter_key, (MODEL_SIZE, KEY_HEADS * HEAD_SIZE)) * MODEL_SIZE ** (-0.5)
    common_rows = jnp.mean(query_vectors.reshape(MODEL_SIZE, KEY_HEADS, QUERY_HEADS // KEY_HEADS, HEAD_SIZE), axis=2).reshape(MODEL_SIZE, KEY_HEADS * HEAD_SIZE)
    return (query_vectors, common_rows + 0.7 * random_jitter)


def draw_query_weight(key, part):
    return query_and_key(key)[0].astype(jnp.bfloat16)


def draw_key_matrix(key, part):
    return query_and_key(key)[1].astype(jnp.bfloat16)


def levels(stream_key, dims, cuts, least, largest):
    gain, own = 1.0, jax.random.fold_in(stream_key, 6)
    for axis_at, parts in cuts:
        steps = jnp.exp(jax.random.uniform(jax.random.fold_in(own, axis_at), (parts,), jnp.float32, least / len(cuts), largest / len(cuts)))
        gain = gain * jnp.repeat(steps, dims[axis_at] // parts).reshape([-1 if axis == axis_at else 1 for axis in range(len(dims))])
    return gain


def bell_draw(key, shape, scale, reach, cuts=(), kind=jnp.bfloat16):
    loudness = levels(key, shape, cuts, -0.22, 0.18) if cuts else 1.0
    drawn = jax.random.normal(key, shape, jnp.float32) * scale * loudness
    return jnp.minimum(jnp.maximum(drawn, -reach), reach).astype(kind)


def setup_inputs(seed: int = 0) -> dict:
    streams_of = jax.random.split(jax.random.key(seed), 19)
    return {
        "draft_states": draw_draft_states(jax.random.fold_in(streams_of[18], 71), 0),
        "parents": draw_parents(jax.random.fold_in(streams_of[18], 71), 0),
        "live_draft_count": draw_live_draft_count(jax.random.fold_in(streams_of[18], 71), 0),
        "path_index": draw_path_index(jax.random.fold_in(streams_of[18], 71), 0),
        "cached_length_list": draw_cached_length_list(jax.random.fold_in(streams_of[18], 71), 0),
        "cached_key_rows": draw_cached_key_rows(jax.random.fold_in(streams_of[18], 71), 0),
        "cached_value_rows": bell_draw(streams_of[6], (POOL_ROWS * N_REQ, KEY_HEADS * HEAD_SIZE), 1.0, 6.0, ((0, 32), (1, 8))),
        "attend_gain": jnp.clip(1.0 + 0.18 * jax.random.normal(streams_of[7], (MODEL_SIZE,), jnp.float32), 0.099609375, 1.8984375).astype(jnp.bfloat16),
        "hidden_gain": jnp.clip(1.0 + 0.18 * jax.random.normal(streams_of[8], (MODEL_SIZE,), jnp.float32), 0.099609375, 1.8984375).astype(jnp.bfloat16),
        "final_gain": jnp.clip(1.0 + 0.18 * jax.random.normal(streams_of[9], (MODEL_SIZE,), jnp.float32), 0.099609375, 1.8984375).astype(jnp.bfloat16),
        "query_weight": draw_query_weight(jax.random.fold_in(streams_of[18], 71), 0),
        "key_matrix": draw_key_matrix(jax.random.fold_in(streams_of[18], 71), 0),
        "value_matrix": bell_draw(streams_of[12], (MODEL_SIZE, KEY_HEADS * HEAD_SIZE), MODEL_SIZE ** -0.5, 0.15625, ((1, 8),)),
        "out_weight": bell_draw(streams_of[13], (QUERY_HEADS * HEAD_SIZE, MODEL_SIZE), (QUERY_HEADS * HEAD_SIZE) ** -0.5, 0.15625, ((0, 8),)),
        "gate_weight": bell_draw(streams_of[14], (MODEL_SIZE, FF), MODEL_SIZE ** -0.5, 0.15625, ((1, 8),)),
        "up_weight": bell_draw(streams_of[15], (MODEL_SIZE, FF), MODEL_SIZE ** -0.5, 0.15625, ((1, 8),)),
        "down_weight": bell_draw(streams_of[16], (FF, MODEL_SIZE), FF ** -0.5, 0.09375, ((0, 8),)),
        "head_weight": bell_draw(streams_of[17], (MODEL_SIZE, VOCAB), (MODEL_SIZE // 9) ** -0.5, 0.4375, ((1, 32),)),
    }


eps_norm = 1e-05
rope_base = 100000.0
masked_score = -1e+30

def apply_rotation(values, token_positions):
    half_dim = values.shape[-1] // 2
    inverse = rope_base ** (-jnp.arange(half_dim, dtype=jnp.float32) * 2.0 / values.shape[-1])
    angles = token_positions.astype(jnp.float32)[:, None] * inverse[None, :]
    cosine = jnp.cos(angles)[:, None, :]
    sine_of = jnp.sin(angles)[:, None, :]
    first_half = values[..., :half_dim]
    second_half = values[..., half_dim:]
    return jnp.concatenate([first_half * cosine - second_half * sine_of, second_half * cosine + first_half * sine_of], axis=-1)

def ancestors(parents):
    draft_length = parents.shape[-1]
    columns = jnp.arange(draft_length, dtype=jnp.int32)
    reached = jnp.eye(draft_length, dtype=jnp.float32) + (parents[..., :, None] == columns).astype(jnp.float32)
    for sweep_number in range((draft_length - 1).bit_length()):
        reached = jnp.minimum(jnp.einsum('bij,bjk->bik', reached, reached, precision=lax.Precision.HIGHEST), 1.0)
    return reached

def rms_scale(values):
    return lax.rsqrt(lax.optimization_barrier(jnp.mean(values * values, axis=-1, keepdims=True)) + eps_norm)

def reference(draft_states, parents, live_draft_count, path_index, cached_length_list, cached_key_rows, cached_value_rows, attend_gain, hidden_gain, final_gain, query_weight, key_matrix, value_matrix, out_weight, gate_weight, up_weight, down_weight, head_weight):
    group_factor = QUERY_HEADS // KEY_HEADS
    score_scale = HEAD_SIZE ** (-0.5)
    token_rows = REQUESTS_LOCAL * DRAFT_SLOTS

    def single_group(inputs):
        group_states, group_parents, group_counts, group_lengths, grouped_key_rows, grouped_value_rows = inputs
        states = group_states.reshape(token_rows, MODEL_SIZE).astype(jnp.float32)
        normalized_states = (states * rms_scale(states) * attend_gain.astype(jnp.float32)).astype(jnp.bfloat16)
        reached = ancestors(group_parents)
        token_positions = (group_lengths[:, None] + (lax.optimization_barrier(jnp.sum(reached, axis=2)) - 1.0).astype(jnp.int32)).reshape(token_rows)
        query_vectors = apply_rotation(jnp.dot(normalized_states, query_weight, preferred_element_type=jnp.float32).reshape(token_rows, QUERY_HEADS, HEAD_SIZE), token_positions).astype(jnp.bfloat16)
        fresh_keys = apply_rotation(jnp.dot(normalized_states, key_matrix, preferred_element_type=jnp.float32).reshape(token_rows, KEY_HEADS, HEAD_SIZE), token_positions).astype(jnp.bfloat16)
        fresh_values = jnp.dot(normalized_states, value_matrix, preferred_element_type=jnp.float32).astype(jnp.bfloat16).reshape(token_rows, KEY_HEADS, HEAD_SIZE)
        query_fourfold = query_vectors.reshape(token_rows, KEY_HEADS, group_factor, HEAD_SIZE).astype(jnp.float32)
        cache_end = jnp.cumsum(group_lengths)
        cache_start = cache_end - group_lengths
        request_of = jnp.arange(token_rows, dtype=jnp.int32) // DRAFT_SLOTS
        slot_index = jnp.arange(POOL_ROWS, dtype=jnp.int32)
        allowed = (slot_index[None, :] >= cache_start[request_of][:, None]) & (slot_index[None, :] < cache_end[request_of][:, None])
        same_request = request_of[:, None] == request_of[None, :]
        reached_rows = reached.reshape(token_rows, DRAFT_SLOTS)
        tree_mask = same_request & (reached_rows[:, jnp.arange(token_rows, dtype=jnp.int32) % DRAFT_SLOTS] > 0.5)
        cached_scores = jnp.einsum('uhwz,ehz->hwue', query_fourfold, grouped_key_rows.reshape(POOL_ROWS, KEY_HEADS, HEAD_SIZE).astype(jnp.float32)) * score_scale
        tree_scores = jnp.einsum('rkgd,mkd->kgrm', query_fourfold, fresh_keys.astype(jnp.float32)) * score_scale
        row_max = jnp.maximum(lax.optimization_barrier(jnp.max(jnp.where(allowed, cached_scores, masked_score), axis=3)), lax.optimization_barrier(jnp.max(jnp.where(tree_mask, tree_scores, masked_score), axis=3)))
        cached_weights = jnp.where(allowed, jnp.exp(cached_scores - row_max[..., None]), 0.0).astype(jnp.bfloat16)
        tree_weights = jnp.where(tree_mask, jnp.exp(tree_scores - row_max[..., None]), 0.0).astype(jnp.bfloat16)
        totals = lax.optimization_barrier(jnp.sum(cached_weights.astype(jnp.float32), axis=3)) + lax.optimization_barrier(jnp.sum(tree_weights.astype(jnp.float32), axis=3))
        weighted_values = jnp.einsum('fhjm,mfl->fhjl', cached_weights.astype(jnp.float32), grouped_value_rows.reshape(POOL_ROWS, KEY_HEADS, HEAD_SIZE).astype(jnp.float32))
        weighted_values = weighted_values + jnp.einsum('kgrm,mkd->kgrd', tree_weights.astype(jnp.float32), fresh_values.astype(jnp.float32))
        attended = (weighted_values / totals[..., None]).transpose(2, 0, 1, 3).reshape(token_rows, QUERY_HEADS * HEAD_SIZE).astype(jnp.bfloat16)
        residual = states + jnp.dot(attended, out_weight, preferred_element_type=jnp.float32)
        hidden_in = (residual * rms_scale(residual) * hidden_gain.astype(jnp.float32)).astype(jnp.bfloat16)
        gate_out = jnp.dot(hidden_in, gate_weight, preferred_element_type=jnp.float32)
        up_out = jnp.dot(hidden_in, up_weight, preferred_element_type=jnp.float32)
        hidden = (jax.nn.silu(gate_out) * up_out).astype(jnp.bfloat16)
        feed_out = jnp.dot(hidden, down_weight, preferred_element_type=jnp.float32).astype(jnp.bfloat16)
        is_live = (jnp.arange(DRAFT_SLOTS, dtype=jnp.int32)[None, :] < group_counts[:, None]).reshape(token_rows)
        layer_output_rows = jnp.where(is_live[:, None], residual + feed_out.astype(jnp.float32), 0.0).astype(jnp.bfloat16)
        return (layer_output_rows.reshape(REQUESTS_LOCAL, DRAFT_SLOTS, MODEL_SIZE), fresh_keys.reshape(REQUESTS_LOCAL, DRAFT_SLOTS, KEY_HEADS * HEAD_SIZE), fresh_values.reshape(REQUESTS_LOCAL, DRAFT_SLOTS, KEY_HEADS * HEAD_SIZE))
    layer_gathered, joined_keys, joined_values = lax.map(single_group, (draft_states.reshape(N_REQ, REQUESTS_LOCAL, DRAFT_SLOTS, MODEL_SIZE), parents.reshape(N_REQ, REQUESTS_LOCAL, DRAFT_SLOTS), live_draft_count.reshape(N_REQ, REQUESTS_LOCAL), cached_length_list.reshape(N_REQ, REQUESTS_LOCAL), cached_key_rows.reshape(N_REQ, POOL_ROWS, KEY_HEADS * HEAD_SIZE), cached_value_rows.reshape(N_REQ, POOL_ROWS, KEY_HEADS * HEAD_SIZE)))
    layer_output_rows = layer_gathered.reshape(REQUEST_TOTAL, DRAFT_SLOTS, MODEL_SIZE)
    request_picker = (path_index[:, :, None] == jnp.arange(DRAFT_SLOTS, dtype=jnp.int32)[None, None, :]).astype(jnp.float32)
    accepted_keys = jnp.einsum('ytm,ymu->ytu', request_picker, joined_keys.reshape(REQUEST_TOTAL, DRAFT_SLOTS, KEY_HEADS * HEAD_SIZE).astype(jnp.float32)).astype(jnp.bfloat16)
    accepted_values = jnp.einsum('ytm,ymu->ytu', request_picker, joined_values.reshape(REQUEST_TOTAL, DRAFT_SLOTS, KEY_HEADS * HEAD_SIZE).astype(jnp.float32)).astype(jnp.bfloat16)
    path_states = jnp.einsum('ytm,ymu->ytu', request_picker, layer_output_rows.astype(jnp.float32)).astype(jnp.bfloat16)
    flat_rows = path_states.reshape(REQUEST_TOTAL * PATH, MODEL_SIZE).astype(jnp.float32)
    mean_square = lax.optimization_barrier(jnp.mean(flat_rows * flat_rows, axis=1))
    norm_values = jnp.sqrt(mean_square + eps_norm).reshape(REQUEST_TOTAL, PATH)
    head_in = (flat_rows * lax.rsqrt(mean_square + eps_norm)[:, None] * final_gain.astype(jnp.float32)).astype(jnp.bfloat16)
    maxima = lax.optimization_barrier(jnp.max(jnp.dot(head_in, head_weight, preferred_element_type=jnp.float32), axis=1)).reshape(REQUEST_TOTAL, PATH)
    return (layer_output_rows, accepted_keys, accepted_values, norm_values, maxima)
```

```python
import jax
import jax.numpy as jnp
from jax import lax
from jax.sharding import PartitionSpec as P

HEAD_SIZE = 96


eps_norm = 1e-05
rope_base = 100000.0
masked_score = -1e30


def apply_rotation(values, token_positions):
    half_dim = values.shape[-1] // 2
    inverse = rope_base ** (-jnp.arange(half_dim, dtype=jnp.float32) * 2.0 / values.shape[-1])
    angles = token_positions.astype(jnp.float32)[:, None] * inverse[None, :]
    cosine = jnp.cos(angles)[:, None, :]
    sine_of = jnp.sin(angles)[:, None, :]
    first_half = values[..., :half_dim]
    second_half = values[..., half_dim:]
    return jnp.concatenate(
        [first_half * cosine - second_half * sine_of, second_half * cosine + first_half * sine_of],
        axis=-1,
    )


def ancestors(parents):
    draft_length = parents.shape[-1]
    columns = jnp.arange(draft_length, dtype=jnp.int32)
    reached = jnp.eye(draft_length, dtype=jnp.float32) + (parents[..., :, None] == columns).astype(
        jnp.float32
    )
    for sweep_number in range((draft_length - 1).bit_length()):
        reached = jnp.minimum(
            jnp.einsum("bij,bjk->bik", reached, reached, precision=lax.Precision.HIGHEST), 1.0
        )
    return reached


def scatter_rows(partial, axis_name, shards):
    rows = partial.shape[0] // shards
    pieces = partial.reshape(shards, rows, *partial.shape[1:])
    arrived = lax.all_to_all(pieces, axis_name, split_axis=0, concat_axis=0, tiled=True)
    return jnp.sum(arrived, axis=0)


def gather_rows(chunk, axis_name, shards):
    copies = jnp.broadcast_to(chunk[None], (shards, *chunk.shape))
    arrived = lax.all_to_all(copies, axis_name, split_axis=0, concat_axis=0, tiled=True)
    return arrived.reshape(shards * chunk.shape[0], *chunk.shape[1:])


def per_device(
    draft_states,
    parents,
    live_draft_count,
    path_index,
    cached_length_list,
    cached_key_rows,
    cached_value_rows,
    attend_gain,
    hidden_gain,
    final_gain,
    query_weight,
    key_matrix,
    value_matrix,
    out_weight,
    gate_weight,
    up_weight,
    down_weight,
    head_weight,
):
    local_requests, draft_length, model_width = draft_states.shape
    token_rows = local_requests * draft_length
    request_shards = lax.axis_size("req")
    request_shard = lax.axis_index("req")
    vocab_shards = lax.axis_size("vocab")
    vocab_shard = lax.axis_index("vocab")
    head_dim = HEAD_SIZE
    key_local = key_matrix.shape[1] // head_dim
    query_local = query_weight.shape[1] // head_dim
    group_factor = query_local // key_local
    pool_rows = cached_key_rows.shape[0]
    states = draft_states.reshape(token_rows, model_width).astype(jnp.float32)
    normalized_states = (
        states
        * lax.rsqrt(jnp.mean(states * states, axis=1, keepdims=True) + eps_norm)
        * attend_gain.astype(jnp.float32)
    ).astype(jnp.bfloat16)
    reached = ancestors(parents)
    token_positions = (
        cached_length_list[:, None] + (jnp.sum(reached, axis=2) - 1.0).astype(jnp.int32)
    ).reshape(token_rows)
    query_vectors = apply_rotation(
        jnp.dot(normalized_states, query_weight, preferred_element_type=jnp.float32).reshape(
            token_rows, query_local, head_dim
        ),
        token_positions,
    ).astype(jnp.bfloat16)
    fresh_keys = apply_rotation(
        jnp.dot(normalized_states, key_matrix, preferred_element_type=jnp.float32).reshape(
            token_rows, key_local, head_dim
        ),
        token_positions,
    ).astype(jnp.bfloat16)
    fresh_values = (
        jnp.dot(normalized_states, value_matrix, preferred_element_type=jnp.float32)
        .astype(jnp.bfloat16)
        .reshape(token_rows, key_local, head_dim)
    )
    score_scale = head_dim ** (-0.5)
    query_rows = query_vectors.reshape(
        local_requests, draft_length, key_local, group_factor, head_dim
    ).transpose(0, 2, 1, 3, 4).reshape(
        local_requests, key_local, draft_length * group_factor, head_dim
    )
    request_keys = fresh_keys.reshape(local_requests, draft_length, key_local, head_dim)
    request_values = fresh_values.reshape(local_requests, draft_length, key_local, head_dim)
    pool_keys = cached_key_rows.reshape(pool_rows, key_local, head_dim)
    pool_values = cached_value_rows.reshape(pool_rows, key_local, head_dim)
    cache_end = jnp.cumsum(cached_length_list)
    cache_start = cache_end - cached_length_list
    slots = jnp.arange(pool_rows, dtype=jnp.int32)
    pool_allowed = (slots[None, :] >= cache_start[:, None]) & (slots[None, :] < cache_end[:, None])
    pool_allowed = pool_allowed[:, None, None, :]
    tree_allowed = jnp.repeat(reached > 0.5, group_factor, axis=1)[:, None, :, :]
    pool_scores = (
        jnp.einsum("rkqd,pkd->rkqp", query_rows, pool_keys, preferred_element_type=jnp.float32)
        * score_scale
    )
    tree_scores = (
        jnp.einsum("rkqd,rmkd->rkqm", query_rows, request_keys, preferred_element_type=jnp.float32)
        * score_scale
    )
    top = jnp.maximum(
        jnp.max(jnp.where(pool_allowed, pool_scores, masked_score), axis=3),
        jnp.max(jnp.where(tree_allowed, tree_scores, masked_score), axis=3),
    )
    pool_weights = jnp.where(pool_allowed, jnp.exp(pool_scores - top[..., None]), 0.0).astype(
        jnp.bfloat16
    )
    tree_weights = jnp.where(tree_allowed, jnp.exp(tree_scores - top[..., None]), 0.0).astype(
        jnp.bfloat16
    )
    totals = jnp.sum(pool_weights.astype(jnp.float32), axis=3) + jnp.sum(
        tree_weights.astype(jnp.float32), axis=3
    )
    weighted_values = jnp.einsum(
        "rkqp,pkd->rkqd", pool_weights, pool_values, preferred_element_type=jnp.float32
    ) + jnp.einsum(
        "rkqm,rmkd->rkqd", tree_weights, request_values, preferred_element_type=jnp.float32
    )
    attended = (
        (weighted_values / totals[..., None])
        .reshape(local_requests, key_local, draft_length, group_factor, head_dim)
        .transpose(0, 2, 1, 3, 4)
        .reshape(token_rows, query_local * head_dim)
        .astype(jnp.bfloat16)
    )
    attend_part = jnp.dot(attended, out_weight, preferred_element_type=jnp.float32)
    chunk_rows = token_rows // vocab_shards
    chunk_start = vocab_shard * chunk_rows
    residual_chunk = lax.dynamic_slice_in_dim(states, chunk_start, chunk_rows, 0) + scatter_rows(
        attend_part, "vocab", vocab_shards
    )
    hidden_chunk = (
        residual_chunk
        * lax.rsqrt(jnp.mean(residual_chunk * residual_chunk, axis=1, keepdims=True) + eps_norm)
        * hidden_gain.astype(jnp.float32)
    ).astype(jnp.bfloat16)
    hidden_in = gather_rows(hidden_chunk, "vocab", vocab_shards)
    gate_out = jnp.dot(hidden_in, gate_weight, preferred_element_type=jnp.float32)
    up_out = jnp.dot(hidden_in, up_weight, preferred_element_type=jnp.float32)
    hidden = (jax.nn.silu(gate_out) * up_out).astype(jnp.bfloat16)
    down_part = jnp.dot(hidden, down_weight, preferred_element_type=jnp.float32)
    feed_chunk = scatter_rows(down_part, "vocab", vocab_shards).astype(jnp.bfloat16)
    local_counts = lax.dynamic_slice_in_dim(
        live_draft_count, request_shard * local_requests, local_requests
    )
    chunk_token = chunk_start + jnp.arange(chunk_rows, dtype=jnp.int32)
    chunk_count = jnp.take(local_counts, chunk_token // draft_length)
    chunk_live = (chunk_token % draft_length) < chunk_count
    layer_chunk = jnp.where(
        chunk_live[:, None], residual_chunk + feed_chunk.astype(jnp.float32), 0.0
    ).astype(jnp.bfloat16)
    updated = gather_rows(layer_chunk, "vocab", vocab_shards)
    share_width = model_width // vocab_shards
    layer_part = lax.dynamic_slice_in_dim(updated, vocab_shard * share_width, share_width, 1)
    path_length = path_index.shape[1]
    request_picker = (
        path_index[:, :, None] == jnp.arange(draft_length, dtype=jnp.int32)[None, None, :]
    ).astype(jnp.bfloat16)
    accepted_keys = jnp.einsum(
        "ytm,ymu->ytu",
        request_picker,
        fresh_keys.reshape(local_requests, draft_length, key_local * head_dim),
        preferred_element_type=jnp.float32,
    ).astype(jnp.bfloat16)
    accepted_values = jnp.einsum(
        "ytm,ymu->ytu",
        request_picker,
        fresh_values.reshape(local_requests, draft_length, key_local * head_dim),
        preferred_element_type=jnp.float32,
    ).astype(jnp.bfloat16)
    per_shard = path_length // vocab_shards
    head_picker = lax.dynamic_slice_in_dim(request_picker, vocab_shard * per_shard, per_shard, 1)
    head_rows = jnp.einsum(
        "ytm,ymu->ytu",
        head_picker,
        updated.reshape(local_requests, draft_length, model_width),
        preferred_element_type=jnp.float32,
    ).astype(jnp.bfloat16)
    flat_rows = head_rows.reshape(local_requests * per_shard, model_width).astype(jnp.float32)
    mean_square = jnp.mean(flat_rows * flat_rows, axis=1)
    norm_values = jnp.sqrt(mean_square + eps_norm).reshape(local_requests, per_shard)
    head_in = (
        flat_rows * lax.rsqrt(mean_square + eps_norm)[:, None] * final_gain.astype(jnp.float32)
    ).astype(jnp.bfloat16)
    local_max = jnp.max(
        jnp.dot(
            gather_rows(head_in, "req", request_shards),
            head_weight,
            preferred_element_type=jnp.float32,
        ),
        axis=1,
    )
    every_max = gather_rows(local_max[None], "req", request_shards)
    maxima = jnp.max(every_max, axis=0).reshape(request_shards * local_requests, per_shard)
    return (
        layer_part.reshape(local_requests, draft_length, share_width),
        accepted_keys,
        accepted_values,
        norm_values,
        maxima,
    )


def solution(mesh):
    in_specs = (
        P("req", None, None),
        P("req", None),
        P(),
        P("req", None),
        P("req"),
        P("req", "vocab"),
        P("req", "vocab"),
        P(),
        P(),
        P(),
        P(None, "vocab"),
        P(None, "vocab"),
        P(None, "vocab"),
        P("vocab", None),
        P(None, "vocab"),
        P(None, "vocab"),
        P("vocab", None),
        P(None, "req"),
    )
    out_specs = (
        P("req", None, "vocab"),
        P("req", None, "vocab"),
        P("req", None, "vocab"),
        P("req", "vocab"),
        P(None, "vocab"),
    )
    return jax.shard_map(
        per_device, mesh=mesh, in_specs=in_specs, out_specs=out_specs, check_vma=False
    )
```

```python
import jax
import jax.numpy as jnp
from jax import lax
from jax.sharding import PartitionSpec as P

HEAD_SIZE = 96


eps_norm = 1e-05
rope_base = 100000.0
masked_score = -1e30


def ancestors(parents):
    draft_length = parents.shape[-1]
    columns = jnp.arange(draft_length, dtype=jnp.int32)
    reached = jnp.eye(draft_length, dtype=jnp.float32) + (parents[..., :, None] == columns).astype(
        jnp.float32
    )
    for sweep_number in range((draft_length - 1).bit_length()):
        reached = jnp.minimum(
            jnp.einsum("bij,bjk->bik", reached, reached, precision=lax.Precision.HIGHEST), 1.0
        )
    return reached


def scatter_rows(partial, axis_name, shards):
    rows = partial.shape[0] // shards
    pieces = partial.reshape(shards, rows, *partial.shape[1:]).astype(jnp.bfloat16)
    arrived = lax.all_to_all(pieces, axis_name, split_axis=0, concat_axis=0, tiled=True)
    return jnp.sum(arrived.astype(jnp.float32), axis=0)


def gather_rows(chunk, axis_name, shards):
    copies = jnp.broadcast_to(chunk[None], (shards, *chunk.shape))
    arrived = lax.all_to_all(copies, axis_name, split_axis=0, concat_axis=0, tiled=True)
    return arrived.reshape(shards * chunk.shape[0], *chunk.shape[1:])


def per_device(
    draft_states,
    parents,
    live_draft_count,
    path_index,
    cached_length_list,
    cached_key_rows,
    cached_value_rows,
    attend_gain,
    hidden_gain,
    final_gain,
    query_weight,
    key_matrix,
    value_matrix,
    out_weight,
    gate_weight,
    up_weight,
    down_weight,
    head_weight,
):
    local_requests, draft_length, model_width = draft_states.shape
    token_rows = local_requests * draft_length
    request_shards = lax.axis_size("req")
    request_shard = lax.axis_index("req")
    vocab_shards = lax.axis_size("vocab")
    vocab_shard = lax.axis_index("vocab")
    head_dim = HEAD_SIZE
    key_local = key_matrix.shape[1] // head_dim
    query_local = query_weight.shape[1] // head_dim
    group_factor = query_local // key_local
    pool_rows = cached_key_rows.shape[0]
    states = draft_states.reshape(token_rows, model_width).astype(jnp.float32)
    normalized_states = (
        states
        * lax.rsqrt(jnp.mean(states * states, axis=1, keepdims=True) + eps_norm)
        * attend_gain.astype(jnp.float32)
    ).astype(jnp.bfloat16)
    reached = ancestors(parents)
    token_positions = (
        cached_length_list[:, None] + (jnp.sum(reached, axis=2) - 1.0).astype(jnp.int32)
    ).reshape(token_rows)
    request_states = normalized_states.reshape(local_requests, draft_length, model_width)
    request_positions = token_positions.reshape(local_requests, draft_length)
    inverse = rope_base ** (-jnp.arange(head_dim // 2, dtype=jnp.float32) * 2.0 / head_dim)
    angles = request_positions.astype(jnp.float32)[:, :, None] * inverse
    cosine = jnp.cos(angles)
    sine_of = jnp.sin(angles)

    def rotate(values):
        half = head_dim // 2
        lift = (local_requests,) + (1,) * (values.ndim - 3) + (draft_length, half)
        cos_b = cosine.reshape(lift)
        sin_b = sine_of.reshape(lift)
        first_half = values[..., :half]
        second_half = values[..., half:]
        return jnp.concatenate(
            [first_half * cos_b - second_half * sin_b, second_half * cos_b + first_half * sin_b],
            axis=-1,
        )

    query_rows = rotate(
        jnp.einsum(
            "rim,mkgd->rkgid",
            request_states,
            query_weight.reshape(model_width, key_local, group_factor, head_dim),
            preferred_element_type=jnp.float32,
        )
    ).astype(jnp.bfloat16)
    fresh_keys = rotate(
        jnp.einsum(
            "rim,mkd->rkid",
            request_states,
            key_matrix.reshape(model_width, key_local, head_dim),
            preferred_element_type=jnp.float32,
        )
    ).astype(jnp.bfloat16)
    fresh_values = jnp.einsum(
        "rim,mkd->rkid",
        request_states,
        value_matrix.reshape(model_width, key_local, head_dim),
        preferred_element_type=jnp.float32,
    ).astype(jnp.bfloat16)
    score_scale = head_dim ** (-0.5)
    pool_keys = cached_key_rows.reshape(pool_rows, key_local, head_dim)
    pool_values = cached_value_rows.reshape(pool_rows, key_local, head_dim)
    earlier = (
        jnp.arange(local_requests, dtype=jnp.int32)[None, :]
        < jnp.arange(local_requests, dtype=jnp.int32)[:, None]
    )
    cache_start = jnp.sum(jnp.where(earlier, cached_length_list[None, :], 0), axis=1)
    cache_end = cache_start + cached_length_list
    slots = jnp.arange(pool_rows, dtype=jnp.int32)
    pool_allowed = (slots[None, :] >= cache_start[:, None]) & (slots[None, :] < cache_end[:, None])
    pool_allowed = pool_allowed[:, None, None, None, :]
    tree_allowed = (reached > 0.5)[:, None, None, :, :]
    pool_scores = (
        jnp.einsum("rkgid,pkd->rkgip", query_rows, pool_keys, preferred_element_type=jnp.float32)
        * score_scale
    )
    tree_scores = (
        jnp.einsum("rkgid,rkmd->rkgim", query_rows, fresh_keys, preferred_element_type=jnp.float32)
        * score_scale
    )
    top = jnp.maximum(
        jnp.max(jnp.where(pool_allowed, pool_scores, masked_score), axis=4),
        jnp.max(jnp.where(tree_allowed, tree_scores, masked_score), axis=4),
    )
    pool_weights = jnp.where(pool_allowed, jnp.exp(pool_scores - top[..., None]), 0.0).astype(
        jnp.bfloat16
    )
    tree_weights = jnp.where(tree_allowed, jnp.exp(tree_scores - top[..., None]), 0.0).astype(
        jnp.bfloat16
    )
    totals = jnp.sum(pool_weights.astype(jnp.float32), axis=4) + jnp.sum(
        tree_weights.astype(jnp.float32), axis=4
    )
    weighted_values = jnp.einsum(
        "rkgip,pkd->rkgid", pool_weights, pool_values, preferred_element_type=jnp.float32
    ) + jnp.einsum(
        "rkgim,rkmd->rkgid", tree_weights, fresh_values, preferred_element_type=jnp.float32
    )
    attended = (weighted_values / totals[..., None]).astype(jnp.bfloat16)
    attend_part = jnp.einsum(
        "rkgid,kgdn->rin",
        attended,
        out_weight.reshape(key_local, group_factor, head_dim, model_width),
        preferred_element_type=jnp.float32,
    ).reshape(token_rows, model_width)
    fresh_keys = fresh_keys.transpose(0, 2, 1, 3)
    fresh_values = fresh_values.transpose(0, 2, 1, 3)
    chunk_rows = token_rows // vocab_shards
    chunk_start = vocab_shard * chunk_rows
    residual_chunk = lax.dynamic_slice_in_dim(states, chunk_start, chunk_rows, 0) + scatter_rows(
        attend_part, "vocab", vocab_shards
    )
    hidden_chunk = (
        residual_chunk
        * lax.rsqrt(jnp.mean(residual_chunk * residual_chunk, axis=1, keepdims=True) + eps_norm)
        * hidden_gain.astype(jnp.float32)
    ).astype(jnp.bfloat16)
    hidden_in = gather_rows(hidden_chunk, "vocab", vocab_shards)
    gate_out = jnp.dot(hidden_in, gate_weight, preferred_element_type=jnp.float32)
    up_out = jnp.dot(hidden_in, up_weight, preferred_element_type=jnp.float32)
    hidden = (jax.nn.silu(gate_out) * up_out).astype(jnp.bfloat16)
    down_part = jnp.dot(hidden, down_weight, preferred_element_type=jnp.float32)
    feed_chunk = scatter_rows(down_part, "vocab", vocab_shards).astype(jnp.bfloat16)
    local_counts = lax.dynamic_slice_in_dim(
        live_draft_count, request_shard * local_requests, local_requests
    )
    chunk_token = chunk_start + jnp.arange(chunk_rows, dtype=jnp.int32)
    chunk_count = jnp.take(local_counts, chunk_token // draft_length)
    chunk_live = (chunk_token % draft_length) < chunk_count
    layer_chunk = jnp.where(
        chunk_live[:, None], residual_chunk + feed_chunk.astype(jnp.float32), 0.0
    ).astype(jnp.bfloat16)
    updated = gather_rows(layer_chunk, "vocab", vocab_shards)
    share_width = model_width // vocab_shards
    layer_part = lax.dynamic_slice_in_dim(updated, vocab_shard * share_width, share_width, 1)
    path_length = path_index.shape[1]
    request_picker = (
        path_index[:, :, None] == jnp.arange(draft_length, dtype=jnp.int32)[None, None, :]
    ).astype(jnp.bfloat16)
    accepted_keys = jnp.einsum(
        "ytm,ymu->ytu",
        request_picker,
        fresh_keys.reshape(local_requests, draft_length, key_local * head_dim),
        preferred_element_type=jnp.float32,
    ).astype(jnp.bfloat16)
    accepted_values = jnp.einsum(
        "ytm,ymu->ytu",
        request_picker,
        fresh_values.reshape(local_requests, draft_length, key_local * head_dim),
        preferred_element_type=jnp.float32,
    ).astype(jnp.bfloat16)
    per_shard = path_length // vocab_shards
    head_picker = lax.dynamic_slice_in_dim(request_picker, vocab_shard * per_shard, per_shard, 1)
    head_rows = jnp.einsum(
        "ytm,ymu->ytu",
        head_picker,
        updated.reshape(local_requests, draft_length, model_width),
        preferred_element_type=jnp.float32,
    ).astype(jnp.bfloat16)
    flat_rows = head_rows.reshape(local_requests * per_shard, model_width).astype(jnp.float32)
    mean_square = jnp.mean(flat_rows * flat_rows, axis=1)
    norm_values = jnp.sqrt(mean_square + eps_norm).reshape(local_requests, per_shard)
    head_in = (
        flat_rows * lax.rsqrt(mean_square + eps_norm)[:, None] * final_gain.astype(jnp.float32)
    ).astype(jnp.bfloat16)
    local_max = jnp.max(
        jnp.dot(
            gather_rows(head_in, "req", request_shards),
            head_weight,
            preferred_element_type=jnp.float32,
        ),
        axis=1,
    )
    every_max = gather_rows(local_max[None], "req", request_shards)
    maxima = jnp.max(every_max, axis=0).reshape(request_shards * local_requests, per_shard)
    return (
        layer_part.reshape(local_requests, draft_length, share_width),
        accepted_keys,
        accepted_values,
        norm_values,
        maxima,
    )


def solution(mesh):
    in_specs = (
        P("req", None, None),
        P("req", None),
        P(),
        P("req", None),
        P("req"),
        P("req", "vocab"),
        P("req", "vocab"),
        P(),
        P(),
        P(),
        P(None, "vocab"),
        P(None, "vocab"),
        P(None, "vocab"),
        P("vocab", None),
        P(None, "vocab"),
        P(None, "vocab"),
        P("vocab", None),
        P(None, "req"),
    )
    out_specs = (
        P("req", None, "vocab"),
        P("req", None, "vocab"),
        P("req", None, "vocab"),
        P("req", "vocab"),
        P(None, "vocab"),
    )
    return jax.shard_map(
        per_device, mesh=mesh, in_specs=in_specs, out_specs=out_specs, check_vma=False
    )
```

```python
import jax
import jax.numpy as jnp
from jax import lax
from jax.sharding import PartitionSpec as P

HEAD_SIZE = 96


eps_norm = 1e-05
rope_base = 100000.0
masked_score = -1e30


def ancestors(parents):
    draft_length = parents.shape[-1]
    columns = jnp.arange(draft_length, dtype=jnp.int32)
    reached = jnp.eye(draft_length, dtype=jnp.float32) + (parents[..., :, None] == columns).astype(
        jnp.float32
    )
    for sweep_number in range((draft_length - 1).bit_length()):
        reached = jnp.minimum(
            jnp.einsum("bij,bjk->bik", reached, reached, precision=lax.Precision.HIGHEST), 1.0
        )
    return reached


def scatter_rows(partial, axis_name, shards):
    rows = partial.shape[0] // shards
    pieces = partial.reshape(shards, rows, *partial.shape[1:]).astype(jnp.bfloat16)
    arrived = lax.all_to_all(pieces, axis_name, split_axis=0, concat_axis=0, tiled=True)
    return jnp.sum(arrived.astype(jnp.float32), axis=0)


def gather_rows(chunk, axis_name, shards):
    copies = jnp.broadcast_to(chunk[None], (shards, *chunk.shape))
    arrived = lax.all_to_all(copies, axis_name, split_axis=0, concat_axis=0, tiled=True)
    return arrived.reshape(shards * chunk.shape[0], *chunk.shape[1:])


def per_device(
    draft_states,
    parents,
    live_draft_count,
    path_index,
    cached_length_list,
    cached_key_rows,
    cached_value_rows,
    attend_gain,
    hidden_gain,
    final_gain,
    query_weight,
    key_matrix,
    value_matrix,
    out_weight,
    gate_weight,
    up_weight,
    down_weight,
    head_weight,
):
    local_requests, draft_length, model_width = draft_states.shape
    token_rows = local_requests * draft_length
    request_shards = lax.axis_size("req")
    request_shard = lax.axis_index("req")
    vocab_shards = lax.axis_size("vocab")
    vocab_shard = lax.axis_index("vocab")
    head_dim = HEAD_SIZE
    key_local = key_matrix.shape[1] // head_dim
    query_local = query_weight.shape[1] // head_dim
    group_factor = query_local // key_local
    pool_rows = cached_key_rows.shape[0]
    states = draft_states.reshape(token_rows, model_width).astype(jnp.float32)
    normalized_states = (
        states
        * lax.rsqrt(jnp.mean(states * states, axis=1, keepdims=True) + eps_norm)
        * attend_gain.astype(jnp.float32)
    ).astype(jnp.bfloat16)
    reached = ancestors(parents)
    token_positions = (
        cached_length_list[:, None] + (jnp.sum(reached, axis=2) - 1.0).astype(jnp.int32)
    ).reshape(token_rows)
    request_states = normalized_states.reshape(local_requests, draft_length, model_width)
    request_positions = token_positions.reshape(local_requests, draft_length)
    inverse = rope_base ** (-jnp.arange(head_dim // 2, dtype=jnp.float32) * 2.0 / head_dim)
    angles = request_positions.astype(jnp.float32)[:, :, None] * inverse
    cosine = jnp.cos(angles)
    sine_of = jnp.sin(angles)

    def rotate(values):
        half = head_dim // 2
        lift = (local_requests,) + (1,) * (values.ndim - 3) + (draft_length, half)
        cos_b = cosine.reshape(lift)
        sin_b = sine_of.reshape(lift)
        first_half = values[..., :half]
        second_half = values[..., half:]
        return jnp.concatenate(
            [first_half * cos_b - second_half * sin_b, second_half * cos_b + first_half * sin_b],
            axis=-1,
        )

    query_rows = rotate(
        jnp.einsum(
            "rim,mkgd->rkgid",
            request_states,
            query_weight.reshape(model_width, key_local, group_factor, head_dim),
            preferred_element_type=jnp.float32,
        )
    ).astype(jnp.bfloat16)
    fresh_keys = rotate(
        jnp.einsum(
            "rim,mkd->rkid",
            request_states,
            key_matrix.reshape(model_width, key_local, head_dim),
            preferred_element_type=jnp.float32,
        )
    ).astype(jnp.bfloat16)
    fresh_values = jnp.einsum(
        "rim,mkd->rkid",
        request_states,
        value_matrix.reshape(model_width, key_local, head_dim),
        preferred_element_type=jnp.float32,
    ).astype(jnp.bfloat16)
    score_scale = head_dim ** (-0.5)
    pool_keys = cached_key_rows.reshape(pool_rows, key_local, head_dim)
    pool_values = cached_value_rows.reshape(pool_rows, key_local, head_dim)
    earlier = (
        jnp.arange(local_requests, dtype=jnp.int32)[None, :]
        < jnp.arange(local_requests, dtype=jnp.int32)[:, None]
    )
    cache_start = jnp.sum(jnp.where(earlier, cached_length_list[None, :], 0), axis=1)
    cache_end = cache_start + cached_length_list
    slots = jnp.arange(pool_rows, dtype=jnp.int32)
    pool_allowed = (slots[None, :] >= cache_start[:, None]) & (slots[None, :] < cache_end[:, None])
    pool_allowed = pool_allowed[:, None, None, None, :]
    tree_allowed = (reached > 0.5)[:, None, None, :, :]
    pool_scores = (
        jnp.einsum("rkgid,pkd->rkgip", query_rows, pool_keys, preferred_element_type=jnp.float32)
        * score_scale
    )
    tree_scores = (
        jnp.einsum("rkgid,rkmd->rkgim", query_rows, fresh_keys, preferred_element_type=jnp.float32)
        * score_scale
    )
    top = jnp.maximum(
        jnp.max(jnp.where(pool_allowed, pool_scores, masked_score), axis=4),
        jnp.max(jnp.where(tree_allowed, tree_scores, masked_score), axis=4),
    )
    pool_weights = jnp.where(pool_allowed, jnp.exp(pool_scores - top[..., None]), 0.0).astype(
        jnp.bfloat16
    )
    tree_weights = jnp.where(tree_allowed, jnp.exp(tree_scores - top[..., None]), 0.0).astype(
        jnp.bfloat16
    )
    totals = jnp.sum(pool_weights.astype(jnp.float32), axis=4) + jnp.sum(
        tree_weights.astype(jnp.float32), axis=4
    )
    weighted_values = jnp.einsum(
        "rkgip,pkd->rkgid", pool_weights, pool_values, preferred_element_type=jnp.float32
    ) + jnp.einsum(
        "rkgim,rkmd->rkgid", tree_weights, fresh_values, preferred_element_type=jnp.float32
    )
    attended = (weighted_values / totals[..., None]).astype(jnp.bfloat16)
    attend_part = jnp.einsum(
        "rkgid,kgdn->rin",
        attended,
        out_weight.reshape(key_local, group_factor, head_dim, model_width),
        preferred_element_type=jnp.float32,
    ).reshape(token_rows, model_width)
    fresh_keys = fresh_keys.transpose(0, 2, 1, 3)
    fresh_values = fresh_values.transpose(0, 2, 1, 3)
    chunk_rows = token_rows // vocab_shards
    chunk_start = vocab_shard * chunk_rows
    share_width = model_width // vocab_shards
    share_start = vocab_shard * share_width
    path_length = path_index.shape[1]
    per_shard = path_length // vocab_shards
    path_count = local_requests * per_shard
    path_rows_all = (
        (
            path_index.reshape(local_requests, vocab_shards, per_shard)
            + (jnp.arange(local_requests, dtype=jnp.int32) * draft_length)[:, None, None]
        )
        .transpose(1, 0, 2)
        .reshape(vocab_shards, path_count)
    )
    own_path_rows = lax.dynamic_index_in_dim(path_rows_all, vocab_shard, keepdims=False)

    def row_pieces(partial):
        return partial.reshape(vocab_shards, chunk_rows * model_width)

    def column_pieces(partial):
        return (
            partial.reshape(token_rows, vocab_shards, share_width)
            .transpose(1, 0, 2)
            .reshape(vocab_shards, token_rows * share_width)
        )

    def path_pieces(partial):
        return jnp.take(partial, path_rows_all.reshape(-1), axis=0).reshape(
            vocab_shards, path_count * model_width
        )

    def exchange(pieces):
        widths = [piece.shape[1] for piece in pieces]
        packed = jnp.concatenate([piece.astype(jnp.bfloat16) for piece in pieces], axis=1)
        arrived = lax.all_to_all(packed, "vocab", split_axis=0, concat_axis=0, tiled=True)
        summed = jnp.sum(arrived.astype(jnp.float32), axis=0)
        parts = []
        at = 0
        for width in widths:
            parts.append(summed[at : at + width])
            at += width
        return parts

    attn_rows, attn_cols, attn_path = exchange(
        [row_pieces(attend_part), column_pieces(attend_part), path_pieces(attend_part)]
    )
    residual_chunk = lax.dynamic_slice_in_dim(
        states, chunk_start, chunk_rows, 0
    ) + attn_rows.reshape(chunk_rows, model_width)
    residual_cols = lax.dynamic_slice_in_dim(
        states, share_start, share_width, 1
    ) + attn_cols.reshape(token_rows, share_width)
    residual_path = jnp.take(states, own_path_rows, axis=0) + attn_path.reshape(
        path_count, model_width
    )
    hidden_chunk = (
        residual_chunk
        * lax.rsqrt(jnp.mean(residual_chunk * residual_chunk, axis=1, keepdims=True) + eps_norm)
        * hidden_gain.astype(jnp.float32)
    ).astype(jnp.bfloat16)
    hidden_in = gather_rows(hidden_chunk, "vocab", vocab_shards)
    gate_out = jnp.dot(hidden_in, gate_weight, preferred_element_type=jnp.float32)
    up_out = jnp.dot(hidden_in, up_weight, preferred_element_type=jnp.float32)
    hidden = (jax.nn.silu(gate_out) * up_out).astype(jnp.bfloat16)
    down_part = jnp.dot(hidden, down_weight, preferred_element_type=jnp.float32)
    feed_cols, feed_path = exchange([column_pieces(down_part), path_pieces(down_part)])
    feed_cols = feed_cols.reshape(token_rows, share_width).astype(jnp.bfloat16)
    feed_path = feed_path.reshape(path_count, model_width).astype(jnp.bfloat16)
    local_counts = lax.dynamic_slice_in_dim(
        live_draft_count, request_shard * local_requests, local_requests
    )
    token_number = jnp.arange(token_rows, dtype=jnp.int32)
    live_rows = (token_number % draft_length) < jnp.take(local_counts, token_number // draft_length)
    layer_part = jnp.where(
        live_rows[:, None], residual_cols + feed_cols.astype(jnp.float32), 0.0
    ).astype(jnp.bfloat16)
    path_live = (own_path_rows % draft_length) < jnp.take(
        local_counts, own_path_rows // draft_length
    )
    head_rows = jnp.where(
        path_live[:, None], residual_path + feed_path.astype(jnp.float32), 0.0
    ).astype(jnp.bfloat16)
    request_picker = (
        path_index[:, :, None] == jnp.arange(draft_length, dtype=jnp.int32)[None, None, :]
    ).astype(jnp.bfloat16)
    accepted_keys = jnp.einsum(
        "ytm,ymu->ytu",
        request_picker,
        fresh_keys.reshape(local_requests, draft_length, key_local * head_dim),
        preferred_element_type=jnp.float32,
    ).astype(jnp.bfloat16)
    accepted_values = jnp.einsum(
        "ytm,ymu->ytu",
        request_picker,
        fresh_values.reshape(local_requests, draft_length, key_local * head_dim),
        preferred_element_type=jnp.float32,
    ).astype(jnp.bfloat16)
    flat_rows = head_rows.astype(jnp.float32)
    mean_square = jnp.mean(flat_rows * flat_rows, axis=1)
    norm_values = jnp.sqrt(mean_square + eps_norm).reshape(local_requests, per_shard)
    head_in = (
        flat_rows * lax.rsqrt(mean_square + eps_norm)[:, None] * final_gain.astype(jnp.float32)
    ).astype(jnp.bfloat16)
    local_max = jnp.max(
        jnp.dot(
            gather_rows(head_in, "req", request_shards),
            head_weight,
            preferred_element_type=jnp.float32,
        ),
        axis=1,
    )
    every_max = gather_rows(local_max[None], "req", request_shards)
    maxima = jnp.max(every_max, axis=0).reshape(request_shards * local_requests, per_shard)
    return (
        layer_part.reshape(local_requests, draft_length, share_width),
        accepted_keys,
        accepted_values,
        norm_values,
        maxima,
    )


def solution(mesh):
    in_specs = (
        P("req", None, None),
        P("req", None),
        P(),
        P("req", None),
        P("req"),
        P("req", "vocab"),
        P("req", "vocab"),
        P(),
        P(),
        P(),
        P(None, "vocab"),
        P(None, "vocab"),
        P(None, "vocab"),
        P("vocab", None),
        P(None, "vocab"),
        P(None, "vocab"),
        P("vocab", None),
        P(None, "req"),
    )
    out_specs = (
        P("req", None, "vocab"),
        P("req", None, "vocab"),
        P("req", None, "vocab"),
        P("req", "vocab"),
        P(None, "vocab"),
    )
    return jax.shard_map(
        per_device, mesh=mesh, in_specs=in_specs, out_specs=out_specs, check_vma=False
    )
```

```python
import jax
import jax.numpy as jnp
from jax import lax
from jax.sharding import PartitionSpec as P

HEAD_SIZE = 96


eps_norm = 1e-05
rope_base = 100000.0
masked_score = -1e30


def ancestors(parents):
    draft_length = parents.shape[-1]
    columns = jnp.arange(draft_length, dtype=jnp.int32)
    reached = jnp.eye(draft_length, dtype=jnp.float32) + (parents[..., :, None] == columns).astype(
        jnp.float32
    )
    for sweep_number in range((draft_length - 1).bit_length()):
        reached = jnp.minimum(
            jnp.einsum("bij,bjk->bik", reached, reached, precision=lax.Precision.HIGHEST), 1.0
        )
    return reached


def scatter_rows(partial, axis_name, shards):
    rows = partial.shape[0] // shards
    pieces = partial.reshape(shards, rows, *partial.shape[1:]).astype(jnp.bfloat16)
    arrived = lax.all_to_all(pieces, axis_name, split_axis=0, concat_axis=0, tiled=True)
    return jnp.sum(arrived.astype(jnp.float32), axis=0)


def gather_rows(chunk, axis_name, shards):
    copies = jnp.broadcast_to(chunk[None], (shards, *chunk.shape))
    arrived = lax.all_to_all(copies, axis_name, split_axis=0, concat_axis=0, tiled=True)
    return arrived.reshape(shards * chunk.shape[0], *chunk.shape[1:])


def per_device(
    draft_states,
    parents,
    live_draft_count,
    path_index,
    cached_length_list,
    cached_key_rows,
    cached_value_rows,
    attend_gain,
    hidden_gain,
    final_gain,
    query_weight,
    key_matrix,
    value_matrix,
    out_weight,
    gate_weight,
    up_weight,
    down_weight,
    head_weight,
):
    local_requests, draft_length, model_width = draft_states.shape
    token_rows = local_requests * draft_length
    request_shards = lax.axis_size("req")
    request_shard = lax.axis_index("req")
    vocab_shards = lax.axis_size("vocab")
    vocab_shard = lax.axis_index("vocab")
    head_dim = HEAD_SIZE
    key_local = key_matrix.shape[1] // head_dim
    query_local = query_weight.shape[1] // head_dim
    group_factor = query_local // key_local
    pool_rows = cached_key_rows.shape[0]
    states = draft_states.reshape(token_rows, model_width).astype(jnp.float32)
    normalized_states = (
        states
        * lax.rsqrt(jnp.mean(states * states, axis=1, keepdims=True) + eps_norm)
        * attend_gain.astype(jnp.float32)
    ).astype(jnp.bfloat16)
    reached = ancestors(parents)
    token_positions = (
        cached_length_list[:, None] + (jnp.sum(reached, axis=2) - 1.0).astype(jnp.int32)
    ).reshape(token_rows)
    request_states = normalized_states.reshape(local_requests, draft_length, model_width)
    request_positions = token_positions.reshape(local_requests, draft_length)
    inverse = rope_base ** (-jnp.arange(head_dim // 2, dtype=jnp.float32) * 2.0 / head_dim)
    angles = request_positions.astype(jnp.float32)[:, :, None] * inverse
    cosine = jnp.cos(angles)
    sine_of = jnp.sin(angles)

    def rotate(values):
        half = head_dim // 2
        lift = (local_requests,) + (1,) * (values.ndim - 3) + (draft_length, half)
        cos_b = cosine.reshape(lift)
        sin_b = sine_of.reshape(lift)
        first_half = values[..., :half]
        second_half = values[..., half:]
        return jnp.concatenate(
            [first_half * cos_b - second_half * sin_b, second_half * cos_b + first_half * sin_b],
            axis=-1,
        )

    query_rows = rotate(
        jnp.einsum(
            "rim,mkgd->rkgid",
            request_states,
            query_weight.reshape(model_width, key_local, group_factor, head_dim),
            preferred_element_type=jnp.float32,
        )
    ).astype(jnp.bfloat16)
    fresh_keys = rotate(
        jnp.einsum(
            "rim,mkd->rkid",
            request_states,
            key_matrix.reshape(model_width, key_local, head_dim),
            preferred_element_type=jnp.float32,
        )
    ).astype(jnp.bfloat16)
    fresh_values = jnp.einsum(
        "rim,mkd->rkid",
        request_states,
        value_matrix.reshape(model_width, key_local, head_dim),
        preferred_element_type=jnp.float32,
    ).astype(jnp.bfloat16)
    score_scale = head_dim ** (-0.5)
    pool_keys = cached_key_rows.reshape(pool_rows, key_local, head_dim)
    pool_values = cached_value_rows.reshape(pool_rows, key_local, head_dim)
    earlier = (
        jnp.arange(local_requests, dtype=jnp.int32)[None, :]
        < jnp.arange(local_requests, dtype=jnp.int32)[:, None]
    )
    cache_start = jnp.sum(jnp.where(earlier, cached_length_list[None, :], 0), axis=1)
    cache_end = cache_start + cached_length_list
    slots = jnp.arange(pool_rows, dtype=jnp.int32)
    pool_allowed = (slots[None, :] >= cache_start[:, None]) & (slots[None, :] < cache_end[:, None])
    pool_allowed = pool_allowed[:, None, None, None, :]
    tree_allowed = (reached > 0.5)[:, None, None, :, :]
    pool_scores = (
        jnp.einsum("rkgid,pkd->rkgip", query_rows, pool_keys, preferred_element_type=jnp.float32)
        * score_scale
    )
    tree_scores = (
        jnp.einsum("rkgid,rkmd->rkgim", query_rows, fresh_keys, preferred_element_type=jnp.float32)
        * score_scale
    )
    top = jnp.maximum(
        jnp.max(jnp.where(pool_allowed, pool_scores, masked_score), axis=4),
        jnp.max(jnp.where(tree_allowed, tree_scores, masked_score), axis=4),
    )
    pool_weights = jnp.where(pool_allowed, jnp.exp(pool_scores - top[..., None]), 0.0).astype(
        jnp.bfloat16
    )
    tree_weights = jnp.where(tree_allowed, jnp.exp(tree_scores - top[..., None]), 0.0).astype(
        jnp.bfloat16
    )
    totals = jnp.sum(pool_weights.astype(jnp.float32), axis=4) + jnp.sum(
        tree_weights.astype(jnp.float32), axis=4
    )
    weighted_values = jnp.einsum(
        "rkgip,pkd->rkgid", pool_weights, pool_values, preferred_element_type=jnp.float32
    ) + jnp.einsum(
        "rkgim,rkmd->rkgid", tree_weights, fresh_values, preferred_element_type=jnp.float32
    )
    attended = (weighted_values / totals[..., None]).astype(jnp.bfloat16)
    attend_part = jnp.einsum(
        "rkgid,kgdn->rin",
        attended,
        out_weight.reshape(key_local, group_factor, head_dim, model_width),
        preferred_element_type=jnp.float32,
    ).reshape(token_rows, model_width)
    fresh_keys = fresh_keys.transpose(0, 2, 1, 3)
    fresh_values = fresh_values.transpose(0, 2, 1, 3)
    chunk_rows = token_rows // vocab_shards
    chunk_start = vocab_shard * chunk_rows
    residual_chunk = lax.dynamic_slice_in_dim(states, chunk_start, chunk_rows, 0) + scatter_rows(
        attend_part, "vocab", vocab_shards
    )
    hidden_chunk = (
        residual_chunk
        * lax.rsqrt(jnp.mean(residual_chunk * residual_chunk, axis=1, keepdims=True) + eps_norm)
        * hidden_gain.astype(jnp.float32)
    ).astype(jnp.bfloat16)
    hidden_in = gather_rows(hidden_chunk, "vocab", vocab_shards)
    gate_out = jnp.dot(hidden_in, gate_weight, preferred_element_type=jnp.float32)
    up_out = jnp.dot(hidden_in, up_weight, preferred_element_type=jnp.float32)
    hidden = (jax.nn.silu(gate_out) * up_out).astype(jnp.bfloat16)
    down_part = jnp.dot(hidden, down_weight, preferred_element_type=jnp.float32)
    feed_chunk = scatter_rows(down_part, "vocab", vocab_shards).astype(jnp.bfloat16)
    local_counts = lax.dynamic_slice_in_dim(
        live_draft_count, request_shard * local_requests, local_requests
    )
    chunk_token = chunk_start + jnp.arange(chunk_rows, dtype=jnp.int32)
    chunk_count = jnp.take(local_counts, chunk_token // draft_length)
    chunk_live = (chunk_token % draft_length) < chunk_count
    layer_chunk = jnp.where(
        chunk_live[:, None], residual_chunk + feed_chunk.astype(jnp.float32), 0.0
    ).astype(jnp.bfloat16)
    share_width = model_width // vocab_shards
    path_length = path_index.shape[1]
    per_shard = path_length // vocab_shards
    path_count = local_requests * per_shard
    path_rows_all = (
        (
            path_index.reshape(local_requests, vocab_shards, per_shard)
            + (jnp.arange(local_requests, dtype=jnp.int32) * draft_length)[:, None, None]
        )
        .transpose(1, 0, 2)
        .reshape(vocab_shards, path_count)
    )
    column_pieces = (
        layer_chunk.reshape(chunk_rows, vocab_shards, share_width)
        .transpose(1, 0, 2)
        .reshape(vocab_shards, chunk_rows * share_width)
    )
    in_chunk = (
        path_rows_all[:, :, None] == chunk_token[None, None, :]
    ).astype(jnp.bfloat16)
    path_pieces = (
        jnp.einsum("vjt,tf->vjf", in_chunk, layer_chunk, preferred_element_type=jnp.float32)
        .astype(jnp.bfloat16)
        .reshape(vocab_shards, path_count * model_width)
    )
    arrived = lax.all_to_all(
        jnp.concatenate([column_pieces, path_pieces], axis=1),
        "vocab",
        split_axis=0,
        concat_axis=0,
        tiled=True,
    )
    layer_part = arrived[:, : chunk_rows * share_width].reshape(token_rows, share_width)
    head_rows = (
        jnp.sum(arrived[:, chunk_rows * share_width :].astype(jnp.float32), axis=0)
        .reshape(path_count, model_width)
        .astype(jnp.bfloat16)
    )
    request_picker = (
        path_index[:, :, None] == jnp.arange(draft_length, dtype=jnp.int32)[None, None, :]
    ).astype(jnp.bfloat16)
    accepted_keys = jnp.einsum(
        "ytm,ymu->ytu",
        request_picker,
        fresh_keys.reshape(local_requests, draft_length, key_local * head_dim),
        preferred_element_type=jnp.float32,
    ).astype(jnp.bfloat16)
    accepted_values = jnp.einsum(
        "ytm,ymu->ytu",
        request_picker,
        fresh_values.reshape(local_requests, draft_length, key_local * head_dim),
        preferred_element_type=jnp.float32,
    ).astype(jnp.bfloat16)
    flat_rows = head_rows.astype(jnp.float32)
    mean_square = jnp.mean(flat_rows * flat_rows, axis=1)
    norm_values = jnp.sqrt(mean_square + eps_norm).reshape(local_requests, per_shard)
    head_in = (
        flat_rows * lax.rsqrt(mean_square + eps_norm)[:, None] * final_gain.astype(jnp.float32)
    ).astype(jnp.bfloat16)
    local_max = jnp.max(
        jnp.dot(
            gather_rows(head_in, "req", request_shards),
            head_weight,
            preferred_element_type=jnp.float32,
        ),
        axis=1,
    )
    every_max = gather_rows(local_max[None], "req", request_shards)
    maxima = jnp.max(every_max, axis=0).reshape(request_shards * local_requests, per_shard)
    return (
        layer_part.reshape(local_requests, draft_length, share_width),
        accepted_keys,
        accepted_values,
        norm_values,
        maxima,
    )


def solution(mesh):
    in_specs = (
        P("req", None, None),
        P("req", None),
        P(),
        P("req", None),
        P("req"),
        P("req", "vocab"),
        P("req", "vocab"),
        P(),
        P(),
        P(),
        P(None, "vocab"),
        P(None, "vocab"),
        P(None, "vocab"),
        P("vocab", None),
        P(None, "vocab"),
        P(None, "vocab"),
        P("vocab", None),
        P(None, "req"),
    )
    out_specs = (
        P("req", None, "vocab"),
        P("req", None, "vocab"),
        P("req", None, "vocab"),
        P("req", "vocab"),
        P(None, "vocab"),
    )
    return jax.shard_map(
        per_device, mesh=mesh, in_specs=in_specs, out_specs=out_specs, check_vma=False
    )
```

```python
import jax
import jax.numpy as jnp
from jax import lax
from jax.sharding import PartitionSpec as P

HEAD_SIZE = 96


eps_norm = 1e-05
rope_base = 100000.0
masked_score = -1e30


def ancestors(parents):
    draft_length = parents.shape[-1]
    columns = jnp.arange(draft_length, dtype=jnp.int32)
    reached = jnp.eye(draft_length, dtype=jnp.float32) + (parents[..., :, None] == columns).astype(
        jnp.float32
    )
    for sweep_number in range((draft_length - 1).bit_length()):
        reached = jnp.minimum(
            jnp.einsum("bij,bjk->bik", reached, reached, precision=lax.Precision.HIGHEST), 1.0
        )
    return reached


def gather_rows(chunk, axis_name, shards):
    copies = jnp.broadcast_to(chunk[None], (shards, *chunk.shape))
    arrived = lax.all_to_all(copies, axis_name, split_axis=0, concat_axis=0, tiled=True)
    return arrived.reshape(shards * chunk.shape[0], *chunk.shape[1:])


def per_device(
    draft_states,
    parents,
    live_draft_count,
    path_index,
    cached_length_list,
    cached_key_rows,
    cached_value_rows,
    attend_gain,
    hidden_gain,
    final_gain,
    query_weight,
    key_matrix,
    value_matrix,
    out_weight,
    gate_weight,
    up_weight,
    down_weight,
    head_weight,
):
    local_requests, draft_length, model_width = draft_states.shape
    token_rows = local_requests * draft_length
    request_shards = lax.axis_size("req")
    request_shard = lax.axis_index("req")
    vocab_shards = lax.axis_size("vocab")
    vocab_shard = lax.axis_index("vocab")
    head_dim = HEAD_SIZE
    key_local = key_matrix.shape[1] // head_dim
    query_local = query_weight.shape[1] // head_dim
    group_factor = query_local // key_local
    pool_rows = cached_key_rows.shape[0]
    states = draft_states.reshape(token_rows, model_width).astype(jnp.float32)
    normalized_states = (
        states
        * lax.rsqrt(jnp.mean(states * states, axis=1, keepdims=True) + eps_norm)
        * attend_gain.astype(jnp.float32)
    ).astype(jnp.bfloat16)
    reached = ancestors(parents)
    token_positions = (
        cached_length_list[:, None] + (jnp.sum(reached, axis=2) - 1.0).astype(jnp.int32)
    ).reshape(token_rows)
    request_states = normalized_states.reshape(local_requests, draft_length, model_width)
    request_positions = token_positions.reshape(local_requests, draft_length)
    inverse = rope_base ** (-jnp.arange(head_dim // 2, dtype=jnp.float32) * 2.0 / head_dim)
    angles = request_positions.astype(jnp.float32)[:, :, None] * inverse
    cosine = jnp.cos(angles)
    sine_of = jnp.sin(angles)

    def rotate(values):
        half = head_dim // 2
        lift = (local_requests,) + (1,) * (values.ndim - 3) + (draft_length, half)
        cos_b = cosine.reshape(lift)
        sin_b = sine_of.reshape(lift)
        first_half = values[..., :half]
        second_half = values[..., half:]
        return jnp.concatenate(
            [first_half * cos_b - second_half * sin_b, second_half * cos_b + first_half * sin_b],
            axis=-1,
        )

    query_rows = rotate(
        jnp.einsum(
            "rim,mkgd->rkgid",
            request_states,
            query_weight.reshape(model_width, key_local, group_factor, head_dim),
            preferred_element_type=jnp.float32,
        )
    ).astype(jnp.bfloat16)
    fresh_keys = rotate(
        jnp.einsum(
            "rim,mkd->rkid",
            request_states,
            key_matrix.reshape(model_width, key_local, head_dim),
            preferred_element_type=jnp.float32,
        )
    ).astype(jnp.bfloat16)
    fresh_values = jnp.einsum(
        "rim,mkd->rkid",
        request_states,
        value_matrix.reshape(model_width, key_local, head_dim),
        preferred_element_type=jnp.float32,
    ).astype(jnp.bfloat16)
    score_scale = head_dim ** (-0.5)
    pool_keys = cached_key_rows.reshape(pool_rows, key_local, head_dim)
    pool_values = cached_value_rows.reshape(pool_rows, key_local, head_dim)
    earlier = (
        jnp.arange(local_requests, dtype=jnp.int32)[None, :]
        < jnp.arange(local_requests, dtype=jnp.int32)[:, None]
    )
    cache_start = jnp.sum(jnp.where(earlier, cached_length_list[None, :], 0), axis=1)
    cache_end = cache_start + cached_length_list
    slots = jnp.arange(pool_rows, dtype=jnp.int32)
    pool_allowed = (slots[None, :] >= cache_start[:, None]) & (slots[None, :] < cache_end[:, None])
    pool_allowed = pool_allowed[:, None, None, None, :]
    tree_allowed = (reached > 0.5)[:, None, None, :, :]
    pool_scores = (
        jnp.einsum("rkgid,pkd->rkgip", query_rows, pool_keys, preferred_element_type=jnp.float32)
        * score_scale
    )
    tree_scores = (
        jnp.einsum("rkgid,rkmd->rkgim", query_rows, fresh_keys, preferred_element_type=jnp.float32)
        * score_scale
    )
    top = jnp.maximum(
        jnp.max(jnp.where(pool_allowed, pool_scores, masked_score), axis=4),
        jnp.max(jnp.where(tree_allowed, tree_scores, masked_score), axis=4),
    )
    pool_weights = jnp.where(pool_allowed, jnp.exp(pool_scores - top[..., None]), 0.0).astype(
        jnp.bfloat16
    )
    tree_weights = jnp.where(tree_allowed, jnp.exp(tree_scores - top[..., None]), 0.0).astype(
        jnp.bfloat16
    )
    totals = jnp.sum(pool_weights.astype(jnp.float32), axis=4) + jnp.sum(
        tree_weights.astype(jnp.float32), axis=4
    )
    weighted_values = jnp.einsum(
        "rkgip,pkd->rkgid", pool_weights, pool_values, preferred_element_type=jnp.float32
    ) + jnp.einsum(
        "rkgim,rkmd->rkgid", tree_weights, fresh_values, preferred_element_type=jnp.float32
    )
    attended = (weighted_values / totals[..., None]).astype(jnp.bfloat16)
    attend_part = jnp.einsum(
        "rkgid,kgdn->rin",
        attended,
        out_weight.reshape(key_local, group_factor, head_dim, model_width),
        preferred_element_type=jnp.float32,
    ).reshape(token_rows, model_width)
    fresh_keys = fresh_keys.transpose(0, 2, 1, 3)
    fresh_values = fresh_values.transpose(0, 2, 1, 3)
    chunk_rows = token_rows // vocab_shards
    chunk_start = vocab_shard * chunk_rows
    share_width = model_width // vocab_shards
    path_length = path_index.shape[1]
    per_shard = path_length // vocab_shards
    path_count = local_requests * per_shard
    path_rows_all = (
        (
            path_index.reshape(local_requests, vocab_shards, per_shard)
            + (jnp.arange(local_requests, dtype=jnp.int32) * draft_length)[:, None, None]
        )
        .transpose(1, 0, 2)
        .reshape(vocab_shards, path_count)
    )
    own_path_rows = lax.dynamic_index_in_dim(path_rows_all, vocab_shard, keepdims=False)
    send_rows = jnp.concatenate(
        [
            jnp.arange(token_rows, dtype=jnp.int32).reshape(vocab_shards, chunk_rows),
            path_rows_all,
        ],
        axis=1,
    ).reshape(-1)

    def scatter_with_path(partial):
        pieces = jnp.take(partial.astype(jnp.bfloat16), send_rows, axis=0).reshape(
            vocab_shards, chunk_rows + path_count, model_width
        )
        arrived = lax.all_to_all(pieces, "vocab", split_axis=0, concat_axis=0, tiled=True)
        summed = jnp.sum(arrived.astype(jnp.float32), axis=0)
        return summed[:chunk_rows], summed[chunk_rows:]

    attn_chunk, attn_path = scatter_with_path(attend_part)
    residual_chunk = lax.dynamic_slice_in_dim(states, chunk_start, chunk_rows, 0) + attn_chunk
    residual_path = jnp.take(states, own_path_rows, axis=0) + attn_path
    hidden_chunk = (
        residual_chunk
        * lax.rsqrt(jnp.mean(residual_chunk * residual_chunk, axis=1, keepdims=True) + eps_norm)
        * hidden_gain.astype(jnp.float32)
    ).astype(jnp.bfloat16)
    hidden_in = gather_rows(hidden_chunk, "vocab", vocab_shards)
    gate_out = jnp.dot(hidden_in, gate_weight, preferred_element_type=jnp.float32)
    up_out = jnp.dot(hidden_in, up_weight, preferred_element_type=jnp.float32)
    hidden = (jax.nn.silu(gate_out) * up_out).astype(jnp.bfloat16)
    down_part = jnp.dot(hidden, down_weight, preferred_element_type=jnp.float32)
    feed_chunk, feed_path = scatter_with_path(down_part)
    feed_chunk = feed_chunk.astype(jnp.bfloat16)
    feed_path = feed_path.astype(jnp.bfloat16)
    local_counts = lax.dynamic_slice_in_dim(
        live_draft_count, request_shard * local_requests, local_requests
    )
    chunk_token = chunk_start + jnp.arange(chunk_rows, dtype=jnp.int32)
    chunk_count = jnp.take(local_counts, chunk_token // draft_length)
    chunk_live = (chunk_token % draft_length) < chunk_count
    layer_chunk = jnp.where(
        chunk_live[:, None], residual_chunk + feed_chunk.astype(jnp.float32), 0.0
    ).astype(jnp.bfloat16)
    column_pieces = (
        layer_chunk.reshape(chunk_rows, vocab_shards, share_width)
        .transpose(1, 0, 2)
        .reshape(vocab_shards, chunk_rows * share_width)
    )
    arrived = lax.all_to_all(column_pieces, "vocab", split_axis=0, concat_axis=0, tiled=True)
    layer_part = arrived.reshape(token_rows, share_width)
    path_live = (own_path_rows % draft_length) < jnp.take(
        local_counts, own_path_rows // draft_length
    )
    head_rows = jnp.where(
        path_live[:, None], residual_path + feed_path.astype(jnp.float32), 0.0
    ).astype(jnp.bfloat16)
    request_picker = (
        path_index[:, :, None] == jnp.arange(draft_length, dtype=jnp.int32)[None, None, :]
    ).astype(jnp.bfloat16)
    accepted_keys = jnp.einsum(
        "ytm,ymu->ytu",
        request_picker,
        fresh_keys.reshape(local_requests, draft_length, key_local * head_dim),
        preferred_element_type=jnp.float32,
    ).astype(jnp.bfloat16)
    accepted_values = jnp.einsum(
        "ytm,ymu->ytu",
        request_picker,
        fresh_values.reshape(local_requests, draft_length, key_local * head_dim),
        preferred_element_type=jnp.float32,
    ).astype(jnp.bfloat16)
    flat_rows = head_rows.astype(jnp.float32)
    mean_square = jnp.mean(flat_rows * flat_rows, axis=1)
    norm_values = jnp.sqrt(mean_square + eps_norm).reshape(local_requests, per_shard)
    head_in = (
        flat_rows * lax.rsqrt(mean_square + eps_norm)[:, None] * final_gain.astype(jnp.float32)
    ).astype(jnp.bfloat16)
    local_max = jnp.max(
        jnp.dot(
            gather_rows(head_in, "req", request_shards),
            head_weight,
            preferred_element_type=jnp.float32,
        ),
        axis=1,
    )
    every_max = gather_rows(local_max[None], "req", request_shards)
    maxima = jnp.max(every_max, axis=0).reshape(request_shards * local_requests, per_shard)
    return (
        layer_part.reshape(local_requests, draft_length, share_width),
        accepted_keys,
        accepted_values,
        norm_values,
        maxima,
    )


def solution(mesh):
    in_specs = (
        P("req", None, None),
        P("req", None),
        P(),
        P("req", None),
        P("req"),
        P("req", "vocab"),
        P("req", "vocab"),
        P(),
        P(),
        P(),
        P(None, "vocab"),
        P(None, "vocab"),
        P(None, "vocab"),
        P("vocab", None),
        P(None, "vocab"),
        P(None, "vocab"),
        P("vocab", None),
        P(None, "req"),
    )
    out_specs = (
        P("req", None, "vocab"),
        P("req", None, "vocab"),
        P("req", None, "vocab"),
        P("req", "vocab"),
        P(None, "vocab"),
    )
    return jax.shard_map(
        per_device, mesh=mesh, in_specs=in_specs, out_specs=out_specs, check_vma=False
    )
```

```python
import jax
import jax.numpy as jnp
from jax import lax
from jax.experimental import pallas as pl
from jax.experimental.pallas import tpu as pltpu
from jax.sharding import PartitionSpec as P

HEAD_SIZE = 96


eps_norm = 1e-05
rope_base = 100000.0
masked_score = -1e30


def ancestors(parents):
    draft_length = parents.shape[-1]
    columns = jnp.arange(draft_length, dtype=jnp.int32)
    reached = jnp.eye(draft_length, dtype=jnp.float32) + (parents[..., :, None] == columns).astype(
        jnp.float32
    )
    for sweep_number in range((draft_length - 1).bit_length()):
        reached = jnp.minimum(
            jnp.einsum("bij,bjk->bik", reached, reached, precision=lax.Precision.HIGHEST), 1.0
        )
    return reached


def feed_forward_kernel(x_ref, gate_ref, up_ref, down_ref, out_ref, acc_ref):
    step = pl.program_id(0)

    @pl.when(step == 0)
    def _():
        acc_ref[...] = jnp.zeros_like(acc_ref)

    x = x_ref[...]
    gate_out = jnp.dot(x, gate_ref[...], preferred_element_type=jnp.float32)
    up_out = jnp.dot(x, up_ref[...], preferred_element_type=jnp.float32)
    hidden = (gate_out / (1.0 + jnp.exp(-gate_out)) * up_out).astype(jnp.bfloat16)
    acc_ref[...] += jnp.dot(hidden, down_ref[...], preferred_element_type=jnp.float32)

    @pl.when(step == pl.num_programs(0) - 1)
    def _():
        out_ref[...] = acc_ref[...].astype(out_ref.dtype)


def feed_forward(hidden_in, gate_weight, up_weight, down_weight, block=256):
    rows, width = hidden_in.shape
    units = gate_weight.shape[1]
    block = min(block, units)
    return pl.pallas_call(
        feed_forward_kernel,
        grid=(units // block,),
        in_specs=[
            pl.BlockSpec((rows, width), lambda j: (0, 0)),
            pl.BlockSpec((width, block), lambda j: (0, j)),
            pl.BlockSpec((width, block), lambda j: (0, j)),
            pl.BlockSpec((block, width), lambda j: (j, 0)),
        ],
        out_specs=pl.BlockSpec((rows, width), lambda j: (0, 0)),
        out_shape=jax.ShapeDtypeStruct((rows, width), jnp.bfloat16),
        scratch_shapes=[pltpu.VMEM((rows, width), jnp.float32)],
        compiler_params=pltpu.CompilerParams(dimension_semantics=("arbitrary",)),
        cost_estimate=pl.CostEstimate(
            flops=6 * rows * width * units,
            transcendentals=rows * units,
            bytes_accessed=2 * (3 * width * units + 2 * rows * width),
        ),
    )(hidden_in, gate_weight, up_weight, down_weight)


def scatter_rows(partial, axis_name, shards):
    rows = partial.shape[0] // shards
    pieces = partial.reshape(shards, rows, *partial.shape[1:]).astype(jnp.bfloat16)
    arrived = lax.all_to_all(pieces, axis_name, split_axis=0, concat_axis=0, tiled=True)
    return jnp.sum(arrived.astype(jnp.float32), axis=0)


def gather_rows(chunk, axis_name, shards):
    copies = jnp.broadcast_to(chunk[None], (shards, *chunk.shape))
    arrived = lax.all_to_all(copies, axis_name, split_axis=0, concat_axis=0, tiled=True)
    return arrived.reshape(shards * chunk.shape[0], *chunk.shape[1:])


def per_device(
    draft_states,
    parents,
    live_draft_count,
    path_index,
    cached_length_list,
    cached_key_rows,
    cached_value_rows,
    attend_gain,
    hidden_gain,
    final_gain,
    query_weight,
    key_matrix,
    value_matrix,
    out_weight,
    gate_weight,
    up_weight,
    down_weight,
    head_weight,
):
    local_requests, draft_length, model_width = draft_states.shape
    token_rows = local_requests * draft_length
    request_shards = lax.axis_size("req")
    request_shard = lax.axis_index("req")
    vocab_shards = lax.axis_size("vocab")
    vocab_shard = lax.axis_index("vocab")
    head_dim = HEAD_SIZE
    key_local = key_matrix.shape[1] // head_dim
    query_local = query_weight.shape[1] // head_dim
    group_factor = query_local // key_local
    pool_rows = cached_key_rows.shape[0]
    states = draft_states.reshape(token_rows, model_width).astype(jnp.float32)
    normalized_states = (
        states
        * lax.rsqrt(jnp.mean(states * states, axis=1, keepdims=True) + eps_norm)
        * attend_gain.astype(jnp.float32)
    ).astype(jnp.bfloat16)
    reached = ancestors(parents)
    token_positions = (
        cached_length_list[:, None] + (jnp.sum(reached, axis=2) - 1.0).astype(jnp.int32)
    ).reshape(token_rows)
    request_states = normalized_states.reshape(local_requests, draft_length, model_width)
    request_positions = token_positions.reshape(local_requests, draft_length)
    inverse = rope_base ** (-jnp.arange(head_dim // 2, dtype=jnp.float32) * 2.0 / head_dim)
    angles = request_positions.astype(jnp.float32)[:, :, None] * inverse
    cosine = jnp.cos(angles)
    sine_of = jnp.sin(angles)

    def rotate(values):
        half = head_dim // 2
        lift = (local_requests,) + (1,) * (values.ndim - 3) + (draft_length, half)
        cos_b = cosine.reshape(lift)
        sin_b = sine_of.reshape(lift)
        first_half = values[..., :half]
        second_half = values[..., half:]
        return jnp.concatenate(
            [first_half * cos_b - second_half * sin_b, second_half * cos_b + first_half * sin_b],
            axis=-1,
        )

    query_rows = rotate(
        jnp.einsum(
            "rim,mkgd->rkgid",
            request_states,
            query_weight.reshape(model_width, key_local, group_factor, head_dim),
            preferred_element_type=jnp.float32,
        )
    ).astype(jnp.bfloat16)
    fresh_keys = rotate(
        jnp.einsum(
            "rim,mkd->rkid",
            request_states,
            key_matrix.reshape(model_width, key_local, head_dim),
            preferred_element_type=jnp.float32,
        )
    ).astype(jnp.bfloat16)
    fresh_values = jnp.einsum(
        "rim,mkd->rkid",
        request_states,
        value_matrix.reshape(model_width, key_local, head_dim),
        preferred_element_type=jnp.float32,
    ).astype(jnp.bfloat16)
    score_scale = head_dim ** (-0.5)
    pool_keys = cached_key_rows.reshape(pool_rows, key_local, head_dim)
    pool_values = cached_value_rows.reshape(pool_rows, key_local, head_dim)
    earlier = (
        jnp.arange(local_requests, dtype=jnp.int32)[None, :]
        < jnp.arange(local_requests, dtype=jnp.int32)[:, None]
    )
    cache_start = jnp.sum(jnp.where(earlier, cached_length_list[None, :], 0), axis=1)
    cache_end = cache_start + cached_length_list
    slots = jnp.arange(pool_rows, dtype=jnp.int32)
    pool_allowed = (slots[None, :] >= cache_start[:, None]) & (slots[None, :] < cache_end[:, None])
    pool_allowed = pool_allowed[:, None, None, None, :]
    tree_allowed = (reached > 0.5)[:, None, None, :, :]
    pool_scores = (
        jnp.einsum("rkgid,pkd->rkgip", query_rows, pool_keys, preferred_element_type=jnp.float32)
        * score_scale
    )
    tree_scores = (
        jnp.einsum("rkgid,rkmd->rkgim", query_rows, fresh_keys, preferred_element_type=jnp.float32)
        * score_scale
    )
    top = jnp.maximum(
        jnp.max(jnp.where(pool_allowed, pool_scores, masked_score), axis=4),
        jnp.max(jnp.where(tree_allowed, tree_scores, masked_score), axis=4),
    )
    pool_weights = jnp.where(pool_allowed, jnp.exp(pool_scores - top[..., None]), 0.0).astype(
        jnp.bfloat16
    )
    tree_weights = jnp.where(tree_allowed, jnp.exp(tree_scores - top[..., None]), 0.0).astype(
        jnp.bfloat16
    )
    totals = jnp.sum(pool_weights.astype(jnp.float32), axis=4) + jnp.sum(
        tree_weights.astype(jnp.float32), axis=4
    )
    weighted_values = jnp.einsum(
        "rkgip,pkd->rkgid", pool_weights, pool_values, preferred_element_type=jnp.float32
    ) + jnp.einsum(
        "rkgim,rkmd->rkgid", tree_weights, fresh_values, preferred_element_type=jnp.float32
    )
    attended = (weighted_values / totals[..., None]).astype(jnp.bfloat16)
    attend_part = jnp.einsum(
        "rkgid,kgdn->rin",
        attended,
        out_weight.reshape(key_local, group_factor, head_dim, model_width),
        preferred_element_type=jnp.float32,
    ).reshape(token_rows, model_width)
    fresh_keys = fresh_keys.transpose(0, 2, 1, 3)
    fresh_values = fresh_values.transpose(0, 2, 1, 3)
    chunk_rows = token_rows // vocab_shards
    chunk_start = vocab_shard * chunk_rows
    residual_chunk = lax.dynamic_slice_in_dim(states, chunk_start, chunk_rows, 0) + scatter_rows(
        attend_part, "vocab", vocab_shards
    )
    hidden_chunk = (
        residual_chunk
        * lax.rsqrt(jnp.mean(residual_chunk * residual_chunk, axis=1, keepdims=True) + eps_norm)
        * hidden_gain.astype(jnp.float32)
    ).astype(jnp.bfloat16)
    hidden_in = gather_rows(hidden_chunk, "vocab", vocab_shards)
    down_part = feed_forward(hidden_in, gate_weight, up_weight, down_weight)
    feed_chunk = scatter_rows(down_part, "vocab", vocab_shards).astype(jnp.bfloat16)
    local_counts = lax.dynamic_slice_in_dim(
        live_draft_count, request_shard * local_requests, local_requests
    )
    chunk_token = chunk_start + jnp.arange(chunk_rows, dtype=jnp.int32)
    chunk_count = jnp.take(local_counts, chunk_token // draft_length)
    chunk_live = (chunk_token % draft_length) < chunk_count
    layer_chunk = jnp.where(
        chunk_live[:, None], residual_chunk + feed_chunk.astype(jnp.float32), 0.0
    ).astype(jnp.bfloat16)
    share_width = model_width // vocab_shards
    path_length = path_index.shape[1]
    per_shard = path_length // vocab_shards
    path_count = local_requests * per_shard
    path_rows_all = (
        (
            path_index.reshape(local_requests, vocab_shards, per_shard)
            + (jnp.arange(local_requests, dtype=jnp.int32) * draft_length)[:, None, None]
        )
        .transpose(1, 0, 2)
        .reshape(vocab_shards, path_count)
    )
    column_pieces = (
        layer_chunk.reshape(chunk_rows, vocab_shards, share_width)
        .transpose(1, 0, 2)
        .reshape(vocab_shards, chunk_rows * share_width)
    )
    in_chunk = (
        path_rows_all[:, :, None] == chunk_token[None, None, :]
    ).astype(jnp.bfloat16)
    path_pieces = (
        jnp.einsum("vjt,tf->vjf", in_chunk, layer_chunk, preferred_element_type=jnp.float32)
        .astype(jnp.bfloat16)
        .reshape(vocab_shards, path_count * model_width)
    )
    arrived = lax.all_to_all(
        jnp.concatenate([column_pieces, path_pieces], axis=1),
        "vocab",
        split_axis=0,
        concat_axis=0,
        tiled=True,
    )
    layer_part = arrived[:, : chunk_rows * share_width].reshape(token_rows, share_width)
    head_rows = (
        jnp.sum(arrived[:, chunk_rows * share_width :].astype(jnp.float32), axis=0)
        .reshape(path_count, model_width)
        .astype(jnp.bfloat16)
    )
    request_picker = (
        path_index[:, :, None] == jnp.arange(draft_length, dtype=jnp.int32)[None, None, :]
    ).astype(jnp.bfloat16)
    accepted_keys = jnp.einsum(
        "ytm,ymu->ytu",
        request_picker,
        fresh_keys.reshape(local_requests, draft_length, key_local * head_dim),
        preferred_element_type=jnp.float32,
    ).astype(jnp.bfloat16)
    accepted_values = jnp.einsum(
        "ytm,ymu->ytu",
        request_picker,
        fresh_values.reshape(local_requests, draft_length, key_local * head_dim),
        preferred_element_type=jnp.float32,
    ).astype(jnp.bfloat16)
    flat_rows = head_rows.astype(jnp.float32)
    mean_square = jnp.mean(flat_rows * flat_rows, axis=1)
    norm_values = jnp.sqrt(mean_square + eps_norm).reshape(local_requests, per_shard)
    head_in = (
        flat_rows * lax.rsqrt(mean_square + eps_norm)[:, None] * final_gain.astype(jnp.float32)
    ).astype(jnp.bfloat16)
    local_max = jnp.max(
        jnp.dot(
            gather_rows(head_in, "req", request_shards),
            head_weight,
            preferred_element_type=jnp.float32,
        ),
        axis=1,
    )
    every_max = gather_rows(local_max[None], "req", request_shards)
    maxima = jnp.max(every_max, axis=0).reshape(request_shards * local_requests, per_shard)
    return (
        layer_part.reshape(local_requests, draft_length, share_width),
        accepted_keys,
        accepted_values,
        norm_values,
        maxima,
    )


def solution(mesh):
    in_specs = (
        P("req", None, None),
        P("req", None),
        P(),
        P("req", None),
        P("req"),
        P("req", "vocab"),
        P("req", "vocab"),
        P(),
        P(),
        P(),
        P(None, "vocab"),
        P(None, "vocab"),
        P(None, "vocab"),
        P("vocab", None),
        P(None, "vocab"),
        P(None, "vocab"),
        P("vocab", None),
        P(None, "req"),
    )
    out_specs = (
        P("req", None, "vocab"),
        P("req", None, "vocab"),
        P("req", None, "vocab"),
        P("req", "vocab"),
        P(None, "vocab"),
    )
    return jax.shard_map(
        per_device, mesh=mesh, in_specs=in_specs, out_specs=out_specs, check_vma=False
    )
```

```python
import jax
import jax.numpy as jnp
from jax import lax
from jax.experimental import pallas as pl
from jax.experimental.pallas import tpu as pltpu
from jax.sharding import PartitionSpec as P

HEAD_SIZE = 96


eps_norm = 1e-05
rope_base = 100000.0
masked_score = -1e30


def ancestors(parents):
    draft_length = parents.shape[-1]
    columns = jnp.arange(draft_length, dtype=jnp.int32)
    reached = jnp.eye(draft_length, dtype=jnp.float32) + (parents[..., :, None] == columns).astype(
        jnp.float32
    )
    for sweep_number in range((draft_length - 1).bit_length()):
        reached = jnp.minimum(
            jnp.einsum("bij,bjk->bik", reached, reached, precision=lax.Precision.HIGHEST), 1.0
        )
    return reached


def feed_forward_kernel(x_ref, gate_ref, up_ref, down_ref, out_ref, acc_ref):
    step = pl.program_id(0)

    @pl.when(step == 0)
    def _():
        acc_ref[...] = jnp.zeros_like(acc_ref)

    x = x_ref[...]
    gate_out = jnp.dot(x, gate_ref[...], preferred_element_type=jnp.float32)
    up_out = jnp.dot(x, up_ref[...], preferred_element_type=jnp.float32)
    hidden = (gate_out / (1.0 + jnp.exp(-gate_out)) * up_out).astype(jnp.bfloat16)
    acc_ref[...] += jnp.dot(hidden, down_ref[...], preferred_element_type=jnp.float32)

    @pl.when(step == pl.num_programs(0) - 1)
    def _():
        out_ref[...] = acc_ref[...].astype(out_ref.dtype)


def feed_forward(hidden_in, gate_weight, up_weight, down_weight, block=256):
    rows, width = hidden_in.shape
    units = gate_weight.shape[1]
    block = min(block, units)
    return pl.pallas_call(
        feed_forward_kernel,
        grid=(units // block,),
        in_specs=[
            pl.BlockSpec((rows, width), lambda j: (0, 0)),
            pl.BlockSpec((width, block), lambda j: (0, j)),
            pl.BlockSpec((width, block), lambda j: (0, j)),
            pl.BlockSpec((block, width), lambda j: (j, 0)),
        ],
        out_specs=pl.BlockSpec((rows, width), lambda j: (0, 0)),
        out_shape=jax.ShapeDtypeStruct((rows, width), jnp.bfloat16),
        scratch_shapes=[pltpu.VMEM((rows, width), jnp.float32)],
        compiler_params=pltpu.CompilerParams(dimension_semantics=("arbitrary",)),
        cost_estimate=pl.CostEstimate(
            flops=6 * rows * width * units,
            transcendentals=rows * units,
            bytes_accessed=2 * (3 * width * units + 2 * rows * width),
        ),
    )(hidden_in, gate_weight, up_weight, down_weight)


def residual_norm_kernel(chunk_ref, arrived_ref, states_ref, gain_ref, residual_ref, copies_ref):
    shards = arrived_ref.shape[0]
    summed = arrived_ref[0].astype(jnp.float32)
    for source in range(1, shards):
        summed = summed + arrived_ref[source].astype(jnp.float32)
    residual = states_ref[...].astype(jnp.float32) + summed
    mean_square = jnp.mean(residual * residual, axis=1, keepdims=True)
    hidden = (
        residual * lax.rsqrt(mean_square + eps_norm) * gain_ref[...].astype(jnp.float32)
    ).astype(copies_ref.dtype)
    residual_ref[...] = residual
    for target in range(shards):
        copies_ref[target] = hidden


def residual_norm(arrived, draft_rows, gain, chunk):
    shards, rows, width = arrived.shape
    return pl.pallas_call(
        residual_norm_kernel,
        grid_spec=pltpu.PrefetchScalarGridSpec(
            num_scalar_prefetch=1,
            grid=(1,),
            in_specs=[
                pl.BlockSpec((shards, rows, width), lambda i, c: (0, 0, 0)),
                pl.BlockSpec((rows, width), lambda i, c: (c[0], 0)),
                pl.BlockSpec((1, width), lambda i, c: (0, 0)),
            ],
            out_specs=[
                pl.BlockSpec((rows, width), lambda i, c: (0, 0)),
                pl.BlockSpec((shards, rows, width), lambda i, c: (0, 0, 0)),
            ],
        ),
        out_shape=[
            jax.ShapeDtypeStruct((rows, width), jnp.float32),
            jax.ShapeDtypeStruct((shards, rows, width), jnp.bfloat16),
        ],
        cost_estimate=pl.CostEstimate(
            flops=12 * shards * rows * width,
            transcendentals=rows,
            bytes_accessed=2 * (2 * shards + 1) * rows * width + 4 * rows * width,
        ),
    )(chunk.reshape(1).astype(jnp.int32), arrived, draft_rows, gain.reshape(1, width))


def scatter_rows(partial, axis_name, shards):
    rows = partial.shape[0] // shards
    pieces = partial.reshape(shards, rows, *partial.shape[1:]).astype(jnp.bfloat16)
    arrived = lax.all_to_all(pieces, axis_name, split_axis=0, concat_axis=0, tiled=True)
    return jnp.sum(arrived.astype(jnp.float32), axis=0)


def gather_rows(chunk, axis_name, shards):
    copies = jnp.broadcast_to(chunk[None], (shards, *chunk.shape))
    arrived = lax.all_to_all(copies, axis_name, split_axis=0, concat_axis=0, tiled=True)
    return arrived.reshape(shards * chunk.shape[0], *chunk.shape[1:])


def per_device(
    draft_states,
    parents,
    live_draft_count,
    path_index,
    cached_length_list,
    cached_key_rows,
    cached_value_rows,
    attend_gain,
    hidden_gain,
    final_gain,
    query_weight,
    key_matrix,
    value_matrix,
    out_weight,
    gate_weight,
    up_weight,
    down_weight,
    head_weight,
):
    local_requests, draft_length, model_width = draft_states.shape
    token_rows = local_requests * draft_length
    request_shards = lax.axis_size("req")
    request_shard = lax.axis_index("req")
    vocab_shards = lax.axis_size("vocab")
    vocab_shard = lax.axis_index("vocab")
    head_dim = HEAD_SIZE
    key_local = key_matrix.shape[1] // head_dim
    query_local = query_weight.shape[1] // head_dim
    group_factor = query_local // key_local
    pool_rows = cached_key_rows.shape[0]
    states = draft_states.reshape(token_rows, model_width).astype(jnp.float32)
    normalized_states = (
        states
        * lax.rsqrt(jnp.mean(states * states, axis=1, keepdims=True) + eps_norm)
        * attend_gain.astype(jnp.float32)
    ).astype(jnp.bfloat16)
    reached = ancestors(parents)
    token_positions = (
        cached_length_list[:, None] + (jnp.sum(reached, axis=2) - 1.0).astype(jnp.int32)
    ).reshape(token_rows)
    request_states = normalized_states.reshape(local_requests, draft_length, model_width)
    request_positions = token_positions.reshape(local_requests, draft_length)
    inverse = rope_base ** (-jnp.arange(head_dim // 2, dtype=jnp.float32) * 2.0 / head_dim)
    angles = request_positions.astype(jnp.float32)[:, :, None] * inverse
    cosine = jnp.cos(angles)
    sine_of = jnp.sin(angles)

    def rotate(values):
        half = head_dim // 2
        lift = (local_requests,) + (1,) * (values.ndim - 3) + (draft_length, half)
        cos_b = cosine.reshape(lift)
        sin_b = sine_of.reshape(lift)
        first_half = values[..., :half]
        second_half = values[..., half:]
        return jnp.concatenate(
            [first_half * cos_b - second_half * sin_b, second_half * cos_b + first_half * sin_b],
            axis=-1,
        )

    query_rows = rotate(
        jnp.einsum(
            "rim,mkgd->rkgid",
            request_states,
            query_weight.reshape(model_width, key_local, group_factor, head_dim),
            preferred_element_type=jnp.float32,
        )
    ).astype(jnp.bfloat16)
    fresh_keys = rotate(
        jnp.einsum(
            "rim,mkd->rkid",
            request_states,
            key_matrix.reshape(model_width, key_local, head_dim),
            preferred_element_type=jnp.float32,
        )
    ).astype(jnp.bfloat16)
    fresh_values = jnp.einsum(
        "rim,mkd->rkid",
        request_states,
        value_matrix.reshape(model_width, key_local, head_dim),
        preferred_element_type=jnp.float32,
    ).astype(jnp.bfloat16)
    score_scale = head_dim ** (-0.5)
    pool_keys = cached_key_rows.reshape(pool_rows, key_local, head_dim)
    pool_values = cached_value_rows.reshape(pool_rows, key_local, head_dim)
    earlier = (
        jnp.arange(local_requests, dtype=jnp.int32)[None, :]
        < jnp.arange(local_requests, dtype=jnp.int32)[:, None]
    )
    cache_start = jnp.sum(jnp.where(earlier, cached_length_list[None, :], 0), axis=1)
    cache_end = cache_start + cached_length_list
    slots = jnp.arange(pool_rows, dtype=jnp.int32)
    pool_allowed = (slots[None, :] >= cache_start[:, None]) & (slots[None, :] < cache_end[:, None])
    pool_allowed = pool_allowed[:, None, None, None, :]
    tree_allowed = (reached > 0.5)[:, None, None, :, :]
    pool_scores = (
        jnp.einsum("rkgid,pkd->rkgip", query_rows, pool_keys, preferred_element_type=jnp.float32)
        * score_scale
    )
    tree_scores = (
        jnp.einsum("rkgid,rkmd->rkgim", query_rows, fresh_keys, preferred_element_type=jnp.float32)
        * score_scale
    )
    top = jnp.maximum(
        jnp.max(jnp.where(pool_allowed, pool_scores, masked_score), axis=4),
        jnp.max(jnp.where(tree_allowed, tree_scores, masked_score), axis=4),
    )
    pool_weights = jnp.where(pool_allowed, jnp.exp(pool_scores - top[..., None]), 0.0).astype(
        jnp.bfloat16
    )
    tree_weights = jnp.where(tree_allowed, jnp.exp(tree_scores - top[..., None]), 0.0).astype(
        jnp.bfloat16
    )
    totals = jnp.sum(pool_weights.astype(jnp.float32), axis=4) + jnp.sum(
        tree_weights.astype(jnp.float32), axis=4
    )
    weighted_values = jnp.einsum(
        "rkgip,pkd->rkgid", pool_weights, pool_values, preferred_element_type=jnp.float32
    ) + jnp.einsum(
        "rkgim,rkmd->rkgid", tree_weights, fresh_values, preferred_element_type=jnp.float32
    )
    attended = (weighted_values / totals[..., None]).astype(jnp.bfloat16)
    attend_part = jnp.einsum(
        "rkgid,kgdn->rin",
        attended,
        out_weight.reshape(key_local, group_factor, head_dim, model_width),
        preferred_element_type=jnp.float32,
    ).reshape(token_rows, model_width)
    fresh_keys = fresh_keys.transpose(0, 2, 1, 3)
    fresh_values = fresh_values.transpose(0, 2, 1, 3)
    chunk_rows = token_rows // vocab_shards
    chunk_start = vocab_shard * chunk_rows
    attn_arrived = lax.all_to_all(
        attend_part.reshape(vocab_shards, chunk_rows, model_width).astype(jnp.bfloat16),
        "vocab",
        split_axis=0,
        concat_axis=0,
        tiled=True,
    )
    residual_chunk, hidden_copies = residual_norm(
        attn_arrived, draft_states.reshape(token_rows, model_width), hidden_gain, vocab_shard
    )
    hidden_in = lax.all_to_all(
        hidden_copies, "vocab", split_axis=0, concat_axis=0, tiled=True
    ).reshape(token_rows, model_width)
    down_part = feed_forward(hidden_in, gate_weight, up_weight, down_weight)
    feed_chunk = scatter_rows(down_part, "vocab", vocab_shards).astype(jnp.bfloat16)
    local_counts = lax.dynamic_slice_in_dim(
        live_draft_count, request_shard * local_requests, local_requests
    )
    chunk_token = chunk_start + jnp.arange(chunk_rows, dtype=jnp.int32)
    chunk_count = jnp.take(local_counts, chunk_token // draft_length)
    chunk_live = (chunk_token % draft_length) < chunk_count
    layer_chunk = jnp.where(
        chunk_live[:, None], residual_chunk + feed_chunk.astype(jnp.float32), 0.0
    ).astype(jnp.bfloat16)
    share_width = model_width // vocab_shards
    path_length = path_index.shape[1]
    per_shard = path_length // vocab_shards
    path_count = local_requests * per_shard
    path_rows_all = (
        (
            path_index.reshape(local_requests, vocab_shards, per_shard)
            + (jnp.arange(local_requests, dtype=jnp.int32) * draft_length)[:, None, None]
        )
        .transpose(1, 0, 2)
        .reshape(vocab_shards, path_count)
    )
    column_pieces = (
        layer_chunk.reshape(chunk_rows, vocab_shards, share_width)
        .transpose(1, 0, 2)
        .reshape(vocab_shards, chunk_rows * share_width)
    )
    in_chunk = (
        path_rows_all[:, :, None] == chunk_token[None, None, :]
    ).astype(jnp.bfloat16)
    path_pieces = (
        jnp.einsum("vjt,tf->vjf", in_chunk, layer_chunk, preferred_element_type=jnp.float32)
        .astype(jnp.bfloat16)
        .reshape(vocab_shards, path_count * model_width)
    )
    arrived = lax.all_to_all(
        jnp.concatenate([column_pieces, path_pieces], axis=1),
        "vocab",
        split_axis=0,
        concat_axis=0,
        tiled=True,
    )
    layer_part = arrived[:, : chunk_rows * share_width].reshape(token_rows, share_width)
    head_rows = (
        jnp.sum(arrived[:, chunk_rows * share_width :].astype(jnp.float32), axis=0)
        .reshape(path_count, model_width)
        .astype(jnp.bfloat16)
    )
    request_picker = (
        path_index[:, :, None] == jnp.arange(draft_length, dtype=jnp.int32)[None, None, :]
    ).astype(jnp.bfloat16)
    accepted_keys = jnp.einsum(
        "ytm,ymu->ytu",
        request_picker,
        fresh_keys.reshape(local_requests, draft_length, key_local * head_dim),
        preferred_element_type=jnp.float32,
    ).astype(jnp.bfloat16)
    accepted_values = jnp.einsum(
        "ytm,ymu->ytu",
        request_picker,
        fresh_values.reshape(local_requests, draft_length, key_local * head_dim),
        preferred_element_type=jnp.float32,
    ).astype(jnp.bfloat16)
    flat_rows = head_rows.astype(jnp.float32)
    mean_square = jnp.mean(flat_rows * flat_rows, axis=1)
    norm_values = jnp.sqrt(mean_square + eps_norm).reshape(local_requests, per_shard)
    head_in = (
        flat_rows * lax.rsqrt(mean_square + eps_norm)[:, None] * final_gain.astype(jnp.float32)
    ).astype(jnp.bfloat16)
    local_max = jnp.max(
        jnp.dot(
            gather_rows(head_in, "req", request_shards),
            head_weight,
            preferred_element_type=jnp.float32,
        ),
        axis=1,
    )
    every_max = gather_rows(local_max[None], "req", request_shards)
    maxima = jnp.max(every_max, axis=0).reshape(request_shards * local_requests, per_shard)
    return (
        layer_part.reshape(local_requests, draft_length, share_width),
        accepted_keys,
        accepted_values,
        norm_values,
        maxima,
    )


def solution(mesh):
    in_specs = (
        P("req", None, None),
        P("req", None),
        P(),
        P("req", None),
        P("req"),
        P("req", "vocab"),
        P("req", "vocab"),
        P(),
        P(),
        P(),
        P(None, "vocab"),
        P(None, "vocab"),
        P(None, "vocab"),
        P("vocab", None),
        P(None, "vocab"),
        P(None, "vocab"),
        P("vocab", None),
        P(None, "req"),
    )
    out_specs = (
        P("req", None, "vocab"),
        P("req", None, "vocab"),
        P("req", None, "vocab"),
        P("req", "vocab"),
        P(None, "vocab"),
    )
    return jax.shard_map(
        per_device, mesh=mesh, in_specs=in_specs, out_specs=out_specs, check_vma=False
    )
```

```python
import jax
import jax.numpy as jnp
from jax import lax
from jax.experimental import pallas as pl
from jax.experimental.pallas import tpu as pltpu
from jax.sharding import PartitionSpec as P

HEAD_SIZE = 96


eps_norm = 1e-05
rope_base = 100000.0
masked_score = -1e30


def ancestors(parents):
    draft_length = parents.shape[-1]
    columns = jnp.arange(draft_length, dtype=jnp.int32)
    reached = jnp.eye(draft_length, dtype=jnp.float32) + (parents[..., :, None] == columns).astype(
        jnp.float32
    )
    for sweep_number in range((draft_length - 1).bit_length()):
        reached = jnp.minimum(
            jnp.einsum("bij,bjk->bik", reached, reached, precision=lax.Precision.HIGHEST), 1.0
        )
    return reached


def feed_forward_kernel(x_ref, gate_ref, up_ref, down_ref, out_ref, acc_ref):
    step = pl.program_id(0)

    @pl.when(step == 0)
    def _():
        acc_ref[...] = jnp.zeros_like(acc_ref)

    x = x_ref[...]
    gate_out = jnp.dot(x, gate_ref[...], preferred_element_type=jnp.float32)
    up_out = jnp.dot(x, up_ref[...], preferred_element_type=jnp.float32)
    hidden = (gate_out / (1.0 + jnp.exp(-gate_out)) * up_out).astype(jnp.bfloat16)
    acc_ref[...] += jnp.dot(hidden, down_ref[...], preferred_element_type=jnp.float32)

    @pl.when(step == pl.num_programs(0) - 1)
    def _():
        out_ref[...] = acc_ref[...].astype(out_ref.dtype)


def feed_forward(hidden_in, gate_weight, up_weight, down_weight, block=256):
    rows, width = hidden_in.shape
    units = gate_weight.shape[1]
    block = min(block, units)
    return pl.pallas_call(
        feed_forward_kernel,
        grid=(units // block,),
        in_specs=[
            pl.BlockSpec((rows, width), lambda j: (0, 0)),
            pl.BlockSpec((width, block), lambda j: (0, j)),
            pl.BlockSpec((width, block), lambda j: (0, j)),
            pl.BlockSpec((block, width), lambda j: (j, 0)),
        ],
        out_specs=pl.BlockSpec((rows, width), lambda j: (0, 0)),
        out_shape=jax.ShapeDtypeStruct((rows, width), jnp.bfloat16),
        scratch_shapes=[pltpu.VMEM((rows, width), jnp.float32)],
        compiler_params=pltpu.CompilerParams(dimension_semantics=("arbitrary",)),
        cost_estimate=pl.CostEstimate(
            flops=6 * rows * width * units,
            transcendentals=rows * units,
            bytes_accessed=2 * (3 * width * units + 2 * rows * width),
        ),
    )(hidden_in, gate_weight, up_weight, down_weight)


def residual_norm_kernel(chunk_ref, arrived_ref, states_ref, gain_ref, residual_ref, copies_ref):
    shards = arrived_ref.shape[0]
    summed = arrived_ref[0].astype(jnp.float32)
    for source in range(1, shards):
        summed = summed + arrived_ref[source].astype(jnp.float32)
    residual = states_ref[...].astype(jnp.float32) + summed
    mean_square = jnp.mean(residual * residual, axis=1, keepdims=True)
    hidden = (
        residual * lax.rsqrt(mean_square + eps_norm) * gain_ref[...].astype(jnp.float32)
    ).astype(copies_ref.dtype)
    residual_ref[...] = residual
    for target in range(shards):
        copies_ref[target] = hidden


def residual_norm(arrived, draft_rows, gain, chunk):
    shards, rows, width = arrived.shape
    return pl.pallas_call(
        residual_norm_kernel,
        grid_spec=pltpu.PrefetchScalarGridSpec(
            num_scalar_prefetch=1,
            grid=(1,),
            in_specs=[
                pl.BlockSpec((shards, rows, width), lambda i, c: (0, 0, 0)),
                pl.BlockSpec((rows, width), lambda i, c: (c[0], 0)),
                pl.BlockSpec((1, width), lambda i, c: (0, 0)),
            ],
            out_specs=[
                pl.BlockSpec((rows, width), lambda i, c: (0, 0)),
                pl.BlockSpec((shards, rows, width), lambda i, c: (0, 0, 0)),
            ],
        ),
        out_shape=[
            jax.ShapeDtypeStruct((rows, width), jnp.float32),
            jax.ShapeDtypeStruct((shards, rows, width), jnp.bfloat16),
        ],
        cost_estimate=pl.CostEstimate(
            flops=12 * shards * rows * width,
            transcendentals=rows,
            bytes_accessed=4 * shards * rows * width + 8 * rows * width,
        ),
    )(chunk.reshape(1).astype(jnp.int32), arrived, draft_rows, gain.reshape(1, width))


def scatter_rows(partial, axis_name, shards):
    rows = partial.shape[0] // shards
    pieces = partial.reshape(shards, rows, *partial.shape[1:]).astype(jnp.bfloat16)
    arrived = lax.all_to_all(pieces, axis_name, split_axis=0, concat_axis=0, tiled=True)
    return jnp.sum(arrived.astype(jnp.float32), axis=0)


def gather_rows(chunk, axis_name, shards):
    copies = jnp.broadcast_to(chunk[None], (shards, *chunk.shape))
    arrived = lax.all_to_all(copies, axis_name, split_axis=0, concat_axis=0, tiled=True)
    return arrived.reshape(shards * chunk.shape[0], *chunk.shape[1:])


def per_device(
    draft_states,
    parents,
    live_draft_count,
    path_index,
    cached_length_list,
    cached_key_rows,
    cached_value_rows,
    attend_gain,
    hidden_gain,
    final_gain,
    query_weight,
    key_matrix,
    value_matrix,
    out_weight,
    gate_weight,
    up_weight,
    down_weight,
    head_weight,
):
    local_requests, draft_length, model_width = draft_states.shape
    token_rows = local_requests * draft_length
    request_shards = lax.axis_size("req")
    request_shard = lax.axis_index("req")
    vocab_shards = lax.axis_size("vocab")
    vocab_shard = lax.axis_index("vocab")
    head_dim = HEAD_SIZE
    key_local = key_matrix.shape[1] // head_dim
    query_local = query_weight.shape[1] // head_dim
    group_factor = query_local // key_local
    pool_rows = cached_key_rows.shape[0]
    states = draft_states.reshape(token_rows, model_width).astype(jnp.float32)
    normalized_states = (
        states
        * lax.rsqrt(jnp.mean(states * states, axis=1, keepdims=True) + eps_norm)
        * attend_gain.astype(jnp.float32)
    ).astype(jnp.bfloat16)
    reached = ancestors(parents)
    token_positions = (
        cached_length_list[:, None] + (jnp.sum(reached, axis=2) - 1.0).astype(jnp.int32)
    ).reshape(token_rows)
    request_states = normalized_states.reshape(local_requests, draft_length, model_width)
    request_positions = token_positions.reshape(local_requests, draft_length)
    inverse = rope_base ** (-jnp.arange(head_dim // 2, dtype=jnp.float32) * 2.0 / head_dim)
    angles = request_positions.astype(jnp.float32)[:, :, None] * inverse
    cosine = jnp.cos(angles)
    sine_of = jnp.sin(angles)

    def rotate(values):
        half = head_dim // 2
        lift = (local_requests,) + (1,) * (values.ndim - 3) + (draft_length, half)
        cos_b = cosine.reshape(lift)
        sin_b = sine_of.reshape(lift)
        first_half = values[..., :half]
        second_half = values[..., half:]
        return jnp.concatenate(
            [first_half * cos_b - second_half * sin_b, second_half * cos_b + first_half * sin_b],
            axis=-1,
        )

    query_rows = rotate(
        jnp.einsum(
            "rim,mkgd->rkgid",
            request_states,
            query_weight.reshape(model_width, key_local, group_factor, head_dim),
            preferred_element_type=jnp.float32,
        )
    ).astype(jnp.bfloat16)
    fresh_keys = rotate(
        jnp.einsum(
            "rim,mkd->rkid",
            request_states,
            key_matrix.reshape(model_width, key_local, head_dim),
            preferred_element_type=jnp.float32,
        )
    ).astype(jnp.bfloat16)
    fresh_values = jnp.einsum(
        "rim,mkd->rkid",
        request_states,
        value_matrix.reshape(model_width, key_local, head_dim),
        preferred_element_type=jnp.float32,
    ).astype(jnp.bfloat16)
    score_scale = head_dim ** (-0.5)
    pool_keys = cached_key_rows.reshape(pool_rows, key_local, head_dim)
    pool_values = cached_value_rows.reshape(pool_rows, key_local, head_dim)
    earlier = (
        jnp.arange(local_requests, dtype=jnp.int32)[None, :]
        < jnp.arange(local_requests, dtype=jnp.int32)[:, None]
    )
    cache_start = jnp.sum(jnp.where(earlier, cached_length_list[None, :], 0), axis=1)
    cache_end = cache_start + cached_length_list
    slots = jnp.arange(pool_rows, dtype=jnp.int32)
    pool_allowed = (slots[None, :] >= cache_start[:, None]) & (slots[None, :] < cache_end[:, None])
    pool_allowed = pool_allowed[:, None, None, None, :]
    tree_allowed = (reached > 0.5)[:, None, None, :, :]
    pool_scores = (
        jnp.einsum("rkgid,pkd->rkgip", query_rows, pool_keys, preferred_element_type=jnp.float32)
        * score_scale
    )
    tree_scores = (
        jnp.einsum("rkgid,rkmd->rkgim", query_rows, fresh_keys, preferred_element_type=jnp.float32)
        * score_scale
    )
    top = jnp.maximum(
        jnp.max(jnp.where(pool_allowed, pool_scores, masked_score), axis=4),
        jnp.max(jnp.where(tree_allowed, tree_scores, masked_score), axis=4),
    )
    pool_weights = jnp.where(pool_allowed, jnp.exp(pool_scores - top[..., None]), 0.0).astype(
        jnp.bfloat16
    )
    tree_weights = jnp.where(tree_allowed, jnp.exp(tree_scores - top[..., None]), 0.0).astype(
        jnp.bfloat16
    )
    totals = jnp.sum(pool_weights.astype(jnp.float32), axis=4) + jnp.sum(
        tree_weights.astype(jnp.float32), axis=4
    )
    weighted_values = jnp.einsum(
        "rkgip,pkd->rkgid", pool_weights, pool_values, preferred_element_type=jnp.float32
    ) + jnp.einsum(
        "rkgim,rkmd->rkgid", tree_weights, fresh_values, preferred_element_type=jnp.float32
    )
    attended = (weighted_values / totals[..., None]).astype(jnp.bfloat16)
    attend_part = jnp.einsum(
        "rkgid,kgdn->rin",
        attended,
        out_weight.reshape(key_local, group_factor, head_dim, model_width),
        preferred_element_type=jnp.float32,
    ).reshape(token_rows, model_width)
    fresh_keys = fresh_keys.transpose(0, 2, 1, 3)
    fresh_values = fresh_values.transpose(0, 2, 1, 3)
    chunk_rows = token_rows // vocab_shards
    chunk_start = vocab_shard * chunk_rows
    attn_arrived = lax.all_to_all(
        attend_part.reshape(vocab_shards, chunk_rows, model_width).astype(jnp.bfloat16),
        "vocab",
        split_axis=0,
        concat_axis=0,
        tiled=True,
    )
    residual_chunk, hidden_copies = residual_norm(
        attn_arrived, states, hidden_gain, vocab_shard
    )
    hidden_in = lax.all_to_all(
        hidden_copies, "vocab", split_axis=0, concat_axis=0, tiled=True
    ).reshape(token_rows, model_width)
    down_part = feed_forward(hidden_in, gate_weight, up_weight, down_weight)
    feed_chunk = scatter_rows(down_part, "vocab", vocab_shards).astype(jnp.bfloat16)
    local_counts = lax.dynamic_slice_in_dim(
        live_draft_count, request_shard * local_requests, local_requests
    )
    chunk_token = chunk_start + jnp.arange(chunk_rows, dtype=jnp.int32)
    chunk_count = jnp.take(local_counts, chunk_token // draft_length)
    chunk_live = (chunk_token % draft_length) < chunk_count
    layer_chunk = jnp.where(
        chunk_live[:, None], residual_chunk + feed_chunk.astype(jnp.float32), 0.0
    ).astype(jnp.bfloat16)
    share_width = model_width // vocab_shards
    path_length = path_index.shape[1]
    per_shard = path_length // vocab_shards
    path_count = local_requests * per_shard
    path_rows_all = (
        (
            path_index.reshape(local_requests, vocab_shards, per_shard)
            + (jnp.arange(local_requests, dtype=jnp.int32) * draft_length)[:, None, None]
        )
        .transpose(1, 0, 2)
        .reshape(vocab_shards, path_count)
    )
    column_pieces = (
        layer_chunk.reshape(chunk_rows, vocab_shards, share_width)
        .transpose(1, 0, 2)
        .reshape(vocab_shards, chunk_rows * share_width)
    )
    in_chunk = (
        path_rows_all[:, :, None] == chunk_token[None, None, :]
    ).astype(jnp.bfloat16)
    path_pieces = (
        jnp.einsum("vjt,tf->vjf", in_chunk, layer_chunk, preferred_element_type=jnp.float32)
        .astype(jnp.bfloat16)
        .reshape(vocab_shards, path_count * model_width)
    )
    arrived = lax.all_to_all(
        jnp.concatenate([column_pieces, path_pieces], axis=1),
        "vocab",
        split_axis=0,
        concat_axis=0,
        tiled=True,
    )
    layer_part = arrived[:, : chunk_rows * share_width].reshape(token_rows, share_width)
    head_rows = (
        jnp.sum(arrived[:, chunk_rows * share_width :].astype(jnp.float32), axis=0)
        .reshape(path_count, model_width)
        .astype(jnp.bfloat16)
    )
    request_picker = (
        path_index[:, :, None] == jnp.arange(draft_length, dtype=jnp.int32)[None, None, :]
    ).astype(jnp.bfloat16)
    accepted_keys = jnp.einsum(
        "ytm,ymu->ytu",
        request_picker,
        fresh_keys.reshape(local_requests, draft_length, key_local * head_dim),
        preferred_element_type=jnp.float32,
    ).astype(jnp.bfloat16)
    accepted_values = jnp.einsum(
        "ytm,ymu->ytu",
        request_picker,
        fresh_values.reshape(local_requests, draft_length, key_local * head_dim),
        preferred_element_type=jnp.float32,
    ).astype(jnp.bfloat16)
    flat_rows = head_rows.astype(jnp.float32)
    mean_square = jnp.mean(flat_rows * flat_rows, axis=1)
    norm_values = jnp.sqrt(mean_square + eps_norm).reshape(local_requests, per_shard)
    head_in = (
        flat_rows * lax.rsqrt(mean_square + eps_norm)[:, None] * final_gain.astype(jnp.float32)
    ).astype(jnp.bfloat16)
    local_max = jnp.max(
        jnp.dot(
            gather_rows(head_in, "req", request_shards),
            head_weight,
            preferred_element_type=jnp.float32,
        ),
        axis=1,
    )
    every_max = gather_rows(local_max[None], "req", request_shards)
    maxima = jnp.max(every_max, axis=0).reshape(request_shards * local_requests, per_shard)
    return (
        layer_part.reshape(local_requests, draft_length, share_width),
        accepted_keys,
        accepted_values,
        norm_values,
        maxima,
    )


def solution(mesh):
    in_specs = (
        P("req", None, None),
        P("req", None),
        P(),
        P("req", None),
        P("req"),
        P("req", "vocab"),
        P("req", "vocab"),
        P(),
        P(),
        P(),
        P(None, "vocab"),
        P(None, "vocab"),
        P(None, "vocab"),
        P("vocab", None),
        P(None, "vocab"),
        P(None, "vocab"),
        P("vocab", None),
        P(None, "req"),
    )
    out_specs = (
        P("req", None, "vocab"),
        P("req", None, "vocab"),
        P("req", None, "vocab"),
        P("req", "vocab"),
        P(None, "vocab"),
    )
    return jax.shard_map(
        per_device, mesh=mesh, in_specs=in_specs, out_specs=out_specs, check_vma=False
    )
```

```python
import jax
import jax.numpy as jnp
from jax import lax
from jax.experimental import pallas as pl
from jax.experimental.pallas import tpu as pltpu
from jax.sharding import PartitionSpec as P

HEAD_SIZE = 96


eps_norm = 1e-05
rope_base = 100000.0
masked_score = -1e30


def ancestors(parents):
    draft_length = parents.shape[-1]
    columns = jnp.arange(draft_length, dtype=jnp.int32)
    reached = jnp.eye(draft_length, dtype=jnp.float32) + (parents[..., :, None] == columns).astype(
        jnp.float32
    )
    for sweep_number in range((draft_length - 1).bit_length()):
        reached = jnp.minimum(
            jnp.einsum("bij,bjk->bik", reached, reached, precision=lax.Precision.HIGHEST), 1.0
        )
    return reached


def feed_forward_kernel(x_ref, gate_ref, up_ref, down_ref, out_ref, acc_ref):
    step = pl.program_id(0)

    @pl.when(step == 0)
    def _():
        acc_ref[...] = jnp.zeros_like(acc_ref)

    x = x_ref[...]
    gate_out = jnp.dot(x, gate_ref[...], preferred_element_type=jnp.float32)
    up_out = jnp.dot(x, up_ref[...], preferred_element_type=jnp.float32)
    hidden = (gate_out / (1.0 + jnp.exp(-gate_out)) * up_out).astype(jnp.bfloat16)
    acc_ref[...] += jnp.dot(hidden, down_ref[...], preferred_element_type=jnp.float32)

    @pl.when(step == pl.num_programs(0) - 1)
    def _():
        out_ref[...] = acc_ref[...].astype(out_ref.dtype)


def feed_forward(hidden_in, gate_weight, up_weight, down_weight, block=128):
    rows, width = hidden_in.shape
    units = gate_weight.shape[1]
    block = min(block, units)
    return pl.pallas_call(
        feed_forward_kernel,
        grid=(units // block,),
        in_specs=[
            pl.BlockSpec((rows, width), lambda j: (0, 0)),
            pl.BlockSpec((width, block), lambda j: (0, j)),
            pl.BlockSpec((width, block), lambda j: (0, j)),
            pl.BlockSpec((block, width), lambda j: (j, 0)),
        ],
        out_specs=pl.BlockSpec((rows, width), lambda j: (0, 0)),
        out_shape=jax.ShapeDtypeStruct((rows, width), jnp.bfloat16),
        scratch_shapes=[pltpu.VMEM((rows, width), jnp.float32)],
        compiler_params=pltpu.CompilerParams(dimension_semantics=("arbitrary",)),
        cost_estimate=pl.CostEstimate(
            flops=6 * rows * width * units,
            transcendentals=rows * units,
            bytes_accessed=2 * (3 * width * units + 2 * rows * width),
        ),
    )(hidden_in, gate_weight, up_weight, down_weight)


def scatter_rows(partial, axis_name, shards):
    rows = partial.shape[0] // shards
    pieces = partial.reshape(shards, rows, *partial.shape[1:]).astype(jnp.bfloat16)
    arrived = lax.all_to_all(pieces, axis_name, split_axis=0, concat_axis=0, tiled=True)
    return jnp.sum(arrived.astype(jnp.float32), axis=0)


def gather_rows(chunk, axis_name, shards):
    copies = jnp.broadcast_to(chunk[None], (shards, *chunk.shape))
    arrived = lax.all_to_all(copies, axis_name, split_axis=0, concat_axis=0, tiled=True)
    return arrived.reshape(shards * chunk.shape[0], *chunk.shape[1:])


def per_device(
    draft_states,
    parents,
    live_draft_count,
    path_index,
    cached_length_list,
    cached_key_rows,
    cached_value_rows,
    attend_gain,
    hidden_gain,
    final_gain,
    query_weight,
    key_matrix,
    value_matrix,
    out_weight,
    gate_weight,
    up_weight,
    down_weight,
    head_weight,
):
    local_requests, draft_length, model_width = draft_states.shape
    token_rows = local_requests * draft_length
    request_shards = lax.axis_size("req")
    request_shard = lax.axis_index("req")
    vocab_shards = lax.axis_size("vocab")
    vocab_shard = lax.axis_index("vocab")
    head_dim = HEAD_SIZE
    key_local = key_matrix.shape[1] // head_dim
    query_local = query_weight.shape[1] // head_dim
    group_factor = query_local // key_local
    pool_rows = cached_key_rows.shape[0]
    states = draft_states.reshape(token_rows, model_width).astype(jnp.float32)
    normalized_states = (
        states
        * lax.rsqrt(jnp.mean(states * states, axis=1, keepdims=True) + eps_norm)
        * attend_gain.astype(jnp.float32)
    ).astype(jnp.bfloat16)
    reached = ancestors(parents)
    token_positions = (
        cached_length_list[:, None] + (jnp.sum(reached, axis=2) - 1.0).astype(jnp.int32)
    ).reshape(token_rows)
    request_states = normalized_states.reshape(local_requests, draft_length, model_width)
    request_positions = token_positions.reshape(local_requests, draft_length)
    inverse = rope_base ** (-jnp.arange(head_dim // 2, dtype=jnp.float32) * 2.0 / head_dim)
    angles = request_positions.astype(jnp.float32)[:, :, None] * inverse
    cosine = jnp.cos(angles)
    sine_of = jnp.sin(angles)

    def rotate(values):
        half = head_dim // 2
        lift = (local_requests,) + (1,) * (values.ndim - 3) + (draft_length, half)
        cos_b = cosine.reshape(lift)
        sin_b = sine_of.reshape(lift)
        first_half = values[..., :half]
        second_half = values[..., half:]
        return jnp.concatenate(
            [first_half * cos_b - second_half * sin_b, second_half * cos_b + first_half * sin_b],
            axis=-1,
        )

    query_rows = rotate(
        jnp.einsum(
            "rim,mkgd->rkgid",
            request_states,
            query_weight.reshape(model_width, key_local, group_factor, head_dim),
            preferred_element_type=jnp.float32,
        )
    ).astype(jnp.bfloat16)
    fresh_keys = rotate(
        jnp.einsum(
            "rim,mkd->rkid",
            request_states,
            key_matrix.reshape(model_width, key_local, head_dim),
            preferred_element_type=jnp.float32,
        )
    ).astype(jnp.bfloat16)
    fresh_values = jnp.einsum(
        "rim,mkd->rkid",
        request_states,
        value_matrix.reshape(model_width, key_local, head_dim),
        preferred_element_type=jnp.float32,
    ).astype(jnp.bfloat16)
    score_scale = head_dim ** (-0.5)
    pool_keys = cached_key_rows.reshape(pool_rows, key_local, head_dim)
    pool_values = cached_value_rows.reshape(pool_rows, key_local, head_dim)
    earlier = (
        jnp.arange(local_requests, dtype=jnp.int32)[None, :]
        < jnp.arange(local_requests, dtype=jnp.int32)[:, None]
    )
    cache_start = jnp.sum(jnp.where(earlier, cached_length_list[None, :], 0), axis=1)
    cache_end = cache_start + cached_length_list
    slots = jnp.arange(pool_rows, dtype=jnp.int32)
    pool_allowed = (slots[None, :] >= cache_start[:, None]) & (slots[None, :] < cache_end[:, None])
    pool_allowed = pool_allowed[:, None, None, None, :]
    tree_allowed = (reached > 0.5)[:, None, None, :, :]
    pool_scores = (
        jnp.einsum("rkgid,pkd->rkgip", query_rows, pool_keys, preferred_element_type=jnp.float32)
        * score_scale
    )
    tree_scores = (
        jnp.einsum("rkgid,rkmd->rkgim", query_rows, fresh_keys, preferred_element_type=jnp.float32)
        * score_scale
    )
    top = jnp.maximum(
        jnp.max(jnp.where(pool_allowed, pool_scores, masked_score), axis=4),
        jnp.max(jnp.where(tree_allowed, tree_scores, masked_score), axis=4),
    )
    pool_weights = jnp.where(pool_allowed, jnp.exp(pool_scores - top[..., None]), 0.0).astype(
        jnp.bfloat16
    )
    tree_weights = jnp.where(tree_allowed, jnp.exp(tree_scores - top[..., None]), 0.0).astype(
        jnp.bfloat16
    )
    totals = jnp.sum(pool_weights.astype(jnp.float32), axis=4) + jnp.sum(
        tree_weights.astype(jnp.float32), axis=4
    )
    weighted_values = jnp.einsum(
        "rkgip,pkd->rkgid", pool_weights, pool_values, preferred_element_type=jnp.float32
    ) + jnp.einsum(
        "rkgim,rkmd->rkgid", tree_weights, fresh_values, preferred_element_type=jnp.float32
    )
    attended = (weighted_values / totals[..., None]).astype(jnp.bfloat16)
    attend_part = jnp.einsum(
        "rkgid,kgdn->rin",
        attended,
        out_weight.reshape(key_local, group_factor, head_dim, model_width),
        preferred_element_type=jnp.float32,
    ).reshape(token_rows, model_width)
    fresh_keys = fresh_keys.transpose(0, 2, 1, 3)
    fresh_values = fresh_values.transpose(0, 2, 1, 3)
    chunk_rows = token_rows // vocab_shards
    chunk_start = vocab_shard * chunk_rows
    residual_chunk = lax.dynamic_slice_in_dim(states, chunk_start, chunk_rows, 0) + scatter_rows(
        attend_part, "vocab", vocab_shards
    )
    hidden_chunk = (
        residual_chunk
        * lax.rsqrt(jnp.mean(residual_chunk * residual_chunk, axis=1, keepdims=True) + eps_norm)
        * hidden_gain.astype(jnp.float32)
    ).astype(jnp.bfloat16)
    hidden_in = gather_rows(hidden_chunk, "vocab", vocab_shards)
    down_part = feed_forward(hidden_in, gate_weight, up_weight, down_weight)
    feed_chunk = scatter_rows(down_part, "vocab", vocab_shards).astype(jnp.bfloat16)
    local_counts = lax.dynamic_slice_in_dim(
        live_draft_count, request_shard * local_requests, local_requests
    )
    chunk_token = chunk_start + jnp.arange(chunk_rows, dtype=jnp.int32)
    chunk_count = jnp.take(local_counts, chunk_token // draft_length)
    chunk_live = (chunk_token % draft_length) < chunk_count
    layer_chunk = jnp.where(
        chunk_live[:, None], residual_chunk + feed_chunk.astype(jnp.float32), 0.0
    ).astype(jnp.bfloat16)
    share_width = model_width // vocab_shards
    path_length = path_index.shape[1]
    per_shard = path_length // vocab_shards
    path_count = local_requests * per_shard
    path_rows_all = (
        (
            path_index.reshape(local_requests, vocab_shards, per_shard)
            + (jnp.arange(local_requests, dtype=jnp.int32) * draft_length)[:, None, None]
        )
        .transpose(1, 0, 2)
        .reshape(vocab_shards, path_count)
    )
    column_pieces = (
        layer_chunk.reshape(chunk_rows, vocab_shards, share_width)
        .transpose(1, 0, 2)
        .reshape(vocab_shards, chunk_rows * share_width)
    )
    in_chunk = (
        path_rows_all[:, :, None] == chunk_token[None, None, :]
    ).astype(jnp.bfloat16)
    path_pieces = (
        jnp.einsum("vjt,tf->vjf", in_chunk, layer_chunk, preferred_element_type=jnp.float32)
        .astype(jnp.bfloat16)
        .reshape(vocab_shards, path_count * model_width)
    )
    arrived = lax.all_to_all(
        jnp.concatenate([column_pieces, path_pieces], axis=1),
        "vocab",
        split_axis=0,
        concat_axis=0,
        tiled=True,
    )
    layer_part = arrived[:, : chunk_rows * share_width].reshape(token_rows, share_width)
    head_rows = (
        jnp.sum(arrived[:, chunk_rows * share_width :].astype(jnp.float32), axis=0)
        .reshape(path_count, model_width)
        .astype(jnp.bfloat16)
    )
    request_picker = (
        path_index[:, :, None] == jnp.arange(draft_length, dtype=jnp.int32)[None, None, :]
    ).astype(jnp.bfloat16)
    accepted_keys = jnp.einsum(
        "ytm,ymu->ytu",
        request_picker,
        fresh_keys.reshape(local_requests, draft_length, key_local * head_dim),
        preferred_element_type=jnp.float32,
    ).astype(jnp.bfloat16)
    accepted_values = jnp.einsum(
        "ytm,ymu->ytu",
        request_picker,
        fresh_values.reshape(local_requests, draft_length, key_local * head_dim),
        preferred_element_type=jnp.float32,
    ).astype(jnp.bfloat16)
    flat_rows = head_rows.astype(jnp.float32)
    mean_square = jnp.mean(flat_rows * flat_rows, axis=1)
    norm_values = jnp.sqrt(mean_square + eps_norm).reshape(local_requests, per_shard)
    head_in = (
        flat_rows * lax.rsqrt(mean_square + eps_norm)[:, None] * final_gain.astype(jnp.float32)
    ).astype(jnp.bfloat16)
    local_max = jnp.max(
        jnp.dot(
            gather_rows(head_in, "req", request_shards),
            head_weight,
            preferred_element_type=jnp.float32,
        ),
        axis=1,
    )
    every_max = gather_rows(local_max[None], "req", request_shards)
    maxima = jnp.max(every_max, axis=0).reshape(request_shards * local_requests, per_shard)
    return (
        layer_part.reshape(local_requests, draft_length, share_width),
        accepted_keys,
        accepted_values,
        norm_values,
        maxima,
    )


def solution(mesh):
    in_specs = (
        P("req", None, None),
        P("req", None),
        P(),
        P("req", None),
        P("req"),
        P("req", "vocab"),
        P("req", "vocab"),
        P(),
        P(),
        P(),
        P(None, "vocab"),
        P(None, "vocab"),
        P(None, "vocab"),
        P("vocab", None),
        P(None, "vocab"),
        P(None, "vocab"),
        P("vocab", None),
        P(None, "req"),
    )
    out_specs = (
        P("req", None, "vocab"),
        P("req", None, "vocab"),
        P("req", None, "vocab"),
        P("req", "vocab"),
        P(None, "vocab"),
    )
    return jax.shard_map(
        per_device, mesh=mesh, in_specs=in_specs, out_specs=out_specs, check_vma=False
    )
```

```python
import jax
import jax.numpy as jnp
from jax import lax
from jax.experimental import pallas as pl
from jax.experimental.pallas import tpu as pltpu
from jax.sharding import PartitionSpec as P

HEAD_SIZE = 96


eps_norm = 1e-05
rope_base = 100000.0
masked_score = -1e30


def ancestors(parents):
    draft_length = parents.shape[-1]
    columns = jnp.arange(draft_length, dtype=jnp.int32)
    reached = jnp.eye(draft_length, dtype=jnp.float32) + (parents[..., :, None] == columns).astype(
        jnp.float32
    )
    for sweep_number in range((draft_length - 1).bit_length()):
        reached = jnp.minimum(
            jnp.einsum("bij,bjk->bik", reached, reached, precision=lax.Precision.HIGHEST), 1.0
        )
    return reached


def feed_forward_kernel(x_ref, gate_ref, up_ref, down_ref, out_ref, acc_ref):
    step = pl.program_id(0)

    @pl.when(step == 0)
    def _():
        acc_ref[...] = jnp.zeros_like(acc_ref)

    x = x_ref[...]
    gate_out = jnp.dot(x, gate_ref[...], preferred_element_type=jnp.float32)
    up_out = jnp.dot(x, up_ref[...], preferred_element_type=jnp.float32)
    hidden = (gate_out / (1.0 + jnp.exp(-gate_out)) * up_out).astype(jnp.bfloat16)
    acc_ref[...] += jnp.dot(hidden, down_ref[...], preferred_element_type=jnp.float32)

    @pl.when(step == pl.num_programs(0) - 1)
    def _():
        out_ref[...] = acc_ref[...].astype(out_ref.dtype)


def feed_forward(hidden_in, gate_weight, up_weight, down_weight, block=512):
    rows, width = hidden_in.shape
    units = gate_weight.shape[1]
    block = min(block, units)
    return pl.pallas_call(
        feed_forward_kernel,
        grid=(units // block,),
        in_specs=[
            pl.BlockSpec((rows, width), lambda j: (0, 0)),
            pl.BlockSpec((width, block), lambda j: (0, j)),
            pl.BlockSpec((width, block), lambda j: (0, j)),
            pl.BlockSpec((block, width), lambda j: (j, 0)),
        ],
        out_specs=pl.BlockSpec((rows, width), lambda j: (0, 0)),
        out_shape=jax.ShapeDtypeStruct((rows, width), jnp.bfloat16),
        scratch_shapes=[pltpu.VMEM((rows, width), jnp.float32)],
        compiler_params=pltpu.CompilerParams(dimension_semantics=("arbitrary",)),
        cost_estimate=pl.CostEstimate(
            flops=6 * rows * width * units,
            transcendentals=rows * units,
            bytes_accessed=2 * (3 * width * units + 2 * rows * width),
        ),
    )(hidden_in, gate_weight, up_weight, down_weight)


def scatter_rows(partial, axis_name, shards):
    rows = partial.shape[0] // shards
    pieces = partial.reshape(shards, rows, *partial.shape[1:]).astype(jnp.bfloat16)
    arrived = lax.all_to_all(pieces, axis_name, split_axis=0, concat_axis=0, tiled=True)
    return jnp.sum(arrived.astype(jnp.float32), axis=0)


def gather_rows(chunk, axis_name, shards):
    copies = jnp.broadcast_to(chunk[None], (shards, *chunk.shape))
    arrived = lax.all_to_all(copies, axis_name, split_axis=0, concat_axis=0, tiled=True)
    return arrived.reshape(shards * chunk.shape[0], *chunk.shape[1:])


def per_device(
    draft_states,
    parents,
    live_draft_count,
    path_index,
    cached_length_list,
    cached_key_rows,
    cached_value_rows,
    attend_gain,
    hidden_gain,
    final_gain,
    query_weight,
    key_matrix,
    value_matrix,
    out_weight,
    gate_weight,
    up_weight,
    down_weight,
    head_weight,
):
    local_requests, draft_length, model_width = draft_states.shape
    token_rows = local_requests * draft_length
    request_shards = lax.axis_size("req")
    request_shard = lax.axis_index("req")
    vocab_shards = lax.axis_size("vocab")
    vocab_shard = lax.axis_index("vocab")
    head_dim = HEAD_SIZE
    key_local = key_matrix.shape[1] // head_dim
    query_local = query_weight.shape[1] // head_dim
    group_factor = query_local // key_local
    pool_rows = cached_key_rows.shape[0]
    states = draft_states.reshape(token_rows, model_width).astype(jnp.float32)
    normalized_states = (
        states
        * lax.rsqrt(jnp.mean(states * states, axis=1, keepdims=True) + eps_norm)
        * attend_gain.astype(jnp.float32)
    ).astype(jnp.bfloat16)
    reached = ancestors(parents)
    token_positions = (
        cached_length_list[:, None] + (jnp.sum(reached, axis=2) - 1.0).astype(jnp.int32)
    ).reshape(token_rows)
    request_states = normalized_states.reshape(local_requests, draft_length, model_width)
    request_positions = token_positions.reshape(local_requests, draft_length)
    inverse = rope_base ** (-jnp.arange(head_dim // 2, dtype=jnp.float32) * 2.0 / head_dim)
    angles = request_positions.astype(jnp.float32)[:, :, None] * inverse
    cosine = jnp.cos(angles)
    sine_of = jnp.sin(angles)

    def rotate(values):
        half = head_dim // 2
        lift = (local_requests,) + (1,) * (values.ndim - 3) + (draft_length, half)
        cos_b = cosine.reshape(lift)
        sin_b = sine_of.reshape(lift)
        first_half = values[..., :half]
        second_half = values[..., half:]
        return jnp.concatenate(
            [first_half * cos_b - second_half * sin_b, second_half * cos_b + first_half * sin_b],
            axis=-1,
        )

    query_rows = rotate(
        jnp.einsum(
            "rim,mkgd->rkgid",
            request_states,
            query_weight.reshape(model_width, key_local, group_factor, head_dim),
            preferred_element_type=jnp.float32,
        )
    ).astype(jnp.bfloat16)
    fresh_keys = rotate(
        jnp.einsum(
            "rim,mkd->rkid",
            request_states,
            key_matrix.reshape(model_width, key_local, head_dim),
            preferred_element_type=jnp.float32,
        )
    ).astype(jnp.bfloat16)
    fresh_values = jnp.einsum(
        "rim,mkd->rkid",
        request_states,
        value_matrix.reshape(model_width, key_local, head_dim),
        preferred_element_type=jnp.float32,
    ).astype(jnp.bfloat16)
    score_scale = head_dim ** (-0.5)
    pool_keys = cached_key_rows.reshape(pool_rows, key_local, head_dim)
    pool_values = cached_value_rows.reshape(pool_rows, key_local, head_dim)
    earlier = (
        jnp.arange(local_requests, dtype=jnp.int32)[None, :]
        < jnp.arange(local_requests, dtype=jnp.int32)[:, None]
    )
    cache_start = jnp.sum(jnp.where(earlier, cached_length_list[None, :], 0), axis=1)
    cache_end = cache_start + cached_length_list
    slots = jnp.arange(pool_rows, dtype=jnp.int32)
    pool_allowed = (slots[None, :] >= cache_start[:, None]) & (slots[None, :] < cache_end[:, None])
    pool_allowed = pool_allowed[:, None, None, None, :]
    tree_allowed = (reached > 0.5)[:, None, None, :, :]
    pool_scores = (
        jnp.einsum("rkgid,pkd->rkgip", query_rows, pool_keys, preferred_element_type=jnp.float32)
        * score_scale
    )
    tree_scores = (
        jnp.einsum("rkgid,rkmd->rkgim", query_rows, fresh_keys, preferred_element_type=jnp.float32)
        * score_scale
    )
    top = jnp.maximum(
        jnp.max(jnp.where(pool_allowed, pool_scores, masked_score), axis=4),
        jnp.max(jnp.where(tree_allowed, tree_scores, masked_score), axis=4),
    )
    pool_weights = jnp.where(pool_allowed, jnp.exp(pool_scores - top[..., None]), 0.0).astype(
        jnp.bfloat16
    )
    tree_weights = jnp.where(tree_allowed, jnp.exp(tree_scores - top[..., None]), 0.0).astype(
        jnp.bfloat16
    )
    totals = jnp.sum(pool_weights.astype(jnp.float32), axis=4) + jnp.sum(
        tree_weights.astype(jnp.float32), axis=4
    )
    weighted_values = jnp.einsum(
        "rkgip,pkd->rkgid", pool_weights, pool_values, preferred_element_type=jnp.float32
    ) + jnp.einsum(
        "rkgim,rkmd->rkgid", tree_weights, fresh_values, preferred_element_type=jnp.float32
    )
    attended = (weighted_values / totals[..., None]).astype(jnp.bfloat16)
    attend_part = jnp.einsum(
        "rkgid,kgdn->rin",
        attended,
        out_weight.reshape(key_local, group_factor, head_dim, model_width),
        preferred_element_type=jnp.float32,
    ).reshape(token_rows, model_width)
    fresh_keys = fresh_keys.transpose(0, 2, 1, 3)
    fresh_values = fresh_values.transpose(0, 2, 1, 3)
    chunk_rows = token_rows // vocab_shards
    chunk_start = vocab_shard * chunk_rows
    residual_chunk = lax.dynamic_slice_in_dim(states, chunk_start, chunk_rows, 0) + scatter_rows(
        attend_part, "vocab", vocab_shards
    )
    hidden_chunk = (
        residual_chunk
        * lax.rsqrt(jnp.mean(residual_chunk * residual_chunk, axis=1, keepdims=True) + eps_norm)
        * hidden_gain.astype(jnp.float32)
    ).astype(jnp.bfloat16)
    hidden_in = gather_rows(hidden_chunk, "vocab", vocab_shards)
    down_part = feed_forward(hidden_in, gate_weight, up_weight, down_weight)
    feed_chunk = scatter_rows(down_part, "vocab", vocab_shards).astype(jnp.bfloat16)
    local_counts = lax.dynamic_slice_in_dim(
        live_draft_count, request_shard * local_requests, local_requests
    )
    chunk_token = chunk_start + jnp.arange(chunk_rows, dtype=jnp.int32)
    chunk_count = jnp.take(local_counts, chunk_token // draft_length)
    chunk_live = (chunk_token % draft_length) < chunk_count
    layer_chunk = jnp.where(
        chunk_live[:, None], residual_chunk + feed_chunk.astype(jnp.float32), 0.0
    ).astype(jnp.bfloat16)
    share_width = model_width // vocab_shards
    path_length = path_index.shape[1]
    per_shard = path_length // vocab_shards
    path_count = local_requests * per_shard
    path_rows_all = (
        (
            path_index.reshape(local_requests, vocab_shards, per_shard)
            + (jnp.arange(local_requests, dtype=jnp.int32) * draft_length)[:, None, None]
        )
        .transpose(1, 0, 2)
        .reshape(vocab_shards, path_count)
    )
    column_pieces = (
        layer_chunk.reshape(chunk_rows, vocab_shards, share_width)
        .transpose(1, 0, 2)
        .reshape(vocab_shards, chunk_rows * share_width)
    )
    in_chunk = (
        path_rows_all[:, :, None] == chunk_token[None, None, :]
    ).astype(jnp.bfloat16)
    path_pieces = (
        jnp.einsum("vjt,tf->vjf", in_chunk, layer_chunk, preferred_element_type=jnp.float32)
        .astype(jnp.bfloat16)
        .reshape(vocab_shards, path_count * model_width)
    )
    arrived = lax.all_to_all(
        jnp.concatenate([column_pieces, path_pieces], axis=1),
        "vocab",
        split_axis=0,
        concat_axis=0,
        tiled=True,
    )
    layer_part = arrived[:, : chunk_rows * share_width].reshape(token_rows, share_width)
    head_rows = (
        jnp.sum(arrived[:, chunk_rows * share_width :].astype(jnp.float32), axis=0)
        .reshape(path_count, model_width)
        .astype(jnp.bfloat16)
    )
    request_picker = (
        path_index[:, :, None] == jnp.arange(draft_length, dtype=jnp.int32)[None, None, :]
    ).astype(jnp.bfloat16)
    accepted_keys = jnp.einsum(
        "ytm,ymu->ytu",
        request_picker,
        fresh_keys.reshape(local_requests, draft_length, key_local * head_dim),
        preferred_element_type=jnp.float32,
    ).astype(jnp.bfloat16)
    accepted_values = jnp.einsum(
        "ytm,ymu->ytu",
        request_picker,
        fresh_values.reshape(local_requests, draft_length, key_local * head_dim),
        preferred_element_type=jnp.float32,
    ).astype(jnp.bfloat16)
    flat_rows = head_rows.astype(jnp.float32)
    mean_square = jnp.mean(flat_rows * flat_rows, axis=1)
    norm_values = jnp.sqrt(mean_square + eps_norm).reshape(local_requests, per_shard)
    head_in = (
        flat_rows * lax.rsqrt(mean_square + eps_norm)[:, None] * final_gain.astype(jnp.float32)
    ).astype(jnp.bfloat16)
    local_max = jnp.max(
        jnp.dot(
            gather_rows(head_in, "req", request_shards),
            head_weight,
            preferred_element_type=jnp.float32,
        ),
        axis=1,
    )
    every_max = gather_rows(local_max[None], "req", request_shards)
    maxima = jnp.max(every_max, axis=0).reshape(request_shards * local_requests, per_shard)
    return (
        layer_part.reshape(local_requests, draft_length, share_width),
        accepted_keys,
        accepted_values,
        norm_values,
        maxima,
    )


def solution(mesh):
    in_specs = (
        P("req", None, None),
        P("req", None),
        P(),
        P("req", None),
        P("req"),
        P("req", "vocab"),
        P("req", "vocab"),
        P(),
        P(),
        P(),
        P(None, "vocab"),
        P(None, "vocab"),
        P(None, "vocab"),
        P("vocab", None),
        P(None, "vocab"),
        P(None, "vocab"),
        P("vocab", None),
        P(None, "req"),
    )
    out_specs = (
        P("req", None, "vocab"),
        P("req", None, "vocab"),
        P("req", None, "vocab"),
        P("req", "vocab"),
        P(None, "vocab"),
    )
    return jax.shard_map(
        per_device, mesh=mesh, in_specs=in_specs, out_specs=out_specs, check_vma=False
    )
```

```python
import functools

import jax
import jax.numpy as jnp
from jax import lax
from jax.experimental import pallas as pl
from jax.experimental.pallas import tpu as pltpu
from jax.sharding import PartitionSpec as P

HEAD_SIZE = 96


eps_norm = 1e-05
rope_base = 100000.0
masked_score = -1e30


def ancestors(parents):
    draft_length = parents.shape[-1]
    columns = jnp.arange(draft_length, dtype=jnp.int32)
    reached = jnp.eye(draft_length, dtype=jnp.float32) + (parents[..., :, None] == columns).astype(
        jnp.float32
    )
    for sweep_number in range((draft_length - 1).bit_length()):
        reached = jnp.minimum(
            jnp.einsum("bij,bjk->bik", reached, reached, precision=lax.Precision.HIGHEST), 1.0
        )
    return reached


def feed_forward_kernel(x_ref, gate_ref, up_ref, down_ref, out_ref, acc_ref):
    step = pl.program_id(0)

    @pl.when(step == 0)
    def _():
        acc_ref[...] = jnp.zeros_like(acc_ref)

    x = x_ref[...]
    gate_out = jnp.dot(x, gate_ref[...], preferred_element_type=jnp.float32)
    up_out = jnp.dot(x, up_ref[...], preferred_element_type=jnp.float32)
    hidden = (gate_out / (1.0 + jnp.exp(-gate_out)) * up_out).astype(jnp.bfloat16)
    acc_ref[...] += jnp.dot(hidden, down_ref[...], preferred_element_type=jnp.float32)

    @pl.when(step == pl.num_programs(0) - 1)
    def _():
        out_ref[...] = acc_ref[...].astype(out_ref.dtype)


def feed_forward(hidden_in, gate_weight, up_weight, down_weight, block=512):
    rows, width = hidden_in.shape
    units = gate_weight.shape[1]
    block = min(block, units)
    return pl.pallas_call(
        feed_forward_kernel,
        grid=(units // block,),
        in_specs=[
            pl.BlockSpec((rows, width), lambda j: (0, 0)),
            pl.BlockSpec((width, block), lambda j: (0, j)),
            pl.BlockSpec((width, block), lambda j: (0, j)),
            pl.BlockSpec((block, width), lambda j: (j, 0)),
        ],
        out_specs=pl.BlockSpec((rows, width), lambda j: (0, 0)),
        out_shape=jax.ShapeDtypeStruct((rows, width), jnp.bfloat16),
        scratch_shapes=[pltpu.VMEM((rows, width), jnp.float32)],
        compiler_params=pltpu.CompilerParams(dimension_semantics=("arbitrary",)),
        cost_estimate=pl.CostEstimate(
            flops=6 * rows * width * units,
            transcendentals=rows * units,
            bytes_accessed=2 * (3 * width * units + 2 * rows * width),
        ),
    )(hidden_in, gate_weight, up_weight, down_weight)


def head_prepare_kernel(head_offset, arrived_ref, gain_ref, copies_ref, norm_ref):
    width = copies_ref.shape[2]
    rows = []
    for row in range(norm_ref.shape[0]):
        start = head_offset + row * width
        piece = arrived_ref[:, start : start + width].astype(jnp.float32)
        rows.append(jnp.sum(piece, axis=0, keepdims=True).astype(jnp.bfloat16).astype(jnp.float32))
    path_rows = jnp.concatenate(rows, axis=0)
    mean_square = jnp.mean(path_rows * path_rows, axis=1, keepdims=True)
    norm_ref[...] = jnp.sqrt(mean_square + eps_norm)
    head_in = (
        path_rows * lax.rsqrt(mean_square + eps_norm) * gain_ref[...].astype(jnp.float32)
    ).astype(copies_ref.dtype)
    for target in range(copies_ref.shape[0]):
        copies_ref[target] = head_in


def head_prepare(arrived, gain, head_offset, path_count, targets):
    width = gain.shape[0]
    return pl.pallas_call(
        functools.partial(head_prepare_kernel, head_offset),
        out_shape=[
            jax.ShapeDtypeStruct((targets, path_count, width), jnp.bfloat16),
            jax.ShapeDtypeStruct((path_count, 1), jnp.float32),
        ],
        cost_estimate=pl.CostEstimate(
            flops=6 * arrived.size,
            transcendentals=2 * path_count,
            bytes_accessed=2 * arrived.size + 2 * targets * path_count * width,
        ),
    )(arrived, gain.reshape(1, width))

def scatter_rows(partial, axis_name, shards):
    rows = partial.shape[0] // shards
    pieces = partial.reshape(shards, rows, *partial.shape[1:]).astype(jnp.bfloat16)
    arrived = lax.all_to_all(pieces, axis_name, split_axis=0, concat_axis=0, tiled=True)
    return jnp.sum(arrived.astype(jnp.float32), axis=0)


def gather_rows(chunk, axis_name, shards):
    copies = jnp.broadcast_to(chunk[None], (shards, *chunk.shape))
    arrived = lax.all_to_all(copies, axis_name, split_axis=0, concat_axis=0, tiled=True)
    return arrived.reshape(shards * chunk.shape[0], *chunk.shape[1:])


def per_device(
    draft_states,
    parents,
    live_draft_count,
    path_index,
    cached_length_list,
    cached_key_rows,
    cached_value_rows,
    attend_gain,
    hidden_gain,
    final_gain,
    query_weight,
    key_matrix,
    value_matrix,
    out_weight,
    gate_weight,
    up_weight,
    down_weight,
    head_weight,
):
    local_requests, draft_length, model_width = draft_states.shape
    token_rows = local_requests * draft_length
    request_shards = lax.axis_size("req")
    request_shard = lax.axis_index("req")
    vocab_shards = lax.axis_size("vocab")
    vocab_shard = lax.axis_index("vocab")
    head_dim = HEAD_SIZE
    key_local = key_matrix.shape[1] // head_dim
    query_local = query_weight.shape[1] // head_dim
    group_factor = query_local // key_local
    pool_rows = cached_key_rows.shape[0]
    states = draft_states.reshape(token_rows, model_width).astype(jnp.float32)
    normalized_states = (
        states
        * lax.rsqrt(jnp.mean(states * states, axis=1, keepdims=True) + eps_norm)
        * attend_gain.astype(jnp.float32)
    ).astype(jnp.bfloat16)
    reached = ancestors(parents)
    token_positions = (
        cached_length_list[:, None] + (jnp.sum(reached, axis=2) - 1.0).astype(jnp.int32)
    ).reshape(token_rows)
    request_states = normalized_states.reshape(local_requests, draft_length, model_width)
    request_positions = token_positions.reshape(local_requests, draft_length)
    inverse = rope_base ** (-jnp.arange(head_dim // 2, dtype=jnp.float32) * 2.0 / head_dim)
    angles = request_positions.astype(jnp.float32)[:, :, None] * inverse
    cosine = jnp.cos(angles)
    sine_of = jnp.sin(angles)

    def rotate(values):
        half = head_dim // 2
        lift = (local_requests,) + (1,) * (values.ndim - 3) + (draft_length, half)
        cos_b = cosine.reshape(lift)
        sin_b = sine_of.reshape(lift)
        first_half = values[..., :half]
        second_half = values[..., half:]
        return jnp.concatenate(
            [first_half * cos_b - second_half * sin_b, second_half * cos_b + first_half * sin_b],
            axis=-1,
        )

    query_rows = rotate(
        jnp.einsum(
            "rim,mkgd->rkgid",
            request_states,
            query_weight.reshape(model_width, key_local, group_factor, head_dim),
            preferred_element_type=jnp.float32,
        )
    ).astype(jnp.bfloat16)
    fresh_keys = rotate(
        jnp.einsum(
            "rim,mkd->rkid",
            request_states,
            key_matrix.reshape(model_width, key_local, head_dim),
            preferred_element_type=jnp.float32,
        )
    ).astype(jnp.bfloat16)
    fresh_values = jnp.einsum(
        "rim,mkd->rkid",
        request_states,
        value_matrix.reshape(model_width, key_local, head_dim),
        preferred_element_type=jnp.float32,
    ).astype(jnp.bfloat16)
    score_scale = head_dim ** (-0.5)
    pool_keys = cached_key_rows.reshape(pool_rows, key_local, head_dim)
    pool_values = cached_value_rows.reshape(pool_rows, key_local, head_dim)
    earlier = (
        jnp.arange(local_requests, dtype=jnp.int32)[None, :]
        < jnp.arange(local_requests, dtype=jnp.int32)[:, None]
    )
    cache_start = jnp.sum(jnp.where(earlier, cached_length_list[None, :], 0), axis=1)
    cache_end = cache_start + cached_length_list
    slots = jnp.arange(pool_rows, dtype=jnp.int32)
    pool_allowed = (slots[None, :] >= cache_start[:, None]) & (slots[None, :] < cache_end[:, None])
    pool_allowed = pool_allowed[:, None, None, None, :]
    tree_allowed = (reached > 0.5)[:, None, None, :, :]
    pool_scores = (
        jnp.einsum("rkgid,pkd->rkgip", query_rows, pool_keys, preferred_element_type=jnp.float32)
        * score_scale
    )
    tree_scores = (
        jnp.einsum("rkgid,rkmd->rkgim", query_rows, fresh_keys, preferred_element_type=jnp.float32)
        * score_scale
    )
    top = jnp.maximum(
        jnp.max(jnp.where(pool_allowed, pool_scores, masked_score), axis=4),
        jnp.max(jnp.where(tree_allowed, tree_scores, masked_score), axis=4),
    )
    pool_weights = jnp.where(pool_allowed, jnp.exp(pool_scores - top[..., None]), 0.0).astype(
        jnp.bfloat16
    )
    tree_weights = jnp.where(tree_allowed, jnp.exp(tree_scores - top[..., None]), 0.0).astype(
        jnp.bfloat16
    )
    totals = jnp.sum(pool_weights.astype(jnp.float32), axis=4) + jnp.sum(
        tree_weights.astype(jnp.float32), axis=4
    )
    weighted_values = jnp.einsum(
        "rkgip,pkd->rkgid", pool_weights, pool_values, preferred_element_type=jnp.float32
    ) + jnp.einsum(
        "rkgim,rkmd->rkgid", tree_weights, fresh_values, preferred_element_type=jnp.float32
    )
    attended = (weighted_values / totals[..., None]).astype(jnp.bfloat16)
    attend_part = jnp.einsum(
        "rkgid,kgdn->rin",
        attended,
        out_weight.reshape(key_local, group_factor, head_dim, model_width),
        preferred_element_type=jnp.float32,
    ).reshape(token_rows, model_width)
    fresh_keys = fresh_keys.transpose(0, 2, 1, 3)
    fresh_values = fresh_values.transpose(0, 2, 1, 3)
    chunk_rows = token_rows // vocab_shards
    chunk_start = vocab_shard * chunk_rows
    residual_chunk = lax.dynamic_slice_in_dim(states, chunk_start, chunk_rows, 0) + scatter_rows(
        attend_part, "vocab", vocab_shards
    )
    hidden_chunk = (
        residual_chunk
        * lax.rsqrt(jnp.mean(residual_chunk * residual_chunk, axis=1, keepdims=True) + eps_norm)
        * hidden_gain.astype(jnp.float32)
    ).astype(jnp.bfloat16)
    hidden_in = gather_rows(hidden_chunk, "vocab", vocab_shards)
    down_part = feed_forward(hidden_in, gate_weight, up_weight, down_weight)
    feed_chunk = scatter_rows(down_part, "vocab", vocab_shards).astype(jnp.bfloat16)
    local_counts = lax.dynamic_slice_in_dim(
        live_draft_count, request_shard * local_requests, local_requests
    )
    chunk_token = chunk_start + jnp.arange(chunk_rows, dtype=jnp.int32)
    chunk_count = jnp.take(local_counts, chunk_token // draft_length)
    chunk_live = (chunk_token % draft_length) < chunk_count
    layer_chunk = jnp.where(
        chunk_live[:, None], residual_chunk + feed_chunk.astype(jnp.float32), 0.0
    ).astype(jnp.bfloat16)
    share_width = model_width // vocab_shards
    path_length = path_index.shape[1]
    per_shard = path_length // vocab_shards
    path_count = local_requests * per_shard
    path_rows_all = (
        (
            path_index.reshape(local_requests, vocab_shards, per_shard)
            + (jnp.arange(local_requests, dtype=jnp.int32) * draft_length)[:, None, None]
        )
        .transpose(1, 0, 2)
        .reshape(vocab_shards, path_count)
    )
    column_pieces = (
        layer_chunk.reshape(chunk_rows, vocab_shards, share_width)
        .transpose(1, 0, 2)
        .reshape(vocab_shards, chunk_rows * share_width)
    )
    in_chunk = (
        path_rows_all[:, :, None] == chunk_token[None, None, :]
    ).astype(jnp.bfloat16)
    path_pieces = (
        jnp.einsum("vjt,tf->vjf", in_chunk, layer_chunk, preferred_element_type=jnp.float32)
        .astype(jnp.bfloat16)
        .reshape(vocab_shards, path_count * model_width)
    )
    arrived = lax.all_to_all(
        jnp.concatenate([column_pieces, path_pieces], axis=1),
        "vocab",
        split_axis=0,
        concat_axis=0,
        tiled=True,
    )
    layer_part = arrived[:, : chunk_rows * share_width].reshape(token_rows, share_width)
    request_picker = (
        path_index[:, :, None] == jnp.arange(draft_length, dtype=jnp.int32)[None, None, :]
    ).astype(jnp.bfloat16)
    accepted_keys = jnp.einsum(
        "ytm,ymu->ytu",
        request_picker,
        fresh_keys.reshape(local_requests, draft_length, key_local * head_dim),
        preferred_element_type=jnp.float32,
    ).astype(jnp.bfloat16)
    accepted_values = jnp.einsum(
        "ytm,ymu->ytu",
        request_picker,
        fresh_values.reshape(local_requests, draft_length, key_local * head_dim),
        preferred_element_type=jnp.float32,
    ).astype(jnp.bfloat16)
    head_copies, path_norms = head_prepare(
        arrived, final_gain, chunk_rows * share_width, path_count, request_shards
    )
    norm_values = path_norms.reshape(local_requests, per_shard)
    gathered_head = lax.all_to_all(
        head_copies, "req", split_axis=0, concat_axis=0, tiled=True
    ).reshape(request_shards * path_count, model_width)
    local_max = jnp.max(
        jnp.dot(gathered_head, head_weight, preferred_element_type=jnp.float32),
        axis=1,
    )
    every_max = gather_rows(local_max[None], "req", request_shards)
    maxima = jnp.max(every_max, axis=0).reshape(request_shards * local_requests, per_shard)
    return (
        layer_part.reshape(local_requests, draft_length, share_width),
        accepted_keys,
        accepted_values,
        norm_values,
        maxima,
    )


def solution(mesh):
    in_specs = (
        P("req", None, None),
        P("req", None),
        P(),
        P("req", None),
        P("req"),
        P("req", "vocab"),
        P("req", "vocab"),
        P(),
        P(),
        P(),
        P(None, "vocab"),
        P(None, "vocab"),
        P(None, "vocab"),
        P("vocab", None),
        P(None, "vocab"),
        P(None, "vocab"),
        P("vocab", None),
        P(None, "req"),
    )
    out_specs = (
        P("req", None, "vocab"),
        P("req", None, "vocab"),
        P("req", None, "vocab"),
        P("req", "vocab"),
        P(None, "vocab"),
    )
    return jax.shard_map(
        per_device, mesh=mesh, in_specs=in_specs, out_specs=out_specs, check_vma=False
    )
```

```python
import jax
import jax.numpy as jnp
from jax import lax
from jax.experimental import pallas as pl
from jax.experimental.pallas import tpu as pltpu
from jax.sharding import PartitionSpec as P

HEAD_SIZE = 96


eps_norm = 1e-05
rope_base = 100000.0
masked_score = -1e30


def ancestors(parents):
    draft_length = parents.shape[-1]
    columns = jnp.arange(draft_length, dtype=jnp.int32)
    reached = jnp.eye(draft_length, dtype=jnp.float32) + (parents[..., :, None] == columns).astype(
        jnp.float32
    )
    for sweep_number in range((draft_length - 1).bit_length()):
        reached = jnp.minimum(
            jnp.einsum("bij,bjk->bik", reached, reached, precision=lax.Precision.HIGHEST), 1.0
        )
    return reached


def feed_forward_kernel(x_ref, gate_ref, up_ref, down_ref, out_ref, acc_ref):
    step = pl.program_id(0)

    @pl.when(step == 0)
    def _():
        acc_ref[...] = jnp.zeros_like(acc_ref)

    x = x_ref[...]
    gate_out = jnp.dot(x, gate_ref[...], preferred_element_type=jnp.float32)
    up_out = jnp.dot(x, up_ref[...], preferred_element_type=jnp.float32)
    hidden = (gate_out / (1.0 + jnp.exp(-gate_out)) * up_out).astype(jnp.bfloat16)
    acc_ref[...] += jnp.dot(hidden, down_ref[...], preferred_element_type=jnp.float32)

    @pl.when(step == pl.num_programs(0) - 1)
    def _():
        out_ref[...] = acc_ref[...].astype(out_ref.dtype)


def feed_forward(hidden_in, gate_weight, up_weight, down_weight, block=512):
    rows, width = hidden_in.shape
    units = gate_weight.shape[1]
    block = min(block, units)
    return pl.pallas_call(
        feed_forward_kernel,
        grid=(units // block,),
        in_specs=[
            pl.BlockSpec((rows, width), lambda j: (0, 0)),
            pl.BlockSpec((width, block), lambda j: (0, j)),
            pl.BlockSpec((width, block), lambda j: (0, j)),
            pl.BlockSpec((block, width), lambda j: (j, 0)),
        ],
        out_specs=pl.BlockSpec((rows, width), lambda j: (0, 0)),
        out_shape=jax.ShapeDtypeStruct((rows, width), jnp.bfloat16),
        scratch_shapes=[pltpu.VMEM((rows, width), jnp.float32)],
        compiler_params=pltpu.CompilerParams(dimension_semantics=("arbitrary",)),
        cost_estimate=pl.CostEstimate(
            flops=6 * rows * width * units,
            transcendentals=rows * units,
            bytes_accessed=2 * (3 * width * units + 2 * rows * width),
        ),
    )(hidden_in, gate_weight, up_weight, down_weight)


def scatter_rows(partial, axis_name, shards):
    rows = partial.shape[0] // shards
    pieces = partial.reshape(shards, rows, *partial.shape[1:]).astype(jnp.bfloat16)
    arrived = lax.all_to_all(pieces, axis_name, split_axis=0, concat_axis=0, tiled=True)
    summed = arrived[0].astype(jnp.float32)
    for source in range(1, shards):
        summed = summed + arrived[source].astype(jnp.float32)
    return summed


def gather_rows(chunk, axis_name, shards):
    copies = jnp.broadcast_to(chunk[None], (shards, *chunk.shape))
    arrived = lax.all_to_all(copies, axis_name, split_axis=0, concat_axis=0, tiled=True)
    return arrived.reshape(shards * chunk.shape[0], *chunk.shape[1:])


def per_device(
    draft_states,
    parents,
    live_draft_count,
    path_index,
    cached_length_list,
    cached_key_rows,
    cached_value_rows,
    attend_gain,
    hidden_gain,
    final_gain,
    query_weight,
    key_matrix,
    value_matrix,
    out_weight,
    gate_weight,
    up_weight,
    down_weight,
    head_weight,
):
    local_requests, draft_length, model_width = draft_states.shape
    token_rows = local_requests * draft_length
    request_shards = lax.axis_size("req")
    request_shard = lax.axis_index("req")
    vocab_shards = lax.axis_size("vocab")
    vocab_shard = lax.axis_index("vocab")
    head_dim = HEAD_SIZE
    key_local = key_matrix.shape[1] // head_dim
    query_local = query_weight.shape[1] // head_dim
    group_factor = query_local // key_local
    pool_rows = cached_key_rows.shape[0]
    states = draft_states.reshape(token_rows, model_width).astype(jnp.float32)
    normalized_states = (
        states
        * lax.rsqrt(jnp.mean(states * states, axis=1, keepdims=True) + eps_norm)
        * attend_gain.astype(jnp.float32)
    ).astype(jnp.bfloat16)
    reached = ancestors(parents)
    token_positions = (
        cached_length_list[:, None] + (jnp.sum(reached, axis=2) - 1.0).astype(jnp.int32)
    ).reshape(token_rows)
    request_states = normalized_states.reshape(local_requests, draft_length, model_width)
    request_positions = token_positions.reshape(local_requests, draft_length)
    inverse = rope_base ** (-jnp.arange(head_dim // 2, dtype=jnp.float32) * 2.0 / head_dim)
    angles = request_positions.astype(jnp.float32)[:, :, None] * inverse
    cosine = jnp.cos(angles)
    sine_of = jnp.sin(angles)

    def rotate(values):
        half = head_dim // 2
        lift = (local_requests,) + (1,) * (values.ndim - 3) + (draft_length, half)
        cos_b = cosine.reshape(lift)
        sin_b = sine_of.reshape(lift)
        first_half = values[..., :half]
        second_half = values[..., half:]
        return jnp.concatenate(
            [first_half * cos_b - second_half * sin_b, second_half * cos_b + first_half * sin_b],
            axis=-1,
        )

    query_rows = rotate(
        jnp.einsum(
            "rim,mkgd->rkgid",
            request_states,
            query_weight.reshape(model_width, key_local, group_factor, head_dim),
            preferred_element_type=jnp.float32,
        )
    ).astype(jnp.bfloat16)
    fresh_keys = rotate(
        jnp.einsum(
            "rim,mkd->rkid",
            request_states,
            key_matrix.reshape(model_width, key_local, head_dim),
            preferred_element_type=jnp.float32,
        )
    ).astype(jnp.bfloat16)
    fresh_values = jnp.einsum(
        "rim,mkd->rkid",
        request_states,
        value_matrix.reshape(model_width, key_local, head_dim),
        preferred_element_type=jnp.float32,
    ).astype(jnp.bfloat16)
    score_scale = head_dim ** (-0.5)
    pool_keys = cached_key_rows.reshape(pool_rows, key_local, head_dim)
    pool_values = cached_value_rows.reshape(pool_rows, key_local, head_dim)
    earlier = (
        jnp.arange(local_requests, dtype=jnp.int32)[None, :]
        < jnp.arange(local_requests, dtype=jnp.int32)[:, None]
    )
    cache_start = jnp.sum(jnp.where(earlier, cached_length_list[None, :], 0), axis=1)
    cache_end = cache_start + cached_length_list
    slots = jnp.arange(pool_rows, dtype=jnp.int32)
    pool_allowed = (slots[None, :] >= cache_start[:, None]) & (slots[None, :] < cache_end[:, None])
    pool_allowed = pool_allowed[:, None, None, None, :]
    tree_allowed = (reached > 0.5)[:, None, None, :, :]
    pool_scores = (
        jnp.einsum("rkgid,pkd->rkgip", query_rows, pool_keys, preferred_element_type=jnp.float32)
        * score_scale
    )
    tree_scores = (
        jnp.einsum("rkgid,rkmd->rkgim", query_rows, fresh_keys, preferred_element_type=jnp.float32)
        * score_scale
    )
    top = jnp.maximum(
        jnp.max(jnp.where(pool_allowed, pool_scores, masked_score), axis=4),
        jnp.max(jnp.where(tree_allowed, tree_scores, masked_score), axis=4),
    )
    pool_weights = jnp.where(pool_allowed, jnp.exp(pool_scores - top[..., None]), 0.0).astype(
        jnp.bfloat16
    )
    tree_weights = jnp.where(tree_allowed, jnp.exp(tree_scores - top[..., None]), 0.0).astype(
        jnp.bfloat16
    )
    totals = jnp.sum(pool_weights.astype(jnp.float32), axis=4) + jnp.sum(
        tree_weights.astype(jnp.float32), axis=4
    )
    weighted_values = jnp.einsum(
        "rkgip,pkd->rkgid", pool_weights, pool_values, preferred_element_type=jnp.float32
    ) + jnp.einsum(
        "rkgim,rkmd->rkgid", tree_weights, fresh_values, preferred_element_type=jnp.float32
    )
    attended = (weighted_values / totals[..., None]).astype(jnp.bfloat16)
    attend_part = jnp.einsum(
        "rkgid,kgdn->rin",
        attended,
        out_weight.reshape(key_local, group_factor, head_dim, model_width),
        preferred_element_type=jnp.float32,
    ).reshape(token_rows, model_width)
    fresh_keys = fresh_keys.transpose(0, 2, 1, 3)
    fresh_values = fresh_values.transpose(0, 2, 1, 3)
    chunk_rows = token_rows // vocab_shards
    chunk_start = vocab_shard * chunk_rows
    residual_chunk = lax.dynamic_slice_in_dim(states, chunk_start, chunk_rows, 0) + scatter_rows(
        attend_part, "vocab", vocab_shards
    )
    hidden_chunk = (
        residual_chunk
        * lax.rsqrt(jnp.mean(residual_chunk * residual_chunk, axis=1, keepdims=True) + eps_norm)
        * hidden_gain.astype(jnp.float32)
    ).astype(jnp.bfloat16)
    hidden_in = gather_rows(hidden_chunk, "vocab", vocab_shards)
    down_part = feed_forward(hidden_in, gate_weight, up_weight, down_weight)
    feed_chunk = scatter_rows(down_part, "vocab", vocab_shards).astype(jnp.bfloat16)
    local_counts = lax.dynamic_slice_in_dim(
        live_draft_count, request_shard * local_requests, local_requests
    )
    chunk_token = chunk_start + jnp.arange(chunk_rows, dtype=jnp.int32)
    chunk_count = jnp.take(local_counts, chunk_token // draft_length)
    chunk_live = (chunk_token % draft_length) < chunk_count
    layer_chunk = jnp.where(
        chunk_live[:, None], residual_chunk + feed_chunk.astype(jnp.float32), 0.0
    ).astype(jnp.bfloat16)
    share_width = model_width // vocab_shards
    path_length = path_index.shape[1]
    per_shard = path_length // vocab_shards
    path_count = local_requests * per_shard
    path_rows_all = (
        (
            path_index.reshape(local_requests, vocab_shards, per_shard)
            + (jnp.arange(local_requests, dtype=jnp.int32) * draft_length)[:, None, None]
        )
        .transpose(1, 0, 2)
        .reshape(vocab_shards, path_count)
    )
    column_pieces = (
        layer_chunk.reshape(chunk_rows, vocab_shards, share_width)
        .transpose(1, 0, 2)
        .reshape(vocab_shards, chunk_rows * share_width)
    )
    in_chunk = (
        path_rows_all[:, :, None] == chunk_token[None, None, :]
    ).astype(jnp.bfloat16)
    path_pieces = (
        jnp.einsum("vjt,tf->vjf", in_chunk, layer_chunk, preferred_element_type=jnp.float32)
        .astype(jnp.bfloat16)
        .reshape(vocab_shards, path_count * model_width)
    )
    arrived = lax.all_to_all(
        jnp.concatenate([column_pieces, path_pieces], axis=1),
        "vocab",
        split_axis=0,
        concat_axis=0,
        tiled=True,
    )
    layer_part = arrived[:, : chunk_rows * share_width].reshape(token_rows, share_width)
    head_rows = (
        jnp.sum(arrived[:, chunk_rows * share_width :].astype(jnp.float32), axis=0)
        .reshape(path_count, model_width)
        .astype(jnp.bfloat16)
    )
    request_picker = (
        path_index[:, :, None] == jnp.arange(draft_length, dtype=jnp.int32)[None, None, :]
    ).astype(jnp.bfloat16)
    accepted_keys = jnp.einsum(
        "ytm,ymu->ytu",
        request_picker,
        fresh_keys.reshape(local_requests, draft_length, key_local * head_dim),
        preferred_element_type=jnp.float32,
    ).astype(jnp.bfloat16)
    accepted_values = jnp.einsum(
        "ytm,ymu->ytu",
        request_picker,
        fresh_values.reshape(local_requests, draft_length, key_local * head_dim),
        preferred_element_type=jnp.float32,
    ).astype(jnp.bfloat16)
    flat_rows = head_rows.astype(jnp.float32)
    mean_square = jnp.mean(flat_rows * flat_rows, axis=1)
    norm_values = jnp.sqrt(mean_square + eps_norm).reshape(local_requests, per_shard)
    head_in = (
        flat_rows * lax.rsqrt(mean_square + eps_norm)[:, None] * final_gain.astype(jnp.float32)
    ).astype(jnp.bfloat16)
    local_max = jnp.max(
        jnp.dot(
            gather_rows(head_in, "req", request_shards),
            head_weight,
            preferred_element_type=jnp.float32,
        ),
        axis=1,
    )
    every_max = gather_rows(local_max[None], "req", request_shards)
    maxima = jnp.max(every_max, axis=0).reshape(request_shards * local_requests, per_shard)
    return (
        layer_part.reshape(local_requests, draft_length, share_width),
        accepted_keys,
        accepted_values,
        norm_values,
        maxima,
    )


def solution(mesh):
    in_specs = (
        P("req", None, None),
        P("req", None),
        P(),
        P("req", None),
        P("req"),
        P("req", "vocab"),
        P("req", "vocab"),
        P(),
        P(),
        P(),
        P(None, "vocab"),
        P(None, "vocab"),
        P(None, "vocab"),
        P("vocab", None),
        P(None, "vocab"),
        P(None, "vocab"),
        P("vocab", None),
        P(None, "req"),
    )
    out_specs = (
        P("req", None, "vocab"),
        P("req", None, "vocab"),
        P("req", None, "vocab"),
        P("req", "vocab"),
        P(None, "vocab"),
    )
    return jax.shard_map(
        per_device, mesh=mesh, in_specs=in_specs, out_specs=out_specs, check_vma=False
    )
```

```python
import functools

import jax
import jax.numpy as jnp
from jax import lax
from jax.experimental import pallas as pl
from jax.experimental.pallas import tpu as pltpu
from jax.sharding import PartitionSpec as P

HEAD_SIZE = 96


eps_norm = 1e-05
rope_base = 100000.0
masked_score = -1e30


def ancestors(parents):
    draft_length = parents.shape[-1]
    columns = jnp.arange(draft_length, dtype=jnp.int32)
    reached = jnp.eye(draft_length, dtype=jnp.float32) + (parents[..., :, None] == columns).astype(
        jnp.float32
    )
    for sweep_number in range((draft_length - 1).bit_length()):
        reached = jnp.minimum(
            jnp.einsum("bij,bjk->bik", reached, reached, precision=lax.Precision.HIGHEST), 1.0
        )
    return reached


def feed_forward_kernel(x_ref, gate_ref, up_ref, down_ref, out_ref, acc_ref):
    step = pl.program_id(0)

    @pl.when(step == 0)
    def _():
        acc_ref[...] = jnp.zeros_like(acc_ref)

    x = x_ref[...]
    gate_out = jnp.dot(x, gate_ref[...], preferred_element_type=jnp.float32)
    up_out = jnp.dot(x, up_ref[...], preferred_element_type=jnp.float32)
    hidden = (gate_out / (1.0 + jnp.exp(-gate_out)) * up_out).astype(jnp.bfloat16)
    acc_ref[...] += jnp.dot(hidden, down_ref[...], preferred_element_type=jnp.float32)

    @pl.when(step == pl.num_programs(0) - 1)
    def _():
        out_ref[...] = acc_ref[...].astype(out_ref.dtype)


def feed_forward(hidden_in, gate_weight, up_weight, down_weight, block=512):
    rows, width = hidden_in.shape
    units = gate_weight.shape[1]
    block = min(block, units)
    return pl.pallas_call(
        feed_forward_kernel,
        grid=(units // block,),
        in_specs=[
            pl.BlockSpec((rows, width), lambda j: (0, 0)),
            pl.BlockSpec((width, block), lambda j: (0, j)),
            pl.BlockSpec((width, block), lambda j: (0, j)),
            pl.BlockSpec((block, width), lambda j: (j, 0)),
        ],
        out_specs=pl.BlockSpec((rows, width), lambda j: (0, 0)),
        out_shape=jax.ShapeDtypeStruct((rows, width), jnp.bfloat16),
        scratch_shapes=[pltpu.VMEM((rows, width), jnp.float32)],
        compiler_params=pltpu.CompilerParams(dimension_semantics=("arbitrary",)),
        cost_estimate=pl.CostEstimate(
            flops=6 * rows * width * units,
            transcendentals=rows * units,
            bytes_accessed=2 * (3 * width * units + 2 * rows * width),
        ),
    )(hidden_in, gate_weight, up_weight, down_weight)


def scatter_rows(partial, axis_name, shards):
    rows = partial.shape[0] // shards
    pieces = partial.reshape(shards, rows, *partial.shape[1:]).astype(jnp.bfloat16)
    arrived = lax.all_to_all(pieces, axis_name, split_axis=0, concat_axis=0, tiled=True)
    summed = arrived[0].astype(jnp.float32)
    for source in range(1, shards):
        summed = summed + arrived[source].astype(jnp.float32)
    return summed


def gather_rows(chunk, axis_name, shards):
    copies = jnp.broadcast_to(chunk[None], (shards, *chunk.shape))
    arrived = lax.all_to_all(copies, axis_name, split_axis=0, concat_axis=0, tiled=True)
    return arrived.reshape(shards * chunk.shape[0], *chunk.shape[1:])


def per_device(
    draft_states,
    parents,
    live_draft_count,
    path_index,
    cached_length_list,
    cached_key_rows,
    cached_value_rows,
    attend_gain,
    hidden_gain,
    final_gain,
    query_weight,
    key_matrix,
    value_matrix,
    out_weight,
    gate_weight,
    up_weight,
    down_weight,
    head_weight,
):
    local_requests, draft_length, model_width = draft_states.shape
    token_rows = local_requests * draft_length
    request_shards = lax.axis_size("req")
    request_shard = lax.axis_index("req")
    vocab_shards = lax.axis_size("vocab")
    vocab_shard = lax.axis_index("vocab")
    head_dim = HEAD_SIZE
    key_local = key_matrix.shape[1] // head_dim
    query_local = query_weight.shape[1] // head_dim
    group_factor = query_local // key_local
    pool_rows = cached_key_rows.shape[0]
    states = draft_states.reshape(token_rows, model_width).astype(jnp.float32)
    normalized_states = (
        states
        * lax.rsqrt(jnp.mean(states * states, axis=1, keepdims=True) + eps_norm)
        * attend_gain.astype(jnp.float32)
    ).astype(jnp.bfloat16)
    reached = ancestors(parents)
    token_positions = (
        cached_length_list[:, None] + (jnp.sum(reached, axis=2) - 1.0).astype(jnp.int32)
    ).reshape(token_rows)
    request_states = normalized_states.reshape(local_requests, draft_length, model_width)
    request_positions = token_positions.reshape(local_requests, draft_length)
    inverse = rope_base ** (-jnp.arange(head_dim // 2, dtype=jnp.float32) * 2.0 / head_dim)
    angles = request_positions.astype(jnp.float32)[:, :, None] * inverse
    cosine = jnp.cos(angles)
    sine_of = jnp.sin(angles)

    def rotate(values):
        half = head_dim // 2
        lift = (local_requests,) + (1,) * (values.ndim - 3) + (draft_length, half)
        cos_b = cosine.reshape(lift)
        sin_b = sine_of.reshape(lift)
        first_half = values[..., :half]
        second_half = values[..., half:]
        return jnp.concatenate(
            [first_half * cos_b - second_half * sin_b, second_half * cos_b + first_half * sin_b],
            axis=-1,
        )

    query_rows = rotate(
        jnp.einsum(
            "rim,mkgd->rkgid",
            request_states,
            query_weight.reshape(model_width, key_local, group_factor, head_dim),
            preferred_element_type=jnp.float32,
        )
    ).astype(jnp.bfloat16)
    fresh_keys = rotate(
        jnp.einsum(
            "rim,mkd->rkid",
            request_states,
            key_matrix.reshape(model_width, key_local, head_dim),
            preferred_element_type=jnp.float32,
        )
    ).astype(jnp.bfloat16)
    fresh_values = jnp.einsum(
        "rim,mkd->rkid",
        request_states,
        value_matrix.reshape(model_width, key_local, head_dim),
        preferred_element_type=jnp.float32,
    ).astype(jnp.bfloat16)
    score_scale = head_dim ** (-0.5)
    pool_keys = cached_key_rows.reshape(pool_rows, key_local, head_dim)
    pool_values = cached_value_rows.reshape(pool_rows, key_local, head_dim)
    earlier = (
        jnp.arange(local_requests, dtype=jnp.int32)[None, :]
        < jnp.arange(local_requests, dtype=jnp.int32)[:, None]
    )
    cache_start = jnp.sum(jnp.where(earlier, cached_length_list[None, :], 0), axis=1)
    cache_end = cache_start + cached_length_list
    slots = jnp.arange(pool_rows, dtype=jnp.int32)
    pool_allowed = (slots[None, :] >= cache_start[:, None]) & (slots[None, :] < cache_end[:, None])
    pool_allowed = pool_allowed[:, None, None, None, :]
    tree_allowed = (reached > 0.5)[:, None, None, :, :]
    pool_scores = (
        jnp.einsum("rkgid,pkd->rkgip", query_rows, pool_keys, preferred_element_type=jnp.float32)
        * score_scale
    )
    tree_scores = (
        jnp.einsum("rkgid,rkmd->rkgim", query_rows, fresh_keys, preferred_element_type=jnp.float32)
        * score_scale
    )
    top = jnp.maximum(
        jnp.max(jnp.where(pool_allowed, pool_scores, masked_score), axis=4),
        jnp.max(jnp.where(tree_allowed, tree_scores, masked_score), axis=4),
    )
    pool_weights = jnp.where(pool_allowed, jnp.exp(pool_scores - top[..., None]), 0.0).astype(
        jnp.bfloat16
    )
    tree_weights = jnp.where(tree_allowed, jnp.exp(tree_scores - top[..., None]), 0.0).astype(
        jnp.bfloat16
    )
    totals = jnp.sum(pool_weights.astype(jnp.float32), axis=4) + jnp.sum(
        tree_weights.astype(jnp.float32), axis=4
    )
    weighted_values = jnp.einsum(
        "rkgip,pkd->rkgid", pool_weights, pool_values, preferred_element_type=jnp.float32
    ) + jnp.einsum(
        "rkgim,rkmd->rkgid", tree_weights, fresh_values, preferred_element_type=jnp.float32
    )
    attended = (weighted_values / totals[..., None]).astype(jnp.bfloat16)
    attend_part = jnp.einsum(
        "rkgid,kgdn->rin",
        attended,
        out_weight.reshape(key_local, group_factor, head_dim, model_width),
        preferred_element_type=jnp.float32,
    ).reshape(token_rows, model_width)
    fresh_keys = fresh_keys.transpose(0, 2, 1, 3)
    fresh_values = fresh_values.transpose(0, 2, 1, 3)
    chunk_rows = token_rows // vocab_shards
    chunk_start = vocab_shard * chunk_rows
    residual_chunk = lax.dynamic_slice_in_dim(states, chunk_start, chunk_rows, 0) + scatter_rows(
        attend_part, "vocab", vocab_shards
    )
    hidden_chunk = (
        residual_chunk
        * lax.rsqrt(jnp.mean(residual_chunk * residual_chunk, axis=1, keepdims=True) + eps_norm)
        * hidden_gain.astype(jnp.float32)
    ).astype(jnp.bfloat16)
    hidden_in = gather_rows(hidden_chunk, "vocab", vocab_shards)
    down_part = feed_forward(hidden_in, gate_weight, up_weight, down_weight)
    feed_chunk = scatter_rows(down_part, "vocab", vocab_shards).astype(jnp.bfloat16)
    local_counts = lax.dynamic_slice_in_dim(
        live_draft_count, request_shard * local_requests, local_requests
    )
    chunk_token = chunk_start + jnp.arange(chunk_rows, dtype=jnp.int32)
    chunk_count = jnp.take(local_counts, chunk_token // draft_length)
    chunk_live = (chunk_token % draft_length) < chunk_count
    layer_chunk = jnp.where(
        chunk_live[:, None], residual_chunk + feed_chunk.astype(jnp.float32), 0.0
    ).astype(jnp.bfloat16)
    share_width = model_width // vocab_shards
    path_length = path_index.shape[1]
    per_shard = path_length // vocab_shards
    path_count = local_requests * per_shard
    path_rows_all = (
        (
            path_index.reshape(local_requests, vocab_shards, per_shard)
            + (jnp.arange(local_requests, dtype=jnp.int32) * draft_length)[:, None, None]
        )
        .transpose(1, 0, 2)
        .reshape(vocab_shards, path_count)
    )
    column_pieces = (
        layer_chunk.reshape(chunk_rows, vocab_shards, share_width)
        .transpose(1, 0, 2)
        .reshape(vocab_shards, chunk_rows * share_width)
    )
    in_chunk = (
        path_rows_all[:, :, None] == chunk_token[None, None, :]
    ).astype(jnp.bfloat16)
    path_pieces = (
        jnp.einsum("vjt,tf->vjf", in_chunk, layer_chunk, preferred_element_type=jnp.float32)
        .astype(jnp.bfloat16)
        .reshape(vocab_shards, path_count * model_width)
    )
    arrived = lax.all_to_all(
        jnp.concatenate([column_pieces, path_pieces], axis=1),
        "vocab",
        split_axis=0,
        concat_axis=0,
        tiled=True,
    )
    layer_part = arrived[:, : chunk_rows * share_width].reshape(token_rows, share_width)
    head_rows = (
        functools.reduce(
            jnp.add,
            [arrived[source, chunk_rows * share_width :].astype(jnp.float32) for source in range(vocab_shards)],
        )
        .reshape(path_count, model_width)
        .astype(jnp.bfloat16)
    )
    request_picker = (
        path_index[:, :, None] == jnp.arange(draft_length, dtype=jnp.int32)[None, None, :]
    ).astype(jnp.bfloat16)
    accepted_keys = jnp.einsum(
        "ytm,ymu->ytu",
        request_picker,
        fresh_keys.reshape(local_requests, draft_length, key_local * head_dim),
        preferred_element_type=jnp.float32,
    ).astype(jnp.bfloat16)
    accepted_values = jnp.einsum(
        "ytm,ymu->ytu",
        request_picker,
        fresh_values.reshape(local_requests, draft_length, key_local * head_dim),
        preferred_element_type=jnp.float32,
    ).astype(jnp.bfloat16)
    flat_rows = head_rows.astype(jnp.float32)
    mean_square = jnp.mean(flat_rows * flat_rows, axis=1)
    norm_values = jnp.sqrt(mean_square + eps_norm).reshape(local_requests, per_shard)
    head_in = (
        flat_rows * lax.rsqrt(mean_square + eps_norm)[:, None] * final_gain.astype(jnp.float32)
    ).astype(jnp.bfloat16)
    local_max = jnp.max(
        jnp.dot(
            gather_rows(head_in, "req", request_shards),
            head_weight,
            preferred_element_type=jnp.float32,
        ),
        axis=1,
    )
    every_max = gather_rows(local_max[None], "req", request_shards)
    maxima = functools.reduce(
        jnp.maximum, [every_max[source] for source in range(request_shards)]
    ).reshape(request_shards * local_requests, per_shard)
    return (
        layer_part.reshape(local_requests, draft_length, share_width),
        accepted_keys,
        accepted_values,
        norm_values,
        maxima,
    )


def solution(mesh):
    in_specs = (
        P("req", None, None),
        P("req", None),
        P(),
        P("req", None),
        P("req"),
        P("req", "vocab"),
        P("req", "vocab"),
        P(),
        P(),
        P(),
        P(None, "vocab"),
        P(None, "vocab"),
        P(None, "vocab"),
        P("vocab", None),
        P(None, "vocab"),
        P(None, "vocab"),
        P("vocab", None),
        P(None, "req"),
    )
    out_specs = (
        P("req", None, "vocab"),
        P("req", None, "vocab"),
        P("req", None, "vocab"),
        P("req", "vocab"),
        P(None, "vocab"),
    )
    return jax.shard_map(
        per_device, mesh=mesh, in_specs=in_specs, out_specs=out_specs, check_vma=False
    )
```

```python
import jax
import jax.numpy as jnp
from jax import lax
from jax.experimental import pallas as pl
from jax.experimental.pallas import tpu as pltpu
from jax.sharding import PartitionSpec as P

HEAD_SIZE = 96


eps_norm = 1e-05
rope_base = 100000.0
masked_score = -1e30


def ancestors(parents):
    draft_length = parents.shape[-1]
    columns = jnp.arange(draft_length, dtype=jnp.int32)
    reached = jnp.eye(draft_length, dtype=jnp.float32) + (parents[..., :, None] == columns).astype(
        jnp.float32
    )
    for sweep_number in range((draft_length - 1).bit_length()):
        reached = jnp.minimum(
            jnp.einsum("bij,bjk->bik", reached, reached, precision=lax.Precision.HIGHEST), 1.0
        )
    return reached


def feed_forward_kernel(x_ref, gate_ref, up_ref, down_ref, out_ref, acc_ref):
    step = pl.program_id(0)

    @pl.when(step == 0)
    def _():
        acc_ref[...] = jnp.zeros_like(acc_ref)

    x = x_ref[...]
    gate_out = jnp.dot(x, gate_ref[...], preferred_element_type=jnp.float32)
    up_out = jnp.dot(x, up_ref[...], preferred_element_type=jnp.float32)
    hidden = (gate_out / (1.0 + jnp.exp(-gate_out)) * up_out).astype(jnp.bfloat16)
    acc_ref[...] += jnp.dot(hidden, down_ref[...], preferred_element_type=jnp.float32)

    @pl.when(step == pl.num_programs(0) - 1)
    def _():
        out_ref[...] = acc_ref[...].astype(out_ref.dtype)


def feed_forward(hidden_in, gate_weight, up_weight, down_weight, block=512):
    rows, width = hidden_in.shape
    units = gate_weight.shape[1]
    block = min(block, units)
    return pl.pallas_call(
        feed_forward_kernel,
        grid=(units // block,),
        in_specs=[
            pl.BlockSpec((rows, width), lambda j: (0, 0)),
            pl.BlockSpec((width, block), lambda j: (0, j)),
            pl.BlockSpec((width, block), lambda j: (0, j)),
            pl.BlockSpec((block, width), lambda j: (j, 0)),
        ],
        out_specs=pl.BlockSpec((rows, width), lambda j: (0, 0)),
        out_shape=jax.ShapeDtypeStruct((rows, width), jnp.bfloat16),
        scratch_shapes=[pltpu.VMEM((rows, width), jnp.float32)],
        compiler_params=pltpu.CompilerParams(dimension_semantics=("arbitrary",)),
        cost_estimate=pl.CostEstimate(
            flops=6 * rows * width * units,
            transcendentals=rows * units,
            bytes_accessed=2 * (3 * width * units + 2 * rows * width),
        ),
    )(hidden_in, gate_weight, up_weight, down_weight)


def scatter_rows(partial, axis_name, shards):
    rows = partial.shape[0] // shards
    pieces = partial.reshape(shards, rows, *partial.shape[1:]).astype(jnp.bfloat16)
    arrived = lax.all_to_all(pieces, axis_name, split_axis=0, concat_axis=0, tiled=True)
    summed = arrived[0].astype(jnp.float32)
    for source in range(1, shards):
        summed = summed + arrived[source].astype(jnp.float32)
    return summed


def gather_rows(chunk, axis_name, shards):
    copies = jnp.broadcast_to(chunk[None], (shards, *chunk.shape))
    arrived = lax.all_to_all(copies, axis_name, split_axis=0, concat_axis=0, tiled=True)
    return arrived.reshape(shards * chunk.shape[0], *chunk.shape[1:])


def per_device(
    draft_states,
    parents,
    live_draft_count,
    path_index,
    cached_length_list,
    cached_key_rows,
    cached_value_rows,
    attend_gain,
    hidden_gain,
    final_gain,
    query_weight,
    key_matrix,
    value_matrix,
    out_weight,
    gate_weight,
    up_weight,
    down_weight,
    head_weight,
):
    local_requests, draft_length, model_width = draft_states.shape
    token_rows = local_requests * draft_length
    request_shards = lax.axis_size("req")
    request_shard = lax.axis_index("req")
    vocab_shards = lax.axis_size("vocab")
    vocab_shard = lax.axis_index("vocab")
    head_dim = HEAD_SIZE
    key_local = key_matrix.shape[1] // head_dim
    query_local = query_weight.shape[1] // head_dim
    group_factor = query_local // key_local
    pool_rows = cached_key_rows.shape[0]
    states = draft_states.reshape(token_rows, model_width).astype(jnp.float32)
    normalized_states = (
        states
        * lax.rsqrt(jnp.mean(states * states, axis=1, keepdims=True) + eps_norm)
        * attend_gain.astype(jnp.float32)
    ).astype(jnp.bfloat16)
    reached = ancestors(parents)
    token_positions = (
        cached_length_list[:, None] + (jnp.sum(reached, axis=2) - 1.0).astype(jnp.int32)
    ).reshape(token_rows)
    request_states = normalized_states.reshape(local_requests, draft_length, model_width)
    request_positions = token_positions.reshape(local_requests, draft_length)
    inverse = rope_base ** (-jnp.arange(head_dim // 2, dtype=jnp.float32) * 2.0 / head_dim)
    angles = request_positions.astype(jnp.float32)[:, :, None] * inverse
    cosine = jnp.cos(angles)
    sine_of = jnp.sin(angles)

    def rotate(values):
        half = head_dim // 2
        lift = (local_requests,) + (1,) * (values.ndim - 3) + (draft_length, half)
        cos_b = cosine.reshape(lift)
        sin_b = sine_of.reshape(lift)
        first_half = values[..., :half]
        second_half = values[..., half:]
        return jnp.concatenate(
            [first_half * cos_b - second_half * sin_b, second_half * cos_b + first_half * sin_b],
            axis=-1,
        )

    query_rows = rotate(
        jnp.einsum(
            "rim,mkgd->rkgid",
            request_states,
            query_weight.reshape(model_width, key_local, group_factor, head_dim),
            preferred_element_type=jnp.float32,
        )
    ).astype(jnp.bfloat16)
    fresh_keys = rotate(
        jnp.einsum(
            "rim,mkd->rkid",
            request_states,
            key_matrix.reshape(model_width, key_local, head_dim),
            preferred_element_type=jnp.float32,
        )
    ).astype(jnp.bfloat16)
    fresh_values = jnp.einsum(
        "rim,mkd->rkid",
        request_states,
        value_matrix.reshape(model_width, key_local, head_dim),
        preferred_element_type=jnp.float32,
    ).astype(jnp.bfloat16)
    score_scale = head_dim ** (-0.5)
    pool_keys = cached_key_rows.reshape(pool_rows, key_local, head_dim)
    pool_values = cached_value_rows.reshape(pool_rows, key_local, head_dim)
    earlier = (
        jnp.arange(local_requests, dtype=jnp.int32)[None, :]
        < jnp.arange(local_requests, dtype=jnp.int32)[:, None]
    )
    cache_start = jnp.sum(jnp.where(earlier, cached_length_list[None, :], 0), axis=1)
    cache_end = cache_start + cached_length_list
    slots = jnp.arange(pool_rows, dtype=jnp.int32)
    pool_allowed = (slots[None, :] >= cache_start[:, None]) & (slots[None, :] < cache_end[:, None])
    pool_allowed = pool_allowed[:, None, None, None, :]
    tree_allowed = (reached > 0.5)[:, None, None, :, :]
    pool_scores = (
        jnp.einsum("rkgid,pkd->rkgip", query_rows, pool_keys, preferred_element_type=jnp.float32)
        * score_scale
    )
    tree_scores = (
        jnp.einsum("rkgid,rkmd->rkgim", query_rows, fresh_keys, preferred_element_type=jnp.float32)
        * score_scale
    )
    top = jnp.maximum(
        jnp.max(jnp.where(pool_allowed, pool_scores, masked_score), axis=4),
        jnp.max(jnp.where(tree_allowed, tree_scores, masked_score), axis=4),
    )
    pool_weights = jnp.where(pool_allowed, jnp.exp(pool_scores - top[..., None]), 0.0).astype(
        jnp.bfloat16
    )
    tree_weights = jnp.where(tree_allowed, jnp.exp(tree_scores - top[..., None]), 0.0).astype(
        jnp.bfloat16
    )
    totals = jnp.sum(pool_weights.astype(jnp.float32), axis=4) + jnp.sum(
        tree_weights.astype(jnp.float32), axis=4
    )
    weighted_values = jnp.einsum(
        "rkgip,pkd->rkgid", pool_weights, pool_values, preferred_element_type=jnp.float32
    ) + jnp.einsum(
        "rkgim,rkmd->rkgid", tree_weights, fresh_values, preferred_element_type=jnp.float32
    )
    attended = (weighted_values / totals[..., None]).astype(jnp.bfloat16)
    attend_part = jnp.einsum(
        "rkgid,kgdn->rin",
        attended,
        out_weight.reshape(key_local, group_factor, head_dim, model_width),
        preferred_element_type=jnp.float32,
    ).reshape(token_rows, model_width)
    fresh_keys = fresh_keys.transpose(0, 2, 1, 3)
    fresh_values = fresh_values.transpose(0, 2, 1, 3)
    chunk_rows = token_rows // vocab_shards
    chunk_start = vocab_shard * chunk_rows
    residual_chunk = lax.dynamic_slice_in_dim(states, chunk_start, chunk_rows, 0) + scatter_rows(
        attend_part, "vocab", vocab_shards
    )
    hidden_copies = (
        jnp.broadcast_to(residual_chunk[None], (vocab_shards, chunk_rows, model_width))
        * lax.rsqrt(jnp.mean(residual_chunk * residual_chunk, axis=1, keepdims=True) + eps_norm)[None]
        * hidden_gain.astype(jnp.float32)
    ).astype(jnp.bfloat16)
    hidden_in = lax.all_to_all(
        hidden_copies, "vocab", split_axis=0, concat_axis=0, tiled=True
    ).reshape(token_rows, model_width)
    down_part = feed_forward(hidden_in, gate_weight, up_weight, down_weight)
    feed_chunk = scatter_rows(down_part, "vocab", vocab_shards).astype(jnp.bfloat16)
    local_counts = lax.dynamic_slice_in_dim(
        live_draft_count, request_shard * local_requests, local_requests
    )
    chunk_token = chunk_start + jnp.arange(chunk_rows, dtype=jnp.int32)
    chunk_count = jnp.take(local_counts, chunk_token // draft_length)
    chunk_live = (chunk_token % draft_length) < chunk_count
    layer_chunk = jnp.where(
        chunk_live[:, None], residual_chunk + feed_chunk.astype(jnp.float32), 0.0
    ).astype(jnp.bfloat16)
    share_width = model_width // vocab_shards
    path_length = path_index.shape[1]
    per_shard = path_length // vocab_shards
    path_count = local_requests * per_shard
    path_rows_all = (
        (
            path_index.reshape(local_requests, vocab_shards, per_shard)
            + (jnp.arange(local_requests, dtype=jnp.int32) * draft_length)[:, None, None]
        )
        .transpose(1, 0, 2)
        .reshape(vocab_shards, path_count)
    )
    column_pieces = (
        layer_chunk.reshape(chunk_rows, vocab_shards, share_width)
        .transpose(1, 0, 2)
        .reshape(vocab_shards, chunk_rows * share_width)
    )
    in_chunk = (
        path_rows_all[:, :, None] == chunk_token[None, None, :]
    ).astype(jnp.bfloat16)
    path_pieces = (
        jnp.einsum("vjt,tf->vjf", in_chunk, layer_chunk, preferred_element_type=jnp.float32)
        .astype(jnp.bfloat16)
        .reshape(vocab_shards, path_count * model_width)
    )
    arrived = lax.all_to_all(
        jnp.concatenate([column_pieces, path_pieces], axis=1),
        "vocab",
        split_axis=0,
        concat_axis=0,
        tiled=True,
    )
    layer_part = arrived[:, : chunk_rows * share_width].reshape(token_rows, share_width)
    head_rows = (
        jnp.sum(arrived[:, chunk_rows * share_width :].astype(jnp.float32), axis=0)
        .reshape(path_count, model_width)
        .astype(jnp.bfloat16)
    )
    request_picker = (
        path_index[:, :, None] == jnp.arange(draft_length, dtype=jnp.int32)[None, None, :]
    ).astype(jnp.bfloat16)
    accepted_keys = jnp.einsum(
        "ytm,ymu->ytu",
        request_picker,
        fresh_keys.reshape(local_requests, draft_length, key_local * head_dim),
        preferred_element_type=jnp.float32,
    ).astype(jnp.bfloat16)
    accepted_values = jnp.einsum(
        "ytm,ymu->ytu",
        request_picker,
        fresh_values.reshape(local_requests, draft_length, key_local * head_dim),
        preferred_element_type=jnp.float32,
    ).astype(jnp.bfloat16)
    flat_rows = head_rows.astype(jnp.float32)
    mean_square = jnp.mean(flat_rows * flat_rows, axis=1)
    norm_values = jnp.sqrt(mean_square + eps_norm).reshape(local_requests, per_shard)
    head_in = (
        flat_rows * lax.rsqrt(mean_square + eps_norm)[:, None] * final_gain.astype(jnp.float32)
    ).astype(jnp.bfloat16)
    local_max = jnp.max(
        jnp.dot(
            gather_rows(head_in, "req", request_shards),
            head_weight,
            preferred_element_type=jnp.float32,
        ),
        axis=1,
    )
    every_max = gather_rows(local_max[None], "req", request_shards)
    maxima = jnp.max(every_max, axis=0).reshape(request_shards * local_requests, per_shard)
    return (
        layer_part.reshape(local_requests, draft_length, share_width),
        accepted_keys,
        accepted_values,
        norm_values,
        maxima,
    )


def solution(mesh):
    in_specs = (
        P("req", None, None),
        P("req", None),
        P(),
        P("req", None),
        P("req"),
        P("req", "vocab"),
        P("req", "vocab"),
        P(),
        P(),
        P(),
        P(None, "vocab"),
        P(None, "vocab"),
        P(None, "vocab"),
        P("vocab", None),
        P(None, "vocab"),
        P(None, "vocab"),
        P("vocab", None),
        P(None, "req"),
    )
    out_specs = (
        P("req", None, "vocab"),
        P("req", None, "vocab"),
        P("req", None, "vocab"),
        P("req", "vocab"),
        P(None, "vocab"),
    )
    return jax.shard_map(
        per_device, mesh=mesh, in_specs=in_specs, out_specs=out_specs, check_vma=False
    )
```

```python
import jax
import jax.numpy as jnp
from jax import lax
from jax.experimental import pallas as pl
from jax.experimental.pallas import tpu as pltpu
from jax.sharding import PartitionSpec as P

HEAD_SIZE = 96


eps_norm = 1e-05
rope_base = 100000.0
masked_score = -1e30


def ancestors(parents):
    draft_length = parents.shape[-1]
    columns = jnp.arange(draft_length, dtype=jnp.int32)
    reached = jnp.eye(draft_length, dtype=jnp.float32) + (parents[..., :, None] == columns).astype(
        jnp.float32
    )
    for sweep_number in range((draft_length - 1).bit_length()):
        reached = jnp.minimum(
            jnp.einsum("bij,bjk->bik", reached, reached, precision=lax.Precision.HIGHEST), 1.0
        )
    return reached


def feed_forward_kernel(x_ref, gate_ref, up_ref, down_ref, out_ref, acc_ref):
    step = pl.program_id(0)

    @pl.when(step == 0)
    def _():
        acc_ref[...] = jnp.zeros_like(acc_ref)

    x = x_ref[...]
    gate_out = jnp.dot(x, gate_ref[...], preferred_element_type=jnp.float32)
    up_out = jnp.dot(x, up_ref[...], preferred_element_type=jnp.float32)
    hidden = (gate_out / (1.0 + jnp.exp(-gate_out)) * up_out).astype(jnp.bfloat16)
    acc_ref[...] += jnp.dot(hidden, down_ref[...], preferred_element_type=jnp.float32)

    @pl.when(step == pl.num_programs(0) - 1)
    def _():
        out_ref[...] = acc_ref[...].astype(out_ref.dtype)


def feed_forward(hidden_in, gate_weight, up_weight, down_weight, block=512):
    rows, width = hidden_in.shape
    units = gate_weight.shape[1]
    block = min(block, units)
    return pl.pallas_call(
        feed_forward_kernel,
        grid=(units // block,),
        in_specs=[
            pl.BlockSpec((rows, width), lambda j: (0, 0)),
            pl.BlockSpec((width, block), lambda j: (0, j)),
            pl.BlockSpec((width, block), lambda j: (0, j)),
            pl.BlockSpec((block, width), lambda j: (j, 0)),
        ],
        out_specs=pl.BlockSpec((rows, width), lambda j: (0, 0)),
        out_shape=jax.ShapeDtypeStruct((rows, width), jnp.bfloat16),
        scratch_shapes=[pltpu.VMEM((rows, width), jnp.float32)],
        compiler_params=pltpu.CompilerParams(dimension_semantics=("arbitrary",)),
        cost_estimate=pl.CostEstimate(
            flops=6 * rows * width * units,
            transcendentals=rows * units,
            bytes_accessed=2 * (3 * width * units + 2 * rows * width),
        ),
    )(hidden_in, gate_weight, up_weight, down_weight)


def scatter_rows(partial, axis_name, shards):
    rows = partial.shape[0] // shards
    pieces = partial.reshape(shards, rows, *partial.shape[1:]).astype(jnp.bfloat16)
    arrived = lax.all_to_all(pieces, axis_name, split_axis=0, concat_axis=0, tiled=True)
    summed = arrived[0].astype(jnp.float32)
    for source in range(1, shards):
        summed = summed + arrived[source].astype(jnp.float32)
    return summed


def gather_rows(chunk, axis_name, shards):
    copies = jnp.broadcast_to(chunk[None], (shards, *chunk.shape))
    arrived = lax.all_to_all(copies, axis_name, split_axis=0, concat_axis=0, tiled=True)
    return arrived.reshape(shards * chunk.shape[0], *chunk.shape[1:])


def per_device(
    draft_states,
    parents,
    live_draft_count,
    path_index,
    cached_length_list,
    cached_key_rows,
    cached_value_rows,
    attend_gain,
    hidden_gain,
    final_gain,
    query_weight,
    key_matrix,
    value_matrix,
    out_weight,
    gate_weight,
    up_weight,
    down_weight,
    head_weight,
):
    local_requests, draft_length, model_width = draft_states.shape
    token_rows = local_requests * draft_length
    request_shards = lax.axis_size("req")
    request_shard = lax.axis_index("req")
    vocab_shards = lax.axis_size("vocab")
    vocab_shard = lax.axis_index("vocab")
    head_dim = HEAD_SIZE
    key_local = key_matrix.shape[1] // head_dim
    query_local = query_weight.shape[1] // head_dim
    group_factor = query_local // key_local
    pool_rows = cached_key_rows.shape[0]
    states = draft_states.reshape(token_rows, model_width).astype(jnp.float32)
    normalized_states = (
        states
        * lax.rsqrt(jnp.mean(states * states, axis=1, keepdims=True) + eps_norm)
        * attend_gain.astype(jnp.float32)
    ).astype(jnp.bfloat16)
    reached = ancestors(parents)
    token_positions = (
        cached_length_list[:, None] + (jnp.sum(reached, axis=2) - 1.0).astype(jnp.int32)
    ).reshape(token_rows)
    request_states = normalized_states.reshape(local_requests, draft_length, model_width)
    request_positions = token_positions.reshape(local_requests, draft_length)
    inverse = rope_base ** (-jnp.arange(head_dim // 2, dtype=jnp.float32) * 2.0 / head_dim)
    angles = request_positions.astype(jnp.float32)[:, :, None] * inverse
    cosine = jnp.cos(angles)
    sine_of = jnp.sin(angles)

    def rotate(values):
        half = head_dim // 2
        lift = (local_requests,) + (1,) * (values.ndim - 3) + (draft_length, half)
        cos_b = cosine.reshape(lift)
        sin_b = sine_of.reshape(lift)
        first_half = values[..., :half]
        second_half = values[..., half:]
        return jnp.concatenate(
            [first_half * cos_b - second_half * sin_b, second_half * cos_b + first_half * sin_b],
            axis=-1,
        )

    query_rows = rotate(
        jnp.einsum(
            "rim,mkgd->rkgid",
            request_states,
            query_weight.reshape(model_width, key_local, group_factor, head_dim),
            preferred_element_type=jnp.float32,
        )
    ).astype(jnp.bfloat16)
    fresh_keys = rotate(
        jnp.einsum(
            "rim,mkd->rkid",
            request_states,
            key_matrix.reshape(model_width, key_local, head_dim),
            preferred_element_type=jnp.float32,
        )
    ).astype(jnp.bfloat16)
    fresh_values = jnp.einsum(
        "rim,mkd->rkid",
        request_states,
        value_matrix.reshape(model_width, key_local, head_dim),
        preferred_element_type=jnp.float32,
    ).astype(jnp.bfloat16)
    score_scale = head_dim ** (-0.5)
    pool_keys = cached_key_rows.reshape(pool_rows, key_local, head_dim)
    pool_values = cached_value_rows.reshape(pool_rows, key_local, head_dim)
    earlier = (
        jnp.arange(local_requests, dtype=jnp.int32)[None, :]
        < jnp.arange(local_requests, dtype=jnp.int32)[:, None]
    )
    cache_start = jnp.sum(jnp.where(earlier, cached_length_list[None, :], 0), axis=1)
    cache_end = cache_start + cached_length_list
    slots = jnp.arange(pool_rows, dtype=jnp.int32)
    pool_allowed = (slots[None, :] >= cache_start[:, None]) & (slots[None, :] < cache_end[:, None])
    pool_allowed = pool_allowed[:, None, None, None, :]
    tree_allowed = (reached > 0.5)[:, None, None, :, :]
    pool_scores = (
        jnp.einsum("rkgid,pkd->rkgip", query_rows, pool_keys, preferred_element_type=jnp.float32)
        * score_scale
    )
    tree_scores = (
        jnp.einsum("rkgid,rkmd->rkgim", query_rows, fresh_keys, preferred_element_type=jnp.float32)
        * score_scale
    )
    top = jnp.maximum(
        jnp.max(jnp.where(pool_allowed, pool_scores, masked_score), axis=4),
        jnp.max(jnp.where(tree_allowed, tree_scores, masked_score), axis=4),
    )
    pool_weights = jnp.where(pool_allowed, jnp.exp(pool_scores - top[..., None]), 0.0).astype(
        jnp.bfloat16
    )
    tree_weights = jnp.where(tree_allowed, jnp.exp(tree_scores - top[..., None]), 0.0).astype(
        jnp.bfloat16
    )
    totals = jnp.sum(pool_weights.astype(jnp.float32), axis=4) + jnp.sum(
        tree_weights.astype(jnp.float32), axis=4
    )
    weighted_values = jnp.einsum(
        "rkgip,pkd->rkgid", pool_weights, pool_values, preferred_element_type=jnp.float32
    ) + jnp.einsum(
        "rkgim,rkmd->rkgid", tree_weights, fresh_values, preferred_element_type=jnp.float32
    )
    attended = (weighted_values / totals[..., None]).astype(jnp.bfloat16)
    attend_part = jnp.einsum(
        "rkgid,kgdn->rin",
        attended,
        out_weight.reshape(key_local, group_factor, head_dim, model_width),
        preferred_element_type=jnp.float32,
    ).reshape(token_rows, model_width)
    fresh_keys = fresh_keys.transpose(0, 2, 1, 3)
    fresh_values = fresh_values.transpose(0, 2, 1, 3)
    chunk_rows = token_rows // vocab_shards
    chunk_start = vocab_shard * chunk_rows
    residual_chunk = lax.dynamic_slice_in_dim(states, chunk_start, chunk_rows, 0) + scatter_rows(
        attend_part, "vocab", vocab_shards
    )
    hidden_copies = (
        jnp.broadcast_to(residual_chunk[None], (vocab_shards, chunk_rows, model_width))
        * lax.rsqrt(jnp.mean(residual_chunk * residual_chunk, axis=1, keepdims=True) + eps_norm)[None]
        * hidden_gain.astype(jnp.float32)
    ).astype(jnp.bfloat16)
    hidden_in = lax.all_to_all(
        hidden_copies, "vocab", split_axis=0, concat_axis=0, tiled=True
    ).reshape(token_rows, model_width)
    down_part = feed_forward(hidden_in, gate_weight, up_weight, down_weight)
    feed_chunk = scatter_rows(down_part, "vocab", vocab_shards).astype(jnp.bfloat16)
    local_counts = lax.dynamic_slice_in_dim(
        live_draft_count, request_shard * local_requests, local_requests
    )
    chunk_token = chunk_start + jnp.arange(chunk_rows, dtype=jnp.int32)
    chunk_count = jnp.take(local_counts, chunk_token // draft_length)
    chunk_live = (chunk_token % draft_length) < chunk_count
    layer_chunk = jnp.where(
        chunk_live[:, None], residual_chunk + feed_chunk.astype(jnp.float32), 0.0
    ).astype(jnp.bfloat16)
    share_width = model_width // vocab_shards
    path_length = path_index.shape[1]
    per_shard = path_length // vocab_shards
    path_count = local_requests * per_shard
    path_rows_all = (
        (
            path_index.reshape(local_requests, vocab_shards, per_shard)
            + (jnp.arange(local_requests, dtype=jnp.int32) * draft_length)[:, None, None]
        )
        .transpose(1, 0, 2)
        .reshape(vocab_shards, path_count)
    )
    column_pieces = (
        layer_chunk.reshape(chunk_rows, vocab_shards, share_width)
        .transpose(1, 0, 2)
        .reshape(vocab_shards, chunk_rows * share_width)
    )
    in_chunk = (
        path_rows_all[:, :, None] == chunk_token[None, None, :]
    ).astype(jnp.bfloat16)
    path_pieces = (
        jnp.einsum("vjt,tf->vjf", in_chunk, layer_chunk, preferred_element_type=jnp.float32)
        .astype(jnp.bfloat16)
        .reshape(vocab_shards, path_count * model_width)
    )
    arrived = lax.all_to_all(
        jnp.concatenate([column_pieces, path_pieces], axis=1),
        "vocab",
        split_axis=0,
        concat_axis=0,
        tiled=True,
    )
    layer_part = arrived[:, : chunk_rows * share_width].reshape(token_rows, share_width)
    head_rows = (
        jnp.sum(arrived[:, chunk_rows * share_width :].astype(jnp.float32), axis=0)
        .reshape(path_count, model_width)
        .astype(jnp.bfloat16)
    )
    request_picker = (
        path_index[:, :, None] == jnp.arange(draft_length, dtype=jnp.int32)[None, None, :]
    ).astype(jnp.bfloat16)
    accepted_keys = jnp.einsum(
        "ytm,ymu->ytu",
        request_picker,
        fresh_keys.reshape(local_requests, draft_length, key_local * head_dim),
        preferred_element_type=jnp.float32,
    ).astype(jnp.bfloat16)
    accepted_values = jnp.einsum(
        "ytm,ymu->ytu",
        request_picker,
        fresh_values.reshape(local_requests, draft_length, key_local * head_dim),
        preferred_element_type=jnp.float32,
    ).astype(jnp.bfloat16)
    flat_rows = head_rows.astype(jnp.float32)
    mean_square = jnp.mean(flat_rows * flat_rows, axis=1)
    norm_values = jnp.sqrt(mean_square + eps_norm).reshape(local_requests, per_shard)
    head_copies = (
        jnp.broadcast_to(flat_rows[None], (request_shards, *flat_rows.shape))
        * lax.rsqrt(mean_square + eps_norm)[None, :, None]
        * final_gain.astype(jnp.float32)
    ).astype(jnp.bfloat16)
    gathered_head = lax.all_to_all(
        head_copies, "req", split_axis=0, concat_axis=0, tiled=True
    ).reshape(request_shards * flat_rows.shape[0], model_width)
    local_max = jnp.max(
        jnp.dot(gathered_head, head_weight, preferred_element_type=jnp.float32),
        axis=1,
    )
    every_max = gather_rows(local_max[None], "req", request_shards)
    maxima = jnp.max(every_max, axis=0).reshape(request_shards * local_requests, per_shard)
    return (
        layer_part.reshape(local_requests, draft_length, share_width),
        accepted_keys,
        accepted_values,
        norm_values,
        maxima,
    )


def solution(mesh):
    in_specs = (
        P("req", None, None),
        P("req", None),
        P(),
        P("req", None),
        P("req"),
        P("req", "vocab"),
        P("req", "vocab"),
        P(),
        P(),
        P(),
        P(None, "vocab"),
        P(None, "vocab"),
        P(None, "vocab"),
        P("vocab", None),
        P(None, "vocab"),
        P(None, "vocab"),
        P("vocab", None),
        P(None, "req"),
    )
    out_specs = (
        P("req", None, "vocab"),
        P("req", None, "vocab"),
        P("req", None, "vocab"),
        P("req", "vocab"),
        P(None, "vocab"),
    )
    return jax.shard_map(
        per_device, mesh=mesh, in_specs=in_specs, out_specs=out_specs, check_vma=False
    )
```
